32 devices in a mesh: ctx: 8 (over z, x), ch: 4 (over y, core).
Axes of the slice: x: 2, y: 2, z: 4, core: 2. Of those that a mesh axis runs over, the one named last changes fastest.
Arguments:
- arrivals: bfloat16 [3, 1024, 4096], P(None, 'ch', 'ctx'), may hold values from -12 to 12
- counts: int32 [8], P('ctx'), may hold values from 0 to 512, as said below
- short_taps: float32 [3, 3, 1024], P(None, None, 'ch'), may hold values from -3 to 3
- filter_taps: bfloat16 [1024, 2048], P('ch'), may hold values from -0.5 to 0.5
- skip_gain: float32 [1024], P('ch'), may hold values from 0.2 to 2
- out_weight: bfloat16 [8192, 1024], P('ch'), may hold values from -0.1875 to 0.1875
Outputs:
- mixed: bfloat16 [8192, 2048], P('ch', 'ctx')
The draws below stay inside these ranges and needn't reach their ends.
Inputs may be any that keep to these rules, and one draw needn't show every extreme that they name: The counts sum to 2048. For every sampler i, offsets[i] differs from i * 256 by at most 128, and this bound is reached in both directions in every draw. counts[0] is 384.
All inputs are finite; a program needn't handle non-finite values.
Results may differ from the reference program's by a relative error of at most 0.0058.
Values may be sent and summed in bfloat16 or wider, within the bound.
No kernel may reach another device: no remote copies, remote signals or barrier semaphores. Data moves between devices by JAX's collectives and lax.ppermute only.
A program may use at most 64 MiB of HBM per device.

```python
import math
import jax
import jax.numpy as jnp
from jax import lax

OUT = 8192
SLAB_FEATURE_DIM = 1024
T_DEV = 256
CAP = 512
SEQUENCE_LENGTH = 2048
ROWS_IN = 4096
N_CTX = 8


def draw_counts(key, part):
    half_len = T_DEV // 2
    derived_seed_pairs = jax.random.split(key, 3)
    drift = jax.random.randint(derived_seed_pairs[0], (N_CTX,), -half_len, half_len + 1, dtype=jnp.int32)
    first_spot = jax.random.randint(derived_seed_pairs[1], (), 1, N_CTX // 2 - 2, dtype=jnp.int32)
    second_spot = jax.random.randint(derived_seed_pairs[2], (), N_CTX // 2 + 2, N_CTX - 1, dtype=jnp.int32)
    positions = jnp.arange(N_CTX, dtype=jnp.int32)
    drift = jnp.where(positions == first_spot, half_len, drift)
    drift = jnp.where(positions == first_spot - 1, -half_len, drift)
    drift = jnp.where(positions == second_spot, -half_len, drift)
    drift = jnp.where(positions == second_spot - 1, half_len, drift)
    drift = jnp.where(positions == N_CTX // 2 - 1, -half_len, drift)
    drift = jnp.where(positions == N_CTX // 2, -half_len, drift)
    drift = jnp.where(positions == 0, half_len, drift)
    drift = jnp.where(positions == N_CTX - 1, 0, drift)
    earlier = jnp.concatenate([jnp.zeros((1,), jnp.int32), drift[:-1]])
    return (T_DEV + drift - earlier).astype(jnp.int32)


def draw_arrivals(key, part):
    seeds = jax.random.split(jax.random.fold_in(key, 11), 2)
    base = jnp.clip(jax.random.normal(seeds[0], (3, SLAB_FEATURE_DIM, ROWS_IN), jnp.float32), -4.0, 4.0)
    scale_low = 0.3
    scale_high = 3.0
    scales = jnp.exp(jax.random.uniform(seeds[1], (3, SLAB_FEATURE_DIM, N_CTX, 1), jnp.float32, math.log(scale_low), math.log(scale_high)))
    values = base.reshape(3, SLAB_FEATURE_DIM, N_CTX, CAP) * scales
    return values.reshape(3, SLAB_FEATURE_DIM, ROWS_IN).astype(jnp.bfloat16)


def draw_filter_taps(key, part):
    derived_seed_pairs = jax.random.split(key, 8)
    shift_amount_count = jnp.arange(SEQUENCE_LENGTH, dtype=jnp.float32)[None, :]
    slow_cut = 5
    negative_cut = 5
    rough_low = 0.5
    rough_high = 1.5
    slow_pick = jax.random.randint(derived_seed_pairs[0], (SLAB_FEATURE_DIM, 1), 0, 10) < slow_cut
    long_len = SEQUENCE_LENGTH * jnp.exp(jax.random.uniform(derived_seed_pairs[1], (SLAB_FEATURE_DIM, 1), jnp.float32, 0.0, math.log(8.0)))
    short_len = jnp.exp(jax.random.uniform(derived_seed_pairs[2], (SLAB_FEATURE_DIM, 1), jnp.float32, math.log(30.0), math.log(50.0)))
    outbreak_location = jax.random.randint(derived_seed_pairs[3], (SLAB_FEATURE_DIM, 3), 0, SEQUENCE_LENGTH).astype(jnp.float32)
    outbreak_survives = jax.random.uniform(derived_seed_pairs[4], (SLAB_FEATURE_DIM, 3), jnp.float32, 0.5, 0.8)
    survival_marks = jnp.where(shift_amount_count >= outbreak_location[:, 0:1], outbreak_survives[:, 0:1], 1.0)
    survival_marks = survival_marks * jnp.where(shift_amount_count >= outbreak_location[:, 1:2], outbreak_survives[:, 1:2], 1.0)
    survival_marks = survival_marks * jnp.where(shift_amount_count >= outbreak_location[:, 2:3], outbreak_survives[:, 2:3], 1.0)
    long_amp = jnp.sqrt(jnp.expm1(-2.0 / long_len) / jnp.expm1(-2.0 * SEQUENCE_LENGTH / long_len))
    short_amp = jnp.sqrt(jnp.expm1(-2.0 / short_len) / jnp.expm1(-2.0 * SEQUENCE_LENGTH / short_len))
    slow_share = jax.random.uniform(derived_seed_pairs[7], (SLAB_FEATURE_DIM, 1), jnp.float32, 0.2, 0.4)
    slow_share = jnp.where(slow_pick, 1.0, slow_share)
    slow_part = long_amp * jnp.exp(-shift_amount_count / long_len) * survival_marks
    fast_part = short_amp * jnp.exp(-shift_amount_count / short_len)
    profile = jnp.sqrt(slow_share) * slow_part + jnp.sqrt(1.0 - slow_share) * fast_part
    roughness = jax.random.uniform(derived_seed_pairs[5], (SLAB_FEATURE_DIM, SEQUENCE_LENGTH), jnp.float32, rough_low, rough_high)
    sign_flip = jnp.where(jax.random.randint(derived_seed_pairs[6], (SLAB_FEATURE_DIM, SEQUENCE_LENGTH), 0, 10) < negative_cut, -1.0, 1.0)
    return (profile * roughness * sign_flip).astype(jnp.bfloat16)


def shard_levels(stream_key, dims, cuts, least, top_value):
    gain, own = 1.0, jax.random.fold_in(stream_key, 6)
    for position, shards_of in cuts:
        steps = jnp.exp(jax.random.uniform(jax.random.fold_in(own, position), (shards_of,), jnp.float32, least / len(cuts), top_value / len(cuts)))
        gain = gain * jnp.repeat(steps, dims[position] // shards_of).reshape([-1 if axis == position else 1 for axis in range(len(dims))])
    return gain


def normal_values(own_key, extent, width, limit, cuts=(), kind=jnp.bfloat16):
    level = shard_levels(own_key, extent, cuts, -0.22, 0.18) if cuts else 1.0
    entries = jax.random.normal(own_key, extent, jnp.float32) * width * level
    return jnp.minimum(jnp.maximum(entries, -limit), limit).astype(kind)


def setup_inputs(seed: int = 0) -> dict:
    key_list = jax.random.split(jax.random.key(seed), 7)
    arrivals = draw_arrivals(jax.random.fold_in(key_list[6], 71), 0)
    counts = draw_counts(jax.random.fold_in(key_list[6], 71), 0)
    short_taps = normal_values(key_list[2], (3, 3, SLAB_FEATURE_DIM), 0.7, 3.0, ((2, 4),), jnp.float32)
    filter_taps = draw_filter_taps(jax.random.fold_in(key_list[6], 71), 0)
    skip_gain = jnp.clip(jnp.exp(math.log(2.0) - 2.3025851 * jax.random.uniform(key_list[4], (SLAB_FEATURE_DIM,), jnp.float32) ** shard_levels(key_list[4], (SLAB_FEATURE_DIM,), ((0, 4),), -0.2, 0.2)), 0.2, 2.0)
    out_weight = normal_values(key_list[5], (OUT, SLAB_FEATURE_DIM), SLAB_FEATURE_DIM ** -0.5, 0.1875, ((0, 4),))
    return dict(arrivals=arrivals, counts=counts, short_taps=short_taps, filter_taps=filter_taps, skip_gain=skip_gain, out_weight=out_weight)


def reference(arrivals, counts, short_taps, filter_taps, skip_gain, out_weight):
    offsets = (jnp.cumsum(counts) - counts).astype(jnp.int32)
    row_index = jnp.arange(CAP, dtype=jnp.int32)
    target = offsets[:, None] + row_index[None, :]
    target = jnp.where(row_index[None, :] < counts[:, None], target, SEQUENCE_LENGTH)
    target = target.reshape(-1).astype(jnp.int32)
    packed = jnp.zeros((3, SLAB_FEATURE_DIM, SEQUENCE_LENGTH), jnp.bfloat16).at[:, :, target].set(arrivals, mode="drop")
    padded = jnp.pad(packed.astype(jnp.float32), ((0, 0), (0, 0), (2, 0)))
    shorted = short_taps[:, 0, :, None] * padded[:, :, 2:]
    shorted = shorted + short_taps[:, 1, :, None] * padded[:, :, 1:-1]
    shorted = shorted + short_taps[:, 2, :, None] * padded[:, :, :-2]
    mixed_input = (shorted[1] * shorted[2]).astype(jnp.bfloat16)
    wide_input = lax.optimization_barrier(mixed_input).astype(jnp.float32)
    period = 2 * SEQUENCE_LENGTH
    spectrum = jnp.fft.rfft(filter_taps.astype(jnp.float32), n=period, axis=1) * jnp.fft.rfft(wide_input, n=period, axis=1)
    conv = jnp.fft.irfft(spectrum, n=period, axis=1)[:, :SEQUENCE_LENGTH] + skip_gain[:, None] * wide_input
    gated = (shorted[0] * conv).astype(jnp.bfloat16)
    return jnp.dot(out_weight, gated, preferred_element_type=jnp.float32).astype(jnp.bfloat16)
```

```python
import math

import jax
import jax.numpy as jnp
import ml_dtypes
import numpy as np
from jax import lax
from jax.sharding import PartitionSpec as P

T_DEV = 256
HALF = T_DEV // 2
PERIOD = 2 * T_DEV
GROUP = 8


def split_bf16(table):
    hi = table.astype(ml_dtypes.bfloat16)
    lo = (table - hi.astype(np.float64)).astype(ml_dtypes.bfloat16)
    return jnp.asarray(hi), jnp.asarray(lo)


def dft_tables():
    t = np.arange(T_DEV)[:, None]
    f = np.arange(T_DEV)[None, :]
    angle = 2.0 * np.pi * ((t * f) % PERIOD) / PERIOD
    forward = np.concatenate([np.cos(angle), -np.sin(angle)], axis=1)
    forward[:, T_DEV] = np.where(np.arange(T_DEV) % 2 == 0, 1.0, -1.0)
    fr = np.arange(T_DEV)[:, None]
    n = np.arange(T_DEV)[None, :]
    angle = 2.0 * np.pi * ((fr * n) % PERIOD) / PERIOD
    inv_re = 2.0 * np.cos(angle) / PERIOD
    inv_re[0, :] = 1.0 / PERIOD
    inv_im = -2.0 * np.sin(angle) / PERIOD
    inv_im[0, :] = np.where(np.arange(T_DEV) % 2 == 0, 1.0, -1.0) / PERIOD
    inverse = np.concatenate([inv_re, inv_im], axis=0).astype(np.float32)
    return split_bf16(forward), jnp.asarray(inverse)


def transform(blocks, forward):
    hi, lo = forward
    return jnp.einsum("kct,tf->kcf", blocks, hi, preferred_element_type=jnp.float32) + jnp.einsum(
        "kct,tf->kcf", blocks, lo, preferred_element_type=jnp.float32
    )


def kernel_spectra(tap_blocks, forward):
    spectra = transform(tap_blocks, forward)
    column = jnp.arange(PERIOD, dtype=jnp.int32) % T_DEV
    signs = jnp.where(column % 2 == 0, 1.0, -1.0).astype(jnp.float32)
    return spectra[1:] + signs * spectra[:-1]


def products(x_spec, g_spec):
    xr, xi = x_spec[..., :T_DEV], x_spec[..., T_DEV:]
    gr, gi = g_spec[..., :T_DEV], g_spec[..., T_DEV:]
    return (
        jnp.sum(xr * gr, axis=0),
        jnp.sum(xi * gi, axis=0),
        jnp.sum(xr * gi, axis=0),
        jnp.sum(xi * gr, axis=0),
    )


def on_device(arrivals, counts, short_taps, filter_taps, skip_gain, out_weight):
    n_ctx = lax.axis_size("ctx")
    device = lax.axis_index("ctx")
    channels = arrivals.shape[1]
    capacity = arrivals.shape[2]
    n_blocks = filter_taps.shape[1] // T_DEV
    forward, inverse = dft_tables()

    every_count = lax.all_gather(counts, "ctx", axis=0, tiled=True)
    earlier = jnp.arange(n_ctx, dtype=jnp.int32) < device
    offset = jnp.sum(jnp.where(earlier, every_count, 0))
    count = counts[0]

    frame = 2 * T_DEV
    row = jnp.arange(capacity, dtype=jnp.int32)[:, None]
    col = jnp.arange(frame, dtype=jnp.int32)[None, :]
    shift = offset - device * T_DEV + HALF
    select = ((row + shift == col) & (row < count)).astype(jnp.bfloat16)
    placed = jnp.einsum(
        "pcr,rj->pcj", arrivals, select, preferred_element_type=jnp.float32
    ).astype(jnp.bfloat16)
    to_prev = placed[:, :, :HALF]
    to_next = placed[:, :, frame - HALF - 2 :]
    from_next = lax.ppermute(to_prev, "ctx", [(i + 1, i) for i in range(n_ctx - 1)])
    from_prev = lax.ppermute(to_next, "ctx", [(i, i + 1) for i in range(n_ctx - 1)])
    window = placed[:, :, HALF - 2 : HALF + T_DEV]
    window = window + jnp.pad(from_prev, ((0, 0), (0, 0), (0, T_DEV - HALF)))
    window = window + jnp.pad(from_next, ((0, 0), (0, 0), (T_DEV + 2 - HALF, 0)))
    wide = window.astype(jnp.float32)
    shorted = short_taps[:, 0, :, None] * wide[:, :, 2:]
    shorted = shorted + short_taps[:, 1, :, None] * wide[:, :, 1:-1]
    shorted = shorted + short_taps[:, 2, :, None] * wide[:, :, :-2]
    mixed_input = (shorted[1] * shorted[2]).astype(jnp.bfloat16)

    tap_blocks = jnp.stack(
        [jnp.zeros((channels, T_DEV), filter_taps.dtype)]
        + [filter_taps[:, k * T_DEV : (k + 1) * T_DEV] for k in range(n_blocks)]
    )
    every_input = lax.all_gather(mixed_input, "ctx", axis=0)
    backwards = jnp.concatenate(
        [jnp.flip(every_input, 0), jnp.zeros_like(every_input)], axis=0
    )
    start = n_ctx - 1 - device
    if n_blocks <= GROUP:
        x_blocks = lax.dynamic_slice_in_dim(backwards, start, n_blocks, 0)
        sums = products(transform(x_blocks, forward), kernel_spectra(tap_blocks, forward))
    else:
        width = max(w for w in range(1, GROUP + 1) if n_blocks % w == 0)

        def group(g, acc):
            k0 = g * width
            x_blocks = lax.dynamic_slice_in_dim(backwards, start + k0, width, 0)
            taps = lax.dynamic_slice_in_dim(tap_blocks, k0, width + 1, 0)
            part = products(transform(x_blocks, forward), kernel_spectra(taps, forward))
            return tuple(a + b for a, b in zip(acc, part))

        zero = jnp.zeros((channels, T_DEV), jnp.float32)
        sums = lax.fori_loop(0, n_blocks // width, group, (zero, zero, zero, zero))
    rr, ii, ri, ir = sums
    first = jnp.arange(T_DEV, dtype=jnp.int32)[None, :] == 0
    spec_re = jnp.where(first, rr, rr - ii)
    spec_im = jnp.where(first, ii, ri + ir)
    spectrum = jnp.concatenate([spec_re, spec_im], axis=1)
    conv_core = jnp.dot(spectrum, inverse, precision=lax.Precision.HIGHEST)
    conv = conv_core + skip_gain[:, None] * mixed_input.astype(jnp.float32)
    gated = (shorted[0] * conv).astype(jnp.bfloat16)
    mixed = jnp.dot(
        out_weight,
        lax.all_gather(gated, "ch", axis=0, tiled=True),
        preferred_element_type=jnp.float32,
    )
    return mixed.astype(jnp.bfloat16)


def solution(mesh):
    return jax.shard_map(
        on_device,
        mesh=mesh,
        in_specs=(
            P(None, "ch", "ctx"),
            P("ctx"),
            P(None, None, "ch"),
            P("ch", None),
            P("ch"),
            P("ch", None),
        ),
        out_specs=P("ch", "ctx"),
        check_vma=False,
    )
```

```python
import math

import jax
import jax.numpy as jnp
import ml_dtypes
import numpy as np
from jax import lax
from jax.sharding import PartitionSpec as P

T_DEV = 256
HALF = T_DEV // 2
PERIOD = 2 * T_DEV
GROUP = 8
SENTINEL = 256.0


def split_bf16(table):
    hi = table.astype(ml_dtypes.bfloat16)
    lo = (table - hi.astype(np.float64)).astype(ml_dtypes.bfloat16)
    return jnp.asarray(hi), jnp.asarray(lo)


def dft_tables():
    t = np.arange(T_DEV)[:, None]
    f = np.arange(T_DEV)[None, :]
    angle = 2.0 * np.pi * ((t * f) % PERIOD) / PERIOD
    forward = np.concatenate([np.cos(angle), -np.sin(angle)], axis=1)
    forward[:, T_DEV] = np.where(np.arange(T_DEV) % 2 == 0, 1.0, -1.0)
    fr = np.arange(T_DEV)[:, None]
    n = np.arange(T_DEV)[None, :]
    angle = 2.0 * np.pi * ((fr * n) % PERIOD) / PERIOD
    inv_re = 2.0 * np.cos(angle) / PERIOD
    inv_re[0, :] = 1.0 / PERIOD
    inv_im = -2.0 * np.sin(angle) / PERIOD
    inv_im[0, :] = np.where(np.arange(T_DEV) % 2 == 0, 1.0, -1.0) / PERIOD
    inverse = np.concatenate([inv_re, inv_im], axis=0).astype(np.float32)
    return split_bf16(forward), jnp.asarray(inverse)


def transform(blocks, forward, spec="kct,tf->kcf"):
    hi, lo = forward
    return jnp.einsum(spec, blocks, hi, preferred_element_type=jnp.float32) + jnp.einsum(
        spec, blocks, lo, preferred_element_type=jnp.float32
    )


def kernel_spectra(tap_blocks, forward):
    spectra = transform(tap_blocks, forward)
    column = jnp.arange(PERIOD, dtype=jnp.int32) % T_DEV
    signs = jnp.where(column % 2 == 0, 1.0, -1.0).astype(jnp.float32)
    return spectra[1:] + signs * spectra[:-1]


def products(x_spec, g_spec):
    xr, xi = x_spec[..., :T_DEV], x_spec[..., T_DEV:]
    gr, gi = g_spec[..., :T_DEV], g_spec[..., T_DEV:]
    return (
        jnp.sum(xr * gr, axis=0),
        jnp.sum(xi * gi, axis=0),
        jnp.sum(xr * gi, axis=0),
        jnp.sum(xi * gr, axis=0),
    )


def by_gather(arrivals, counts, short_taps, filter_taps, skip_gain, out_weight):
    n_ctx = lax.axis_size("ctx")
    device = lax.axis_index("ctx")
    channels = arrivals.shape[1]
    capacity = arrivals.shape[2]
    n_blocks = filter_taps.shape[1] // T_DEV
    forward, inverse = dft_tables()

    every_count = lax.all_gather(counts, "ctx", axis=0, tiled=True)
    earlier = jnp.arange(n_ctx, dtype=jnp.int32) < device
    offset = jnp.sum(jnp.where(earlier, every_count, 0))
    count = counts[0]

    frame = 2 * T_DEV
    row = jnp.arange(capacity, dtype=jnp.int32)[:, None]
    col = jnp.arange(frame, dtype=jnp.int32)[None, :]
    shift = offset - device * T_DEV + HALF
    select = ((row + shift == col) & (row < count)).astype(jnp.bfloat16)
    placed = jnp.einsum(
        "pcr,rj->pcj", arrivals, select, preferred_element_type=jnp.float32
    ).astype(jnp.bfloat16)
    to_prev = placed[:, :, :HALF]
    to_next = placed[:, :, frame - HALF - 2 :]
    from_next = lax.ppermute(to_prev, "ctx", [(i + 1, i) for i in range(n_ctx - 1)])
    from_prev = lax.ppermute(to_next, "ctx", [(i, i + 1) for i in range(n_ctx - 1)])
    window = placed[:, :, HALF - 2 : HALF + T_DEV]
    window = window + jnp.pad(from_prev, ((0, 0), (0, 0), (0, T_DEV - HALF)))
    window = window + jnp.pad(from_next, ((0, 0), (0, 0), (T_DEV + 2 - HALF, 0)))
    wide = window.astype(jnp.float32)
    shorted = short_taps[:, 0, :, None] * wide[:, :, 2:]
    shorted = shorted + short_taps[:, 1, :, None] * wide[:, :, 1:-1]
    shorted = shorted + short_taps[:, 2, :, None] * wide[:, :, :-2]
    mixed_input = (shorted[1] * shorted[2]).astype(jnp.bfloat16)

    tap_blocks = jnp.stack(
        [jnp.zeros((channels, T_DEV), filter_taps.dtype)]
        + [filter_taps[:, k * T_DEV : (k + 1) * T_DEV] for k in range(n_blocks)]
    )
    every_input = lax.all_gather(mixed_input, "ctx", axis=0)
    backwards = jnp.concatenate(
        [jnp.flip(every_input, 0), jnp.zeros_like(every_input)], axis=0
    )
    start = n_ctx - 1 - device
    if n_blocks <= GROUP:
        x_blocks = lax.dynamic_slice_in_dim(backwards, start, n_blocks, 0)
        sums = products(transform(x_blocks, forward), kernel_spectra(tap_blocks, forward))
    else:
        width = max(w for w in range(1, GROUP + 1) if n_blocks % w == 0)

        def group(g, acc):
            k0 = g * width
            x_blocks = lax.dynamic_slice_in_dim(backwards, start + k0, width, 0)
            taps = lax.dynamic_slice_in_dim(tap_blocks, k0, width + 1, 0)
            part = products(transform(x_blocks, forward), kernel_spectra(taps, forward))
            return tuple(a + b for a, b in zip(acc, part))

        zero = jnp.zeros((channels, T_DEV), jnp.float32)
        sums = lax.fori_loop(0, n_blocks // width, group, (zero, zero, zero, zero))
    rr, ii, ri, ir = sums
    first = jnp.arange(T_DEV, dtype=jnp.int32)[None, :] == 0
    spec_re = jnp.where(first, rr, rr - ii)
    spec_im = jnp.where(first, ii, ri + ir)
    spectrum = jnp.concatenate([spec_re, spec_im], axis=1)
    conv_core = jnp.dot(spectrum, inverse, precision=lax.Precision.HIGHEST)
    conv = conv_core + skip_gain[:, None] * mixed_input.astype(jnp.float32)
    gated = (shorted[0] * conv).astype(jnp.bfloat16)
    mixed = jnp.dot(
        out_weight,
        lax.all_gather(gated, "ch", axis=0, tiled=True),
        preferred_element_type=jnp.float32,
    )
    return mixed.astype(jnp.bfloat16)


def by_transpose(arrivals, counts, short_taps, filter_taps, skip_gain, out_weight):
    n_ctx = lax.axis_size("ctx")
    device = lax.axis_index("ctx")
    channels = arrivals.shape[1]
    capacity = arrivals.shape[2]
    length = filter_taps.shape[1]
    n_blocks = length // T_DEV
    own = channels // n_ctx
    forward, inverse = dft_tables()

    live = jnp.arange(capacity, dtype=jnp.int32) < counts[0]
    marked = jnp.where(live[None, None, :], arrivals, jnp.asarray(SENTINEL, arrivals.dtype))
    marked = marked.reshape(3, n_ctx, own, capacity)
    rows = lax.all_to_all(marked, "ctx", 1, 1, tiled=False)
    every_count = jnp.sum((rows[0, :, 0, :] != SENTINEL).astype(jnp.int32), axis=1)
    offsets = jnp.cumsum(every_count) - every_count

    frame = 3 * T_DEV
    row = jnp.arange(capacity, dtype=jnp.int32)[None, :, None]
    col = jnp.arange(frame, dtype=jnp.int32)[None, None, :]
    sampler = jnp.arange(n_ctx, dtype=jnp.int32)[:, None, None]
    shift = offsets[:, None, None] - (sampler - 1) * T_DEV
    select = ((row + shift == col) & (row < every_count[:, None, None])).astype(jnp.bfloat16)
    placed = jnp.einsum("picr,irj->ipcj", rows, select, preferred_element_type=jnp.float32)
    full = sum(
        jnp.pad(placed[i], ((0, 0), (0, 0), (i * T_DEV, (n_ctx - 1 - i) * T_DEV)))
        for i in range(n_ctx)
    )
    wide = full[:, :, T_DEV - 2 : T_DEV + length]
    first = device * own
    taps = lax.dynamic_slice_in_dim(short_taps, first, own, 2)
    shorted = taps[:, 0, :, None] * wide[:, :, 2:]
    shorted = shorted + taps[:, 1, :, None] * wide[:, :, 1:-1]
    shorted = shorted + taps[:, 2, :, None] * wide[:, :, :-2]
    mixed_input = (shorted[1] * shorted[2]).astype(jnp.bfloat16)

    x_spec = transform(mixed_input.reshape(own, n_blocks, T_DEV), forward, "cnt,tf->cnf")
    own_taps = lax.dynamic_slice_in_dim(filter_taps, first, own, 0)
    tap_blocks = jnp.concatenate(
        [jnp.zeros((own, T_DEV), own_taps.dtype), own_taps], axis=1
    ).reshape(own, n_blocks + 1, T_DEV)
    h_spec = transform(tap_blocks, forward, "cnt,tf->cnf")
    column = jnp.arange(PERIOD, dtype=jnp.int32) % T_DEV
    signs = jnp.where(column % 2 == 0, 1.0, -1.0).astype(jnp.float32)
    g_spec = h_spec[:, 1:] + signs * h_spec[:, :-1]
    xr, xi = x_spec[..., :T_DEV], x_spec[..., T_DEV:]
    gr, gi = g_spec[..., :T_DEV], g_spec[..., T_DEV:]
    sums = [jnp.zeros((own, n_blocks, T_DEV), jnp.float32) for _ in range(4)]
    for k in range(n_blocks):
        pad = ((0, 0), (k, 0), (0, 0))
        terms = (
            xr[:, : n_blocks - k] * gr[:, k : k + 1],
            xi[:, : n_blocks - k] * gi[:, k : k + 1],
            xr[:, : n_blocks - k] * gi[:, k : k + 1],
            xi[:, : n_blocks - k] * gr[:, k : k + 1],
        )
        sums = [s + jnp.pad(t, pad) for s, t in zip(sums, terms)]
    rr, ii, ri, ir = sums
    at_zero = jnp.arange(T_DEV, dtype=jnp.int32)[None, None, :] == 0
    spectrum = jnp.concatenate(
        [jnp.where(at_zero, rr, rr - ii), jnp.where(at_zero, ii, ri + ir)], axis=2
    )
    conv_core = jnp.einsum("cnf,ft->cnt", spectrum, inverse, precision=lax.Precision.HIGHEST)
    gains = lax.dynamic_slice_in_dim(skip_gain, first, own, 0)
    conv = conv_core.reshape(own, length) + gains[:, None] * mixed_input.astype(jnp.float32)
    gated = (shorted[0] * conv).astype(jnp.bfloat16)
    back = lax.all_to_all(gated.reshape(own, n_ctx, T_DEV), "ctx", 1, 0, tiled=False)
    gated_block = back.reshape(channels, T_DEV)
    mixed = jnp.dot(
        out_weight,
        lax.all_gather(gated_block, "ch", axis=0, tiled=True),
        preferred_element_type=jnp.float32,
    )
    return mixed.astype(jnp.bfloat16)


def on_device(arrivals, counts, short_taps, filter_taps, skip_gain, out_weight):
    n_ctx = lax.axis_size("ctx")
    blocks = filter_taps.shape[1] // T_DEV
    if arrivals.shape[1] % n_ctx == 0 and blocks == n_ctx:
        return by_transpose(arrivals, counts, short_taps, filter_taps, skip_gain, out_weight)
    return by_gather(arrivals, counts, short_taps, filter_taps, skip_gain, out_weight)


def solution(mesh):
    return jax.shard_map(
        on_device,
        mesh=mesh,
        in_specs=(
            P(None, "ch", "ctx"),
            P("ctx"),
            P(None, None, "ch"),
            P("ch", None),
            P("ch"),
            P("ch", None),
        ),
        out_specs=P("ch", "ctx"),
        check_vma=False,
    )
```

```python
import math

import jax
import jax.numpy as jnp
import ml_dtypes
import numpy as np
from jax import lax
from jax.sharding import PartitionSpec as P

T_DEV = 256
HALF = T_DEV // 2
PERIOD = 2 * T_DEV
GROUP = 8
SENTINEL = 256.0


def split_bf16(table):
    hi = table.astype(ml_dtypes.bfloat16)
    lo = (table - hi.astype(np.float64)).astype(ml_dtypes.bfloat16)
    return jnp.asarray(hi), jnp.asarray(lo)


def dft_tables():
    t = np.arange(T_DEV)[:, None]
    f = np.arange(T_DEV)[None, :]
    angle = 2.0 * np.pi * ((t * f) % PERIOD) / PERIOD
    forward = np.concatenate([np.cos(angle), -np.sin(angle)], axis=1)
    forward[:, T_DEV] = np.where(np.arange(T_DEV) % 2 == 0, 1.0, -1.0)
    fr = np.arange(T_DEV)[:, None]
    n = np.arange(T_DEV)[None, :]
    angle = 2.0 * np.pi * ((fr * n) % PERIOD) / PERIOD
    inv_re = 2.0 * np.cos(angle) / PERIOD
    inv_re[0, :] = 1.0 / PERIOD
    inv_im = -2.0 * np.sin(angle) / PERIOD
    inv_im[0, :] = np.where(np.arange(T_DEV) % 2 == 0, 1.0, -1.0) / PERIOD
    inverse = np.concatenate([inv_re, inv_im], axis=0).astype(np.float32)
    return split_bf16(forward), jnp.asarray(inverse)


def transform(blocks, forward, spec="kct,tf->kcf"):
    hi, lo = forward
    return jnp.einsum(spec, blocks, hi, preferred_element_type=jnp.float32) + jnp.einsum(
        spec, blocks, lo, preferred_element_type=jnp.float32
    )


def kernel_spectra(tap_blocks, forward):
    spectra = transform(tap_blocks, forward)
    column = jnp.arange(PERIOD, dtype=jnp.int32) % T_DEV
    signs = jnp.where(column % 2 == 0, 1.0, -1.0).astype(jnp.float32)
    return spectra[1:] + signs * spectra[:-1]


def products(x_spec, g_spec):
    xr, xi = x_spec[..., :T_DEV], x_spec[..., T_DEV:]
    gr, gi = g_spec[..., :T_DEV], g_spec[..., T_DEV:]
    return (
        jnp.sum(xr * gr, axis=0),
        jnp.sum(xi * gi, axis=0),
        jnp.sum(xr * gi, axis=0),
        jnp.sum(xi * gr, axis=0),
    )


def by_gather(arrivals, counts, short_taps, filter_taps, skip_gain, out_weight):
    n_ctx = lax.axis_size("ctx")
    device = lax.axis_index("ctx")
    channels = arrivals.shape[1]
    capacity = arrivals.shape[2]
    n_blocks = filter_taps.shape[1] // T_DEV
    forward, inverse = dft_tables()

    every_count = lax.all_gather(counts, "ctx", axis=0, tiled=True)
    earlier = jnp.arange(n_ctx, dtype=jnp.int32) < device
    offset = jnp.sum(jnp.where(earlier, every_count, 0))
    count = counts[0]

    frame = 2 * T_DEV
    row = jnp.arange(capacity, dtype=jnp.int32)[:, None]
    col = jnp.arange(frame, dtype=jnp.int32)[None, :]
    shift = offset - device * T_DEV + HALF
    select = ((row + shift == col) & (row < count)).astype(jnp.bfloat16)
    placed = jnp.einsum(
        "pcr,rj->pcj", arrivals, select, preferred_element_type=jnp.float32
    ).astype(jnp.bfloat16)
    to_prev = placed[:, :, :HALF]
    to_next = placed[:, :, frame - HALF - 2 :]
    from_next = lax.ppermute(to_prev, "ctx", [(i + 1, i) for i in range(n_ctx - 1)])
    from_prev = lax.ppermute(to_next, "ctx", [(i, i + 1) for i in range(n_ctx - 1)])
    window = placed[:, :, HALF - 2 : HALF + T_DEV]
    window = window + jnp.pad(from_prev, ((0, 0), (0, 0), (0, T_DEV - HALF)))
    window = window + jnp.pad(from_next, ((0, 0), (0, 0), (T_DEV + 2 - HALF, 0)))
    wide = window.astype(jnp.float32)
    shorted = short_taps[:, 0, :, None] * wide[:, :, 2:]
    shorted = shorted + short_taps[:, 1, :, None] * wide[:, :, 1:-1]
    shorted = shorted + short_taps[:, 2, :, None] * wide[:, :, :-2]
    mixed_input = (shorted[1] * shorted[2]).astype(jnp.bfloat16)

    tap_blocks = jnp.stack(
        [jnp.zeros((channels, T_DEV), filter_taps.dtype)]
        + [filter_taps[:, k * T_DEV : (k + 1) * T_DEV] for k in range(n_blocks)]
    )
    every_input = lax.all_gather(mixed_input, "ctx", axis=0)
    backwards = jnp.concatenate(
        [jnp.flip(every_input, 0), jnp.zeros_like(every_input)], axis=0
    )
    start = n_ctx - 1 - device
    if n_blocks <= GROUP:
        x_blocks = lax.dynamic_slice_in_dim(backwards, start, n_blocks, 0)
        sums = products(transform(x_blocks, forward), kernel_spectra(tap_blocks, forward))
    else:
        width = max(w for w in range(1, GROUP + 1) if n_blocks % w == 0)

        def group(g, acc):
            k0 = g * width
            x_blocks = lax.dynamic_slice_in_dim(backwards, start + k0, width, 0)
            taps = lax.dynamic_slice_in_dim(tap_blocks, k0, width + 1, 0)
            part = products(transform(x_blocks, forward), kernel_spectra(taps, forward))
            return tuple(a + b for a, b in zip(acc, part))

        zero = jnp.zeros((channels, T_DEV), jnp.float32)
        sums = lax.fori_loop(0, n_blocks // width, group, (zero, zero, zero, zero))
    rr, ii, ri, ir = sums
    first = jnp.arange(T_DEV, dtype=jnp.int32)[None, :] == 0
    spec_re = jnp.where(first, rr, rr - ii)
    spec_im = jnp.where(first, ii, ri + ir)
    spectrum = jnp.concatenate([spec_re, spec_im], axis=1)
    conv_core = jnp.dot(spectrum, inverse, precision=lax.Precision.HIGHEST)
    conv = conv_core + skip_gain[:, None] * mixed_input.astype(jnp.float32)
    gated = (shorted[0] * conv).astype(jnp.bfloat16)
    mixed = jnp.dot(
        out_weight,
        lax.all_gather(gated, "ch", axis=0, tiled=True),
        preferred_element_type=jnp.float32,
    )
    return mixed.astype(jnp.bfloat16)


def by_transpose(arrivals, counts, short_taps, filter_taps, skip_gain, out_weight):
    n_ctx = lax.axis_size("ctx")
    device = lax.axis_index("ctx")
    channels = arrivals.shape[1]
    capacity = arrivals.shape[2]
    length = filter_taps.shape[1]
    n_blocks = length // T_DEV
    own = channels // n_ctx
    forward, inverse = dft_tables()

    live = jnp.arange(capacity, dtype=jnp.int32) < counts[0]
    by_owner = jnp.transpose(arrivals.reshape(3, n_ctx, own, capacity), (1, 0, 2, 3))
    marked = jnp.where(live, by_owner, jnp.asarray(SENTINEL, arrivals.dtype))
    rows = jnp.transpose(lax.all_to_all(marked, "ctx", 0, 0, tiled=False), (1, 0, 2, 3))
    every_count = jnp.sum((rows[0, :, 0, :] != SENTINEL).astype(jnp.int32), axis=1)
    offsets = jnp.cumsum(every_count) - every_count

    full = jnp.zeros((3, own, length + capacity), arrivals.dtype)
    for i in range(n_ctx):
        full = lax.dynamic_update_slice(full, rows[:, i], (0, 0, offsets[i]))
    full = jnp.pad(full[:, :, :length], ((0, 0), (0, 0), (2, 0))).astype(jnp.float32)
    wide = full
    first = device * own
    taps = lax.dynamic_slice_in_dim(short_taps, first, own, 2)
    shorted = taps[:, 0, :, None] * wide[:, :, 2:]
    shorted = shorted + taps[:, 1, :, None] * wide[:, :, 1:-1]
    shorted = shorted + taps[:, 2, :, None] * wide[:, :, :-2]
    mixed_input = (shorted[1] * shorted[2]).astype(jnp.bfloat16)

    x_spec = transform(mixed_input.reshape(own, n_blocks, T_DEV), forward, "cnt,tf->cnf")
    own_taps = lax.dynamic_slice_in_dim(filter_taps, first, own, 0)
    tap_blocks = jnp.concatenate(
        [jnp.zeros((own, T_DEV), own_taps.dtype), own_taps], axis=1
    ).reshape(own, n_blocks + 1, T_DEV)
    h_spec = transform(tap_blocks, forward, "cnt,tf->cnf")
    column = jnp.arange(PERIOD, dtype=jnp.int32) % T_DEV
    signs = jnp.where(column % 2 == 0, 1.0, -1.0).astype(jnp.float32)
    g_spec = h_spec[:, 1:] + signs * h_spec[:, :-1]
    xr, xi = x_spec[..., :T_DEV], x_spec[..., T_DEV:]
    gr, gi = g_spec[..., :T_DEV], g_spec[..., T_DEV:]
    sums = [jnp.zeros((own, n_blocks, T_DEV), jnp.float32) for _ in range(4)]
    for k in range(n_blocks):
        pad = ((0, 0), (k, 0), (0, 0))
        terms = (
            xr[:, : n_blocks - k] * gr[:, k : k + 1],
            xi[:, : n_blocks - k] * gi[:, k : k + 1],
            xr[:, : n_blocks - k] * gi[:, k : k + 1],
            xi[:, : n_blocks - k] * gr[:, k : k + 1],
        )
        sums = [s + jnp.pad(t, pad) for s, t in zip(sums, terms)]
    rr, ii, ri, ir = sums
    at_zero = jnp.arange(T_DEV, dtype=jnp.int32)[None, None, :] == 0
    spectrum = jnp.concatenate(
        [jnp.where(at_zero, rr, rr - ii), jnp.where(at_zero, ii, ri + ir)], axis=2
    )
    conv_core = jnp.einsum("cnf,ft->cnt", spectrum, inverse, precision=lax.Precision.HIGHEST)
    gains = lax.dynamic_slice_in_dim(skip_gain, first, own, 0)
    conv = conv_core.reshape(own, length) + gains[:, None] * mixed_input.astype(jnp.float32)
    gated = (shorted[0] * conv).astype(jnp.bfloat16)
    back = lax.all_to_all(gated.reshape(own, n_ctx, T_DEV), "ctx", 1, 0, tiled=False)
    gated_block = back.reshape(channels, T_DEV)
    mixed = jnp.dot(
        out_weight,
        lax.all_gather(gated_block, "ch", axis=0, tiled=True),
        preferred_element_type=jnp.float32,
    )
    return mixed.astype(jnp.bfloat16)


def on_device(arrivals, counts, short_taps, filter_taps, skip_gain, out_weight):
    n_ctx = lax.axis_size("ctx")
    blocks = filter_taps.shape[1] // T_DEV
    if arrivals.shape[1] % n_ctx == 0 and blocks == n_ctx:
        return by_transpose(arrivals, counts, short_taps, filter_taps, skip_gain, out_weight)
    return by_gather(arrivals, counts, short_taps, filter_taps, skip_gain, out_weight)


def solution(mesh):
    return jax.shard_map(
        on_device,
        mesh=mesh,
        in_specs=(
            P(None, "ch", "ctx"),
            P("ctx"),
            P(None, None, "ch"),
            P("ch", None),
            P("ch"),
            P("ch", None),
        ),
        out_specs=P("ch", "ctx"),
        check_vma=False,
    )
```

```python
import math

import jax
import jax.numpy as jnp
import ml_dtypes
import numpy as np
from jax import lax
from jax.sharding import PartitionSpec as P

T_DEV = 256
HALF = T_DEV // 2
PERIOD = 2 * T_DEV
GROUP = 8
SENTINEL = 256.0


def split_bf16(table):
    hi = table.astype(ml_dtypes.bfloat16)
    lo = (table - hi.astype(np.float64)).astype(ml_dtypes.bfloat16)
    return jnp.asarray(hi), jnp.asarray(lo)


def dft_tables():
    t = np.arange(T_DEV)[:, None]
    f = np.arange(T_DEV)[None, :]
    angle = 2.0 * np.pi * ((t * f) % PERIOD) / PERIOD
    forward = np.concatenate([np.cos(angle), -np.sin(angle)], axis=1)
    forward[:, T_DEV] = np.where(np.arange(T_DEV) % 2 == 0, 1.0, -1.0)
    fr = np.arange(T_DEV)[:, None]
    n = np.arange(T_DEV)[None, :]
    angle = 2.0 * np.pi * ((fr * n) % PERIOD) / PERIOD
    inv_re = 2.0 * np.cos(angle) / PERIOD
    inv_re[0, :] = 1.0 / PERIOD
    inv_im = -2.0 * np.sin(angle) / PERIOD
    inv_im[0, :] = np.where(np.arange(T_DEV) % 2 == 0, 1.0, -1.0) / PERIOD
    inverse = np.concatenate([inv_re, inv_im], axis=0).astype(np.float32)
    return split_bf16(forward), jnp.asarray(inverse)


def transform(blocks, forward, spec="kct,tf->kcf"):
    hi, lo = forward
    return jnp.einsum(spec, blocks, hi, preferred_element_type=jnp.float32) + jnp.einsum(
        spec, blocks, lo, preferred_element_type=jnp.float32
    )


def kernel_spectra(tap_blocks, forward):
    spectra = transform(tap_blocks, forward)
    column = jnp.arange(PERIOD, dtype=jnp.int32) % T_DEV
    signs = jnp.where(column % 2 == 0, 1.0, -1.0).astype(jnp.float32)
    return spectra[1:] + signs * spectra[:-1]


def products(x_spec, g_spec):
    xr, xi = x_spec[..., :T_DEV], x_spec[..., T_DEV:]
    gr, gi = g_spec[..., :T_DEV], g_spec[..., T_DEV:]
    return (
        jnp.sum(xr * gr, axis=0),
        jnp.sum(xi * gi, axis=0),
        jnp.sum(xr * gi, axis=0),
        jnp.sum(xi * gr, axis=0),
    )


def by_gather(arrivals, counts, short_taps, filter_taps, skip_gain, out_weight):
    n_ctx = lax.axis_size("ctx")
    device = lax.axis_index("ctx")
    channels = arrivals.shape[1]
    capacity = arrivals.shape[2]
    n_blocks = filter_taps.shape[1] // T_DEV
    forward, inverse = dft_tables()

    every_count = lax.all_gather(counts, "ctx", axis=0, tiled=True)
    earlier = jnp.arange(n_ctx, dtype=jnp.int32) < device
    offset = jnp.sum(jnp.where(earlier, every_count, 0))
    count = counts[0]

    frame = 2 * T_DEV
    row = jnp.arange(capacity, dtype=jnp.int32)[:, None]
    col = jnp.arange(frame, dtype=jnp.int32)[None, :]
    shift = offset - device * T_DEV + HALF
    select = ((row + shift == col) & (row < count)).astype(jnp.bfloat16)
    placed = jnp.einsum(
        "pcr,rj->pcj", arrivals, select, preferred_element_type=jnp.float32
    ).astype(jnp.bfloat16)
    to_prev = placed[:, :, :HALF]
    to_next = placed[:, :, frame - HALF - 2 :]
    from_next = lax.ppermute(to_prev, "ctx", [(i + 1, i) for i in range(n_ctx - 1)])
    from_prev = lax.ppermute(to_next, "ctx", [(i, i + 1) for i in range(n_ctx - 1)])
    window = placed[:, :, HALF - 2 : HALF + T_DEV]
    window = window + jnp.pad(from_prev, ((0, 0), (0, 0), (0, T_DEV - HALF)))
    window = window + jnp.pad(from_next, ((0, 0), (0, 0), (T_DEV + 2 - HALF, 0)))
    wide = window.astype(jnp.float32)
    shorted = short_taps[:, 0, :, None] * wide[:, :, 2:]
    shorted = shorted + short_taps[:, 1, :, None] * wide[:, :, 1:-1]
    shorted = shorted + short_taps[:, 2, :, None] * wide[:, :, :-2]
    mixed_input = (shorted[1] * shorted[2]).astype(jnp.bfloat16)

    tap_blocks = jnp.stack(
        [jnp.zeros((channels, T_DEV), filter_taps.dtype)]
        + [filter_taps[:, k * T_DEV : (k + 1) * T_DEV] for k in range(n_blocks)]
    )
    every_input = lax.all_gather(mixed_input, "ctx", axis=0)
    backwards = jnp.concatenate(
        [jnp.flip(every_input, 0), jnp.zeros_like(every_input)], axis=0
    )
    start = n_ctx - 1 - device
    if n_blocks <= GROUP:
        x_blocks = lax.dynamic_slice_in_dim(backwards, start, n_blocks, 0)
        sums = products(transform(x_blocks, forward), kernel_spectra(tap_blocks, forward))
    else:
        width = max(w for w in range(1, GROUP + 1) if n_blocks % w == 0)

        def group(g, acc):
            k0 = g * width
            x_blocks = lax.dynamic_slice_in_dim(backwards, start + k0, width, 0)
            taps = lax.dynamic_slice_in_dim(tap_blocks, k0, width + 1, 0)
            part = products(transform(x_blocks, forward), kernel_spectra(taps, forward))
            return tuple(a + b for a, b in zip(acc, part))

        zero = jnp.zeros((channels, T_DEV), jnp.float32)
        sums = lax.fori_loop(0, n_blocks // width, group, (zero, zero, zero, zero))
    rr, ii, ri, ir = sums
    first = jnp.arange(T_DEV, dtype=jnp.int32)[None, :] == 0
    spec_re = jnp.where(first, rr, rr - ii)
    spec_im = jnp.where(first, ii, ri + ir)
    spectrum = jnp.concatenate([spec_re, spec_im], axis=1)
    conv_core = jnp.dot(spectrum, inverse, precision=lax.Precision.HIGHEST)
    conv = conv_core + skip_gain[:, None] * mixed_input.astype(jnp.float32)
    gated = (shorted[0] * conv).astype(jnp.bfloat16)
    mixed = jnp.dot(
        out_weight,
        lax.all_gather(gated, "ch", axis=0, tiled=True),
        preferred_element_type=jnp.float32,
    )
    return mixed.astype(jnp.bfloat16)


def by_transpose(arrivals, counts, short_taps, filter_taps, skip_gain, out_weight):
    n_ctx = lax.axis_size("ctx")
    device = lax.axis_index("ctx")
    channels = arrivals.shape[1]
    capacity = arrivals.shape[2]
    length = filter_taps.shape[1]
    n_blocks = length // T_DEV
    own = channels // n_ctx
    forward, inverse = dft_tables()

    live = jnp.arange(capacity, dtype=jnp.int32) < counts[0]
    by_owner = jnp.transpose(arrivals.reshape(3, n_ctx, own, capacity), (1, 0, 2, 3))
    marker = jnp.where(live, by_owner[:, 0, 0, :], jnp.asarray(SENTINEL, arrivals.dtype))
    marked = by_owner.at[:, 0, 0, :].set(marker)
    rows = lax.all_to_all(marked, "ctx", 0, 0, tiled=False)
    every_count = jnp.sum((rows[:, 0, 0, :] != SENTINEL).astype(jnp.int32), axis=1)
    offsets = jnp.cumsum(every_count) - every_count

    local = jnp.arange(T_DEV, dtype=jnp.int32)[None, :, None]
    col = jnp.arange(PERIOD, dtype=jnp.int32)[None, None, :]
    sampler = jnp.arange(n_ctx, dtype=jnp.int32)[:, None, None]
    shift = offsets[:, None, None] - (sampler - 1) * T_DEV - HALF
    total = (n_ctx + 3) * T_DEV
    full = 0.0
    for q in range(capacity // T_DEV):
        select = (local + shift == col) & (local + q * T_DEV < every_count[:, None, None])
        placed = jnp.einsum(
            "ipcr,irj->ipcj",
            rows[..., q * T_DEV : (q + 1) * T_DEV],
            select.astype(jnp.bfloat16),
            preferred_element_type=jnp.float32,
        )
        for i in range(n_ctx):
            left = i * T_DEV + q * T_DEV + HALF
            full = full + jnp.pad(placed[i], ((0, 0), (0, 0), (left, total - left - PERIOD)))
    wide = full[:, :, T_DEV - 2 : T_DEV + length]
    first = device * own
    taps = lax.dynamic_slice_in_dim(short_taps, first, own, 2)
    shorted = taps[:, 0, :, None] * wide[:, :, 2:]
    shorted = shorted + taps[:, 1, :, None] * wide[:, :, 1:-1]
    shorted = shorted + taps[:, 2, :, None] * wide[:, :, :-2]
    mixed_input = (shorted[1] * shorted[2]).astype(jnp.bfloat16)

    x_spec = transform(mixed_input.reshape(own, n_blocks, T_DEV), forward, "cnt,tf->cnf")
    own_taps = lax.dynamic_slice_in_dim(filter_taps, first, own, 0)
    tap_blocks = jnp.concatenate(
        [jnp.zeros((own, T_DEV), own_taps.dtype), own_taps], axis=1
    ).reshape(own, n_blocks + 1, T_DEV)
    h_spec = transform(tap_blocks, forward, "cnt,tf->cnf")
    column = jnp.arange(PERIOD, dtype=jnp.int32) % T_DEV
    signs = jnp.where(column % 2 == 0, 1.0, -1.0).astype(jnp.float32)
    g_spec = h_spec[:, 1:] + signs * h_spec[:, :-1]
    xr, xi = x_spec[..., :T_DEV], x_spec[..., T_DEV:]
    gr, gi = g_spec[..., :T_DEV], g_spec[..., T_DEV:]
    sums = [jnp.zeros((own, n_blocks, T_DEV), jnp.float32) for _ in range(4)]
    for k in range(n_blocks):
        pad = ((0, 0), (k, 0), (0, 0))
        terms = (
            xr[:, : n_blocks - k] * gr[:, k : k + 1],
            xi[:, : n_blocks - k] * gi[:, k : k + 1],
            xr[:, : n_blocks - k] * gi[:, k : k + 1],
            xi[:, : n_blocks - k] * gr[:, k : k + 1],
        )
        sums = [s + jnp.pad(t, pad) for s, t in zip(sums, terms)]
    rr, ii, ri, ir = sums
    at_zero = jnp.arange(T_DEV, dtype=jnp.int32)[None, None, :] == 0
    spectrum = jnp.concatenate(
        [jnp.where(at_zero, rr, rr - ii), jnp.where(at_zero, ii, ri + ir)], axis=2
    )
    conv_core = jnp.einsum("cnf,ft->cnt", spectrum, inverse, precision=lax.Precision.HIGHEST)
    gains = lax.dynamic_slice_in_dim(skip_gain, first, own, 0)
    conv = conv_core.reshape(own, length) + gains[:, None] * mixed_input.astype(jnp.float32)
    gated = (shorted[0] * conv).astype(jnp.bfloat16)
    back = lax.all_to_all(gated.reshape(own, n_ctx, T_DEV), "ctx", 1, 0, tiled=False)
    gated_block = back.reshape(channels, T_DEV)
    mixed = jnp.dot(
        out_weight,
        lax.all_gather(gated_block, "ch", axis=0, tiled=True),
        preferred_element_type=jnp.float32,
    )
    return mixed.astype(jnp.bfloat16)


def on_device(arrivals, counts, short_taps, filter_taps, skip_gain, out_weight):
    n_ctx = lax.axis_size("ctx")
    blocks = filter_taps.shape[1] // T_DEV
    if arrivals.shape[1] % n_ctx == 0 and blocks == n_ctx:
        return by_transpose(arrivals, counts, short_taps, filter_taps, skip_gain, out_weight)
    return by_gather(arrivals, counts, short_taps, filter_taps, skip_gain, out_weight)


def solution(mesh):
    return jax.shard_map(
        on_device,
        mesh=mesh,
        in_specs=(
            P(None, "ch", "ctx"),
            P("ctx"),
            P(None, None, "ch"),
            P("ch", None),
            P("ch"),
            P("ch", None),
        ),
        out_specs=P("ch", "ctx"),
        check_vma=False,
    )
```

```python
import math

import jax
import jax.numpy as jnp
import ml_dtypes
import numpy as np
from jax import lax
from jax.experimental import pallas as pl
from jax.sharding import PartitionSpec as P

T_DEV = 256
HALF = T_DEV // 2
PERIOD = 2 * T_DEV
GROUP = 8
SENTINEL = 256.0


def split_bf16(table):
    hi = table.astype(ml_dtypes.bfloat16)
    lo = (table - hi.astype(np.float64)).astype(ml_dtypes.bfloat16)
    return jnp.asarray(hi), jnp.asarray(lo)


def dft_tables():
    t = np.arange(T_DEV)[:, None]
    f = np.arange(T_DEV)[None, :]
    angle = 2.0 * np.pi * ((t * f) % PERIOD) / PERIOD
    forward = np.concatenate([np.cos(angle), -np.sin(angle)], axis=1)
    forward[:, T_DEV] = np.where(np.arange(T_DEV) % 2 == 0, 1.0, -1.0)
    fr = np.arange(T_DEV)[:, None]
    n = np.arange(T_DEV)[None, :]
    angle = 2.0 * np.pi * ((fr * n) % PERIOD) / PERIOD
    inv_re = 2.0 * np.cos(angle) / PERIOD
    inv_re[0, :] = 1.0 / PERIOD
    inv_im = -2.0 * np.sin(angle) / PERIOD
    inv_im[0, :] = np.where(np.arange(T_DEV) % 2 == 0, 1.0, -1.0) / PERIOD
    inverse = np.concatenate([inv_re, inv_im], axis=0).astype(np.float32)
    return split_bf16(forward), jnp.asarray(inverse)


def transform(blocks, forward, spec="kct,tf->kcf"):
    hi, lo = forward
    return jnp.einsum(spec, blocks, hi, preferred_element_type=jnp.float32) + jnp.einsum(
        spec, blocks, lo, preferred_element_type=jnp.float32
    )


def kernel_spectra(tap_blocks, forward):
    spectra = transform(tap_blocks, forward)
    column = jnp.arange(PERIOD, dtype=jnp.int32) % T_DEV
    signs = jnp.where(column % 2 == 0, 1.0, -1.0).astype(jnp.float32)
    return spectra[1:] + signs * spectra[:-1]


def products(x_spec, g_spec):
    xr, xi = x_spec[..., :T_DEV], x_spec[..., T_DEV:]
    gr, gi = g_spec[..., :T_DEV], g_spec[..., T_DEV:]
    return (
        jnp.sum(xr * gr, axis=0),
        jnp.sum(xi * gi, axis=0),
        jnp.sum(xr * gi, axis=0),
        jnp.sum(xi * gr, axis=0),
    )


def by_gather(arrivals, counts, short_taps, filter_taps, skip_gain, out_weight):
    n_ctx = lax.axis_size("ctx")
    device = lax.axis_index("ctx")
    channels = arrivals.shape[1]
    capacity = arrivals.shape[2]
    n_blocks = filter_taps.shape[1] // T_DEV
    forward, inverse = dft_tables()

    every_count = lax.all_gather(counts, "ctx", axis=0, tiled=True)
    earlier = jnp.arange(n_ctx, dtype=jnp.int32) < device
    offset = jnp.sum(jnp.where(earlier, every_count, 0))
    count = counts[0]

    frame = 2 * T_DEV
    row = jnp.arange(capacity, dtype=jnp.int32)[:, None]
    col = jnp.arange(frame, dtype=jnp.int32)[None, :]
    shift = offset - device * T_DEV + HALF
    select = ((row + shift == col) & (row < count)).astype(jnp.bfloat16)
    placed = jnp.einsum(
        "pcr,rj->pcj", arrivals, select, preferred_element_type=jnp.float32
    ).astype(jnp.bfloat16)
    to_prev = placed[:, :, :HALF]
    to_next = placed[:, :, frame - HALF - 2 :]
    from_next = lax.ppermute(to_prev, "ctx", [(i + 1, i) for i in range(n_ctx - 1)])
    from_prev = lax.ppermute(to_next, "ctx", [(i, i + 1) for i in range(n_ctx - 1)])
    window = placed[:, :, HALF - 2 : HALF + T_DEV]
    window = window + jnp.pad(from_prev, ((0, 0), (0, 0), (0, T_DEV - HALF)))
    window = window + jnp.pad(from_next, ((0, 0), (0, 0), (T_DEV + 2 - HALF, 0)))
    wide = window.astype(jnp.float32)
    shorted = short_taps[:, 0, :, None] * wide[:, :, 2:]
    shorted = shorted + short_taps[:, 1, :, None] * wide[:, :, 1:-1]
    shorted = shorted + short_taps[:, 2, :, None] * wide[:, :, :-2]
    mixed_input = (shorted[1] * shorted[2]).astype(jnp.bfloat16)

    tap_blocks = jnp.stack(
        [jnp.zeros((channels, T_DEV), filter_taps.dtype)]
        + [filter_taps[:, k * T_DEV : (k + 1) * T_DEV] for k in range(n_blocks)]
    )
    every_input = lax.all_gather(mixed_input, "ctx", axis=0)
    backwards = jnp.concatenate(
        [jnp.flip(every_input, 0), jnp.zeros_like(every_input)], axis=0
    )
    start = n_ctx - 1 - device
    if n_blocks <= GROUP:
        x_blocks = lax.dynamic_slice_in_dim(backwards, start, n_blocks, 0)
        sums = products(transform(x_blocks, forward), kernel_spectra(tap_blocks, forward))
    else:
        width = max(w for w in range(1, GROUP + 1) if n_blocks % w == 0)

        def group(g, acc):
            k0 = g * width
            x_blocks = lax.dynamic_slice_in_dim(backwards, start + k0, width, 0)
            taps = lax.dynamic_slice_in_dim(tap_blocks, k0, width + 1, 0)
            part = products(transform(x_blocks, forward), kernel_spectra(taps, forward))
            return tuple(a + b for a, b in zip(acc, part))

        zero = jnp.zeros((channels, T_DEV), jnp.float32)
        sums = lax.fori_loop(0, n_blocks // width, group, (zero, zero, zero, zero))
    rr, ii, ri, ir = sums
    first = jnp.arange(T_DEV, dtype=jnp.int32)[None, :] == 0
    spec_re = jnp.where(first, rr, rr - ii)
    spec_im = jnp.where(first, ii, ri + ir)
    spectrum = jnp.concatenate([spec_re, spec_im], axis=1)
    conv_core = jnp.dot(spectrum, inverse, precision=lax.Precision.HIGHEST)
    conv = conv_core + skip_gain[:, None] * mixed_input.astype(jnp.float32)
    gated = (shorted[0] * conv).astype(jnp.bfloat16)
    mixed = jnp.dot(
        out_weight,
        lax.all_gather(gated, "ch", axis=0, tiled=True),
        preferred_element_type=jnp.float32,
    )
    return mixed.astype(jnp.bfloat16)


def by_transpose(arrivals, counts, short_taps, filter_taps, skip_gain, out_weight):
    n_ctx = lax.axis_size("ctx")
    device = lax.axis_index("ctx")
    channels = arrivals.shape[1]
    capacity = arrivals.shape[2]
    length = filter_taps.shape[1]
    n_blocks = length // T_DEV
    own = channels // n_ctx
    forward, inverse = dft_tables()

    live = jnp.arange(capacity, dtype=jnp.int32) < counts[0]
    marked = jnp.where(live[None, None, :], arrivals, jnp.asarray(SENTINEL, arrivals.dtype))
    marked = marked.reshape(3, n_ctx, own, capacity)
    rows = lax.all_to_all(marked, "ctx", 1, 1, tiled=False)
    every_count = jnp.sum((rows[0, :, 0, :] != SENTINEL).astype(jnp.int32), axis=1)
    offsets = jnp.cumsum(every_count) - every_count

    frame = 3 * T_DEV
    row = jnp.arange(capacity, dtype=jnp.int32)[None, :, None]
    col = jnp.arange(frame, dtype=jnp.int32)[None, None, :]
    sampler = jnp.arange(n_ctx, dtype=jnp.int32)[:, None, None]
    shift = offsets[:, None, None] - (sampler - 1) * T_DEV
    select = ((row + shift == col) & (row < every_count[:, None, None])).astype(jnp.bfloat16)
    placed = jnp.einsum("picr,irj->ipcj", rows, select, preferred_element_type=jnp.bfloat16)
    full = sum(
        jnp.pad(placed[i], ((0, 0), (0, 0), (i * T_DEV, (n_ctx - 1 - i) * T_DEV)))
        for i in range(n_ctx)
    )
    wide = full[:, :, T_DEV - 2 : T_DEV + length]
    first = device * own
    taps = lax.dynamic_slice_in_dim(short_taps, first, own, 2)
    shorted = taps[:, 0, :, None] * wide[:, :, 2:]
    shorted = shorted + taps[:, 1, :, None] * wide[:, :, 1:-1]
    shorted = shorted + taps[:, 2, :, None] * wide[:, :, :-2]
    mixed_input = (shorted[1] * shorted[2]).astype(jnp.bfloat16)

    x_spec = transform(mixed_input.reshape(own, n_blocks, T_DEV), forward, "cnt,tf->cnf")
    own_taps = lax.dynamic_slice_in_dim(filter_taps, first, own, 0)
    tap_blocks = jnp.concatenate(
        [jnp.zeros((own, T_DEV), own_taps.dtype), own_taps], axis=1
    ).reshape(own, n_blocks + 1, T_DEV)
    h_spec = transform(tap_blocks, forward, "cnt,tf->cnf")
    column = jnp.arange(PERIOD, dtype=jnp.int32) % T_DEV
    signs = jnp.where(column % 2 == 0, 1.0, -1.0).astype(jnp.float32)
    g_spec = h_spec[:, 1:] + signs * h_spec[:, :-1]
    xr, xi = x_spec[..., :T_DEV], x_spec[..., T_DEV:]
    gr, gi = g_spec[..., :T_DEV], g_spec[..., T_DEV:]
    sums = [jnp.zeros((own, n_blocks, T_DEV), jnp.float32) for _ in range(4)]
    for k in range(n_blocks):
        pad = ((0, 0), (k, 0), (0, 0))
        terms = (
            xr[:, : n_blocks - k] * gr[:, k : k + 1],
            xi[:, : n_blocks - k] * gi[:, k : k + 1],
            xr[:, : n_blocks - k] * gi[:, k : k + 1],
            xi[:, : n_blocks - k] * gr[:, k : k + 1],
        )
        sums = [s + jnp.pad(t, pad) for s, t in zip(sums, terms)]
    rr, ii, ri, ir = sums
    at_zero = jnp.arange(T_DEV, dtype=jnp.int32)[None, None, :] == 0
    spectrum = jnp.concatenate(
        [jnp.where(at_zero, rr, rr - ii), jnp.where(at_zero, ii, ri + ir)], axis=2
    )
    conv_core = jnp.einsum("cnf,ft->cnt", spectrum, inverse, precision=lax.Precision.HIGHEST)
    gains = lax.dynamic_slice_in_dim(skip_gain, first, own, 0)
    conv = conv_core.reshape(own, length) + gains[:, None] * mixed_input.astype(jnp.float32)
    gated = (shorted[0] * conv).astype(jnp.bfloat16)
    back = lax.all_to_all(gated.reshape(own, n_ctx, T_DEV), "ctx", 1, 0, tiled=False)
    gated_block = back.reshape(channels, T_DEV)
    return project(out_weight, lax.all_gather(gated_block, "ch", axis=0, tiled=True))


def project_kernel(w_ref, g_ref, o_ref):
    o_ref[...] = jnp.dot(
        w_ref[...], g_ref[...], preferred_element_type=jnp.float32
    ).astype(o_ref.dtype)


def project(weight, gated, rows=512):
    features, width = weight.shape
    tokens = gated.shape[1]
    return pl.pallas_call(
        project_kernel,
        grid=(features // rows,),
        in_specs=[
            pl.BlockSpec((rows, width), lambda i: (i, 0)),
            pl.BlockSpec((width, tokens), lambda i: (0, 0)),
        ],
        out_specs=pl.BlockSpec((rows, tokens), lambda i: (i, 0)),
        out_shape=jax.ShapeDtypeStruct((features, tokens), jnp.bfloat16),
    )(weight, gated)


def on_device(arrivals, counts, short_taps, filter_taps, skip_gain, out_weight):
    n_ctx = lax.axis_size("ctx")
    blocks = filter_taps.shape[1] // T_DEV
    if arrivals.shape[1] % n_ctx == 0 and blocks == n_ctx:
        return by_transpose(arrivals, counts, short_taps, filter_taps, skip_gain, out_weight)
    return by_gather(arrivals, counts, short_taps, filter_taps, skip_gain, out_weight)


def solution(mesh):
    return jax.shard_map(
        on_device,
        mesh=mesh,
        in_specs=(
            P(None, "ch", "ctx"),
            P("ctx"),
            P(None, None, "ch"),
            P("ch", None),
            P("ch"),
            P("ch", None),
        ),
        out_specs=P("ch", "ctx"),
        check_vma=False,
    )
```

```python
import math

import jax
import jax.numpy as jnp
import ml_dtypes
import numpy as np
from jax import lax
from jax.sharding import PartitionSpec as P

T_DEV = 256
HALF = T_DEV // 2
PERIOD = 2 * T_DEV
GROUP = 8
SENTINEL = 256.0


def split_bf16(table):
    hi = table.astype(ml_dtypes.bfloat16)
    lo = (table - hi.astype(np.float64)).astype(ml_dtypes.bfloat16)
    return jnp.asarray(hi), jnp.asarray(lo)


def dft_tables():
    t = np.arange(T_DEV)[:, None]
    f = np.arange(T_DEV)[None, :]
    angle = 2.0 * np.pi * ((t * f) % PERIOD) / PERIOD
    forward = np.concatenate([np.cos(angle), -np.sin(angle)], axis=1)
    forward[:, T_DEV] = np.where(np.arange(T_DEV) % 2 == 0, 1.0, -1.0)
    fr = np.arange(T_DEV)[:, None]
    n = np.arange(T_DEV)[None, :]
    angle = 2.0 * np.pi * ((fr * n) % PERIOD) / PERIOD
    inv_re = 2.0 * np.cos(angle) / PERIOD
    inv_re[0, :] = 1.0 / PERIOD
    inv_im = -2.0 * np.sin(angle) / PERIOD
    inv_im[0, :] = np.where(np.arange(T_DEV) % 2 == 0, 1.0, -1.0) / PERIOD
    inverse = np.concatenate([inv_re, inv_im], axis=0).astype(np.float32)
    return split_bf16(forward), jnp.asarray(inverse)


def transform(blocks, forward, spec="kct,tf->kcf"):
    hi, lo = forward
    return jnp.einsum(spec, blocks, hi, preferred_element_type=jnp.float32) + jnp.einsum(
        spec, blocks, lo, preferred_element_type=jnp.float32
    )


def kernel_spectra(tap_blocks, forward):
    spectra = transform(tap_blocks, forward)
    column = jnp.arange(PERIOD, dtype=jnp.int32) % T_DEV
    signs = jnp.where(column % 2 == 0, 1.0, -1.0).astype(jnp.float32)
    return spectra[1:] + signs * spectra[:-1]


def products(x_spec, g_spec):
    xr, xi = x_spec[..., :T_DEV], x_spec[..., T_DEV:]
    gr, gi = g_spec[..., :T_DEV], g_spec[..., T_DEV:]
    return (
        jnp.sum(xr * gr, axis=0),
        jnp.sum(xi * gi, axis=0),
        jnp.sum(xr * gi, axis=0),
        jnp.sum(xi * gr, axis=0),
    )


def by_gather(arrivals, counts, short_taps, filter_taps, skip_gain, out_weight):
    n_ctx = lax.axis_size("ctx")
    device = lax.axis_index("ctx")
    channels = arrivals.shape[1]
    capacity = arrivals.shape[2]
    n_blocks = filter_taps.shape[1] // T_DEV
    forward, inverse = dft_tables()

    every_count = lax.all_gather(counts, "ctx", axis=0, tiled=True)
    earlier = jnp.arange(n_ctx, dtype=jnp.int32) < device
    offset = jnp.sum(jnp.where(earlier, every_count, 0))
    count = counts[0]

    frame = 2 * T_DEV
    row = jnp.arange(capacity, dtype=jnp.int32)[:, None]
    col = jnp.arange(frame, dtype=jnp.int32)[None, :]
    shift = offset - device * T_DEV + HALF
    select = ((row + shift == col) & (row < count)).astype(jnp.bfloat16)
    placed = jnp.einsum(
        "pcr,rj->pcj", arrivals, select, preferred_element_type=jnp.float32
    ).astype(jnp.bfloat16)
    to_prev = placed[:, :, :HALF]
    to_next = placed[:, :, frame - HALF - 2 :]
    from_next = lax.ppermute(to_prev, "ctx", [(i + 1, i) for i in range(n_ctx - 1)])
    from_prev = lax.ppermute(to_next, "ctx", [(i, i + 1) for i in range(n_ctx - 1)])
    window = placed[:, :, HALF - 2 : HALF + T_DEV]
    window = window + jnp.pad(from_prev, ((0, 0), (0, 0), (0, T_DEV - HALF)))
    window = window + jnp.pad(from_next, ((0, 0), (0, 0), (T_DEV + 2 - HALF, 0)))
    wide = window.astype(jnp.float32)
    shorted = short_taps[:, 0, :, None] * wide[:, :, 2:]
    shorted = shorted + short_taps[:, 1, :, None] * wide[:, :, 1:-1]
    shorted = shorted + short_taps[:, 2, :, None] * wide[:, :, :-2]
    mixed_input = (shorted[1] * shorted[2]).astype(jnp.bfloat16)

    tap_blocks = jnp.stack(
        [jnp.zeros((channels, T_DEV), filter_taps.dtype)]
        + [filter_taps[:, k * T_DEV : (k + 1) * T_DEV] for k in range(n_blocks)]
    )
    every_input = lax.all_gather(mixed_input, "ctx", axis=0)
    backwards = jnp.concatenate(
        [jnp.flip(every_input, 0), jnp.zeros_like(every_input)], axis=0
    )
    start = n_ctx - 1 - device
    if n_blocks <= GROUP:
        x_blocks = lax.dynamic_slice_in_dim(backwards, start, n_blocks, 0)
        sums = products(transform(x_blocks, forward), kernel_spectra(tap_blocks, forward))
    else:
        width = max(w for w in range(1, GROUP + 1) if n_blocks % w == 0)

        def group(g, acc):
            k0 = g * width
            x_blocks = lax.dynamic_slice_in_dim(backwards, start + k0, width, 0)
            taps = lax.dynamic_slice_in_dim(tap_blocks, k0, width + 1, 0)
            part = products(transform(x_blocks, forward), kernel_spectra(taps, forward))
            return tuple(a + b for a, b in zip(acc, part))

        zero = jnp.zeros((channels, T_DEV), jnp.float32)
        sums = lax.fori_loop(0, n_blocks // width, group, (zero, zero, zero, zero))
    rr, ii, ri, ir = sums
    first = jnp.arange(T_DEV, dtype=jnp.int32)[None, :] == 0
    spec_re = jnp.where(first, rr, rr - ii)
    spec_im = jnp.where(first, ii, ri + ir)
    spectrum = jnp.concatenate([spec_re, spec_im], axis=1)
    conv_core = jnp.dot(spectrum, inverse, precision=lax.Precision.HIGHEST)
    conv = conv_core + skip_gain[:, None] * mixed_input.astype(jnp.float32)
    gated = (shorted[0] * conv).astype(jnp.bfloat16)
    mixed = jnp.dot(
        out_weight,
        lax.all_gather(gated, "ch", axis=0, tiled=True),
        preferred_element_type=jnp.float32,
    )
    return mixed.astype(jnp.bfloat16)


def by_transpose(arrivals, counts, short_taps, filter_taps, skip_gain, out_weight):
    n_ctx = lax.axis_size("ctx")
    device = lax.axis_index("ctx")
    channels = arrivals.shape[1]
    capacity = arrivals.shape[2]
    length = filter_taps.shape[1]
    n_blocks = length // T_DEV
    own = channels // n_ctx
    forward, inverse = dft_tables()

    live = jnp.arange(capacity, dtype=jnp.int32) < counts[0]
    marked = jnp.where(live[None, None, :], arrivals, jnp.asarray(SENTINEL, arrivals.dtype))
    marked = marked.reshape(3, n_ctx, own, capacity)
    rows = lax.all_to_all(marked, "ctx", 1, 1, tiled=False)
    every_count = jnp.sum((rows[0, :, 0, :] != SENTINEL).astype(jnp.int32), axis=1)
    offsets = jnp.cumsum(every_count) - every_count

    frame = 3 * T_DEV
    row = jnp.arange(capacity, dtype=jnp.int32)[None, :, None]
    col = jnp.arange(frame, dtype=jnp.int32)[None, None, :]
    sampler = jnp.arange(n_ctx, dtype=jnp.int32)[:, None, None]
    shift = offsets[:, None, None] - (sampler - 1) * T_DEV
    select = ((row + shift == col) & (row < every_count[:, None, None])).astype(jnp.bfloat16)
    placed = jnp.einsum("picr,irj->ipcj", rows, select, preferred_element_type=jnp.bfloat16)
    full = sum(
        jnp.pad(placed[i], ((0, 0), (0, 0), (i * T_DEV, (n_ctx - 1 - i) * T_DEV)))
        for i in range(n_ctx)
    )
    wide = full[:, :, T_DEV - 2 : T_DEV + length]
    first = device * own
    taps = lax.dynamic_slice_in_dim(short_taps, first, own, 2)
    shorted = taps[:, 0, :, None] * wide[:, :, 2:]
    shorted = shorted + taps[:, 1, :, None] * wide[:, :, 1:-1]
    shorted = shorted + taps[:, 2, :, None] * wide[:, :, :-2]
    mixed_input = (shorted[1] * shorted[2]).astype(jnp.bfloat16)

    x_spec = transform(mixed_input.reshape(own, n_blocks, T_DEV), forward, "cnt,tf->cnf")
    own_taps = lax.dynamic_slice_in_dim(filter_taps, first, own, 0)
    tap_blocks = jnp.concatenate(
        [jnp.zeros((own, T_DEV), own_taps.dtype), own_taps], axis=1
    ).reshape(own, n_blocks + 1, T_DEV)
    h_spec = transform(tap_blocks, forward, "cnt,tf->cnf")
    column = jnp.arange(PERIOD, dtype=jnp.int32) % T_DEV
    signs = jnp.where(column % 2 == 0, 1.0, -1.0).astype(jnp.float32)
    g_spec = h_spec[:, 1:] + signs * h_spec[:, :-1]
    xr, xi = x_spec[..., :T_DEV], x_spec[..., T_DEV:]
    gr, gi = g_spec[..., :T_DEV], g_spec[..., T_DEV:]
    sums = [jnp.zeros((own, n_blocks, T_DEV), jnp.float32) for _ in range(4)]
    for k in range(n_blocks):
        pad = ((0, 0), (k, 0), (0, 0))
        terms = (
            xr[:, : n_blocks - k] * gr[:, k : k + 1],
            xi[:, : n_blocks - k] * gi[:, k : k + 1],
            xr[:, : n_blocks - k] * gi[:, k : k + 1],
            xi[:, : n_blocks - k] * gr[:, k : k + 1],
        )
        sums = [s + jnp.pad(t, pad) for s, t in zip(sums, terms)]
    rr, ii, ri, ir = sums
    at_zero = jnp.arange(T_DEV, dtype=jnp.int32)[None, None, :] == 0
    spectrum = jnp.concatenate(
        [jnp.where(at_zero, rr, rr - ii), jnp.where(at_zero, ii, ri + ir)], axis=2
    )
    conv_core = jnp.einsum("cnf,ft->cnt", spectrum, inverse, precision=lax.Precision.HIGHEST)
    gains = lax.dynamic_slice_in_dim(skip_gain, first, own, 0)
    conv = conv_core.reshape(own, length) + gains[:, None] * mixed_input.astype(jnp.float32)
    gated = (shorted[0] * conv).astype(jnp.bfloat16)
    back = lax.all_to_all(gated.reshape(own, n_ctx, T_DEV), "ctx", 1, 0, tiled=False)
    gated_block = back.reshape(channels, T_DEV)
    mixed = jnp.dot(
        out_weight,
        lax.all_gather(gated_block, "ch", axis=0, tiled=True),
        preferred_element_type=jnp.float32,
    )
    return mixed.astype(jnp.bfloat16)


def on_device(arrivals, counts, short_taps, filter_taps, skip_gain, out_weight):
    n_ctx = lax.axis_size("ctx")
    blocks = filter_taps.shape[1] // T_DEV
    if arrivals.shape[1] % n_ctx == 0 and blocks == n_ctx:
        return by_transpose(arrivals, counts, short_taps, filter_taps, skip_gain, out_weight)
    return by_gather(arrivals, counts, short_taps, filter_taps, skip_gain, out_weight)


def solution(mesh):
    return jax.shard_map(
        on_device,
        mesh=mesh,
        in_specs=(
            P(None, "ch", "ctx"),
            P("ctx"),
            P(None, None, "ch"),
            P("ch", None),
            P("ch"),
            P("ch", None),
        ),
        out_specs=P("ch", "ctx"),
        check_vma=False,
    )
```

```python
import math

import jax
import jax.numpy as jnp
import ml_dtypes
import numpy as np
from jax import lax
from jax.sharding import PartitionSpec as P

T_DEV = 256
HALF = T_DEV // 2
PERIOD = 2 * T_DEV
GROUP = 8


def split_bf16(table):
    hi = table.astype(ml_dtypes.bfloat16)
    lo = (table - hi.astype(np.float64)).astype(ml_dtypes.bfloat16)
    return jnp.asarray(hi), jnp.asarray(lo)


def dft_tables():
    t = np.arange(T_DEV)[:, None]
    f = np.arange(T_DEV)[None, :]
    angle = 2.0 * np.pi * ((t * f) % PERIOD) / PERIOD
    forward = np.concatenate([np.cos(angle), -np.sin(angle)], axis=1)
    forward[:, T_DEV] = np.where(np.arange(T_DEV) % 2 == 0, 1.0, -1.0)
    fr = np.arange(T_DEV)[:, None]
    n = np.arange(T_DEV)[None, :]
    angle = 2.0 * np.pi * ((fr * n) % PERIOD) / PERIOD
    inv_re = 2.0 * np.cos(angle) / PERIOD
    inv_re[0, :] = 1.0 / PERIOD
    inv_im = -2.0 * np.sin(angle) / PERIOD
    inv_im[0, :] = np.where(np.arange(T_DEV) % 2 == 0, 1.0, -1.0) / PERIOD
    inverse = np.concatenate([inv_re, inv_im], axis=0).astype(np.float32)
    return split_bf16(forward), jnp.asarray(inverse)


def transform(blocks, forward, spec="kct,tf->kcf"):
    hi, lo = forward
    return jnp.einsum(spec, blocks, hi, preferred_element_type=jnp.float32) + jnp.einsum(
        spec, blocks, lo, preferred_element_type=jnp.float32
    )


def kernel_spectra(tap_blocks, forward):
    spectra = transform(tap_blocks, forward)
    column = jnp.arange(PERIOD, dtype=jnp.int32) % T_DEV
    signs = jnp.where(column % 2 == 0, 1.0, -1.0).astype(jnp.float32)
    return spectra[1:] + signs * spectra[:-1]


def products(x_spec, g_spec):
    xr, xi = x_spec[..., :T_DEV], x_spec[..., T_DEV:]
    gr, gi = g_spec[..., :T_DEV], g_spec[..., T_DEV:]
    return (
        jnp.sum(xr * gr, axis=0),
        jnp.sum(xi * gi, axis=0),
        jnp.sum(xr * gi, axis=0),
        jnp.sum(xi * gr, axis=0),
    )


def by_gather(arrivals, counts, short_taps, filter_taps, skip_gain, out_weight):
    n_ctx = lax.axis_size("ctx")
    device = lax.axis_index("ctx")
    channels = arrivals.shape[1]
    capacity = arrivals.shape[2]
    n_blocks = filter_taps.shape[1] // T_DEV
    forward, inverse = dft_tables()

    every_count = lax.all_gather(counts, "ctx", axis=0, tiled=True)
    earlier = jnp.arange(n_ctx, dtype=jnp.int32) < device
    offset = jnp.sum(jnp.where(earlier, every_count, 0))
    count = counts[0]

    frame = 2 * T_DEV
    row = jnp.arange(capacity, dtype=jnp.int32)[:, None]
    col = jnp.arange(frame, dtype=jnp.int32)[None, :]
    shift = offset - device * T_DEV + HALF
    select = ((row + shift == col) & (row < count)).astype(jnp.bfloat16)
    placed = jnp.einsum(
        "pcr,rj->pcj", arrivals, select, preferred_element_type=jnp.float32
    ).astype(jnp.bfloat16)
    to_prev = placed[:, :, :HALF]
    to_next = placed[:, :, frame - HALF - 2 :]
    from_next = lax.ppermute(to_prev, "ctx", [(i + 1, i) for i in range(n_ctx - 1)])
    from_prev = lax.ppermute(to_next, "ctx", [(i, i + 1) for i in range(n_ctx - 1)])
    window = placed[:, :, HALF - 2 : HALF + T_DEV]
    window = window + jnp.pad(from_prev, ((0, 0), (0, 0), (0, T_DEV - HALF)))
    window = window + jnp.pad(from_next, ((0, 0), (0, 0), (T_DEV + 2 - HALF, 0)))
    wide = window.astype(jnp.float32)
    shorted = short_taps[:, 0, :, None] * wide[:, :, 2:]
    shorted = shorted + short_taps[:, 1, :, None] * wide[:, :, 1:-1]
    shorted = shorted + short_taps[:, 2, :, None] * wide[:, :, :-2]
    mixed_input = (shorted[1] * shorted[2]).astype(jnp.bfloat16)

    tap_blocks = jnp.stack(
        [jnp.zeros((channels, T_DEV), filter_taps.dtype)]
        + [filter_taps[:, k * T_DEV : (k + 1) * T_DEV] for k in range(n_blocks)]
    )
    every_input = lax.all_gather(mixed_input, "ctx", axis=0)
    backwards = jnp.concatenate(
        [jnp.flip(every_input, 0), jnp.zeros_like(every_input)], axis=0
    )
    start = n_ctx - 1 - device
    if n_blocks <= GROUP:
        x_blocks = lax.dynamic_slice_in_dim(backwards, start, n_blocks, 0)
        sums = products(transform(x_blocks, forward), kernel_spectra(tap_blocks, forward))
    else:
        width = max(w for w in range(1, GROUP + 1) if n_blocks % w == 0)

        def group(g, acc):
            k0 = g * width
            x_blocks = lax.dynamic_slice_in_dim(backwards, start + k0, width, 0)
            taps = lax.dynamic_slice_in_dim(tap_blocks, k0, width + 1, 0)
            part = products(transform(x_blocks, forward), kernel_spectra(taps, forward))
            return tuple(a + b for a, b in zip(acc, part))

        zero = jnp.zeros((channels, T_DEV), jnp.float32)
        sums = lax.fori_loop(0, n_blocks // width, group, (zero, zero, zero, zero))
    rr, ii, ri, ir = sums
    first = jnp.arange(T_DEV, dtype=jnp.int32)[None, :] == 0
    spec_re = jnp.where(first, rr, rr - ii)
    spec_im = jnp.where(first, ii, ri + ir)
    spectrum = jnp.concatenate([spec_re, spec_im], axis=1)
    conv_core = jnp.dot(spectrum, inverse, precision=lax.Precision.HIGHEST)
    conv = conv_core + skip_gain[:, None] * mixed_input.astype(jnp.float32)
    gated = (shorted[0] * conv).astype(jnp.bfloat16)
    mixed = jnp.dot(
        out_weight,
        lax.all_gather(gated, "ch", axis=0, tiled=True),
        preferred_element_type=jnp.float32,
    )
    return mixed.astype(jnp.bfloat16)


def by_transpose(arrivals, counts, short_taps, filter_taps, skip_gain, out_weight):
    n_ctx = lax.axis_size("ctx")
    device = lax.axis_index("ctx")
    channels = arrivals.shape[1]
    capacity = arrivals.shape[2]
    length = filter_taps.shape[1]
    n_blocks = length // T_DEV
    own = channels // n_ctx
    forward, inverse = dft_tables()

    rows = lax.all_to_all(arrivals.reshape(3, n_ctx, own, capacity), "ctx", 1, 1, tiled=False)
    every_count = lax.all_gather(counts, "ctx", axis=0, tiled=True)
    offsets = jnp.cumsum(every_count) - every_count

    frame = 3 * T_DEV
    row = jnp.arange(capacity, dtype=jnp.int32)[None, :, None]
    col = jnp.arange(frame, dtype=jnp.int32)[None, None, :]
    sampler = jnp.arange(n_ctx, dtype=jnp.int32)[:, None, None]
    shift = offsets[:, None, None] - (sampler - 1) * T_DEV
    select = ((row + shift == col) & (row < every_count[:, None, None])).astype(jnp.bfloat16)
    placed = jnp.einsum("picr,irj->ipcj", rows, select, preferred_element_type=jnp.bfloat16)
    full = sum(
        jnp.pad(placed[i], ((0, 0), (0, 0), (i * T_DEV, (n_ctx - 1 - i) * T_DEV)))
        for i in range(n_ctx)
    )
    wide = full[:, :, T_DEV - 2 : T_DEV + length]
    first = device * own
    taps = lax.dynamic_slice_in_dim(short_taps, first, own, 2)
    shorted = taps[:, 0, :, None] * wide[:, :, 2:]
    shorted = shorted + taps[:, 1, :, None] * wide[:, :, 1:-1]
    shorted = shorted + taps[:, 2, :, None] * wide[:, :, :-2]
    mixed_input = (shorted[1] * shorted[2]).astype(jnp.bfloat16)

    x_spec = transform(mixed_input.reshape(own, n_blocks, T_DEV), forward, "cnt,tf->cnf")
    own_taps = lax.dynamic_slice_in_dim(filter_taps, first, own, 0)
    tap_blocks = jnp.concatenate(
        [jnp.zeros((own, T_DEV), own_taps.dtype), own_taps], axis=1
    ).reshape(own, n_blocks + 1, T_DEV)
    h_spec = transform(tap_blocks, forward, "cnt,tf->cnf")
    column = jnp.arange(PERIOD, dtype=jnp.int32) % T_DEV
    signs = jnp.where(column % 2 == 0, 1.0, -1.0).astype(jnp.float32)
    g_spec = h_spec[:, 1:] + signs * h_spec[:, :-1]
    xr, xi = x_spec[..., :T_DEV], x_spec[..., T_DEV:]
    gr, gi = g_spec[..., :T_DEV], g_spec[..., T_DEV:]
    sums = [jnp.zeros((own, n_blocks, T_DEV), jnp.float32) for _ in range(4)]
    for k in range(n_blocks):
        pad = ((0, 0), (k, 0), (0, 0))
        terms = (
            xr[:, : n_blocks - k] * gr[:, k : k + 1],
            xi[:, : n_blocks - k] * gi[:, k : k + 1],
            xr[:, : n_blocks - k] * gi[:, k : k + 1],
            xi[:, : n_blocks - k] * gr[:, k : k + 1],
        )
        sums = [s + jnp.pad(t, pad) for s, t in zip(sums, terms)]
    rr, ii, ri, ir = sums
    at_zero = jnp.arange(T_DEV, dtype=jnp.int32)[None, None, :] == 0
    spectrum = jnp.concatenate(
        [jnp.where(at_zero, rr, rr - ii), jnp.where(at_zero, ii, ri + ir)], axis=2
    )
    conv_core = jnp.einsum("cnf,ft->cnt", spectrum, inverse, precision=lax.Precision.HIGHEST)
    gains = lax.dynamic_slice_in_dim(skip_gain, first, own, 0)
    conv = conv_core.reshape(own, length) + gains[:, None] * mixed_input.astype(jnp.float32)
    gated = (shorted[0] * conv).astype(jnp.bfloat16)
    back = lax.all_to_all(gated.reshape(own, n_ctx, T_DEV), "ctx", 1, 0, tiled=False)
    gated_block = back.reshape(channels, T_DEV)
    mixed = jnp.dot(
        out_weight,
        lax.all_gather(gated_block, "ch", axis=0, tiled=True),
        preferred_element_type=jnp.float32,
    )
    return mixed.astype(jnp.bfloat16)


def on_device(arrivals, counts, short_taps, filter_taps, skip_gain, out_weight):
    n_ctx = lax.axis_size("ctx")
    blocks = filter_taps.shape[1] // T_DEV
    if arrivals.shape[1] % n_ctx == 0 and blocks == n_ctx:
        return by_transpose(arrivals, counts, short_taps, filter_taps, skip_gain, out_weight)
    return by_gather(arrivals, counts, short_taps, filter_taps, skip_gain, out_weight)


def solution(mesh):
    return jax.shard_map(
        on_device,
        mesh=mesh,
        in_specs=(
            P(None, "ch", "ctx"),
            P("ctx"),
            P(None, None, "ch"),
            P("ch", None),
            P("ch"),
            P("ch", None),
        ),
        out_specs=P("ch", "ctx"),
        check_vma=False,
    )
```

```python
import math

import jax
import jax.numpy as jnp
import ml_dtypes
import numpy as np
from jax import lax
from jax.sharding import PartitionSpec as P

T_DEV = 256
HALF = T_DEV // 2
PERIOD = 2 * T_DEV
GROUP = 8


def split_bf16(table):
    hi = table.astype(ml_dtypes.bfloat16)
    lo = (table - hi.astype(np.float64)).astype(ml_dtypes.bfloat16)
    return jnp.asarray(hi), jnp.asarray(lo)


def dft_tables():
    t = np.arange(T_DEV)[:, None]
    f = np.arange(T_DEV)[None, :]
    angle = 2.0 * np.pi * ((t * f) % PERIOD) / PERIOD
    forward = np.concatenate([np.cos(angle), -np.sin(angle)], axis=1)
    forward[:, T_DEV] = np.where(np.arange(T_DEV) % 2 == 0, 1.0, -1.0)
    fr = np.arange(T_DEV)[:, None]
    n = np.arange(T_DEV)[None, :]
    angle = 2.0 * np.pi * ((fr * n) % PERIOD) / PERIOD
    inv_re = 2.0 * np.cos(angle) / PERIOD
    inv_re[0, :] = 1.0 / PERIOD
    inv_im = -2.0 * np.sin(angle) / PERIOD
    inv_im[0, :] = np.where(np.arange(T_DEV) % 2 == 0, 1.0, -1.0) / PERIOD
    inverse = np.concatenate([inv_re, inv_im], axis=0).astype(np.float32)
    return split_bf16(forward), jnp.asarray(inverse)


def transform(blocks, forward, spec="kct,tf->kcf"):
    hi, lo = forward
    return jnp.einsum(spec, blocks, hi, preferred_element_type=jnp.float32) + jnp.einsum(
        spec, blocks, lo, preferred_element_type=jnp.float32
    )


def kernel_spectra(tap_blocks, forward):
    spectra = transform(tap_blocks, forward)
    column = jnp.arange(PERIOD, dtype=jnp.int32) % T_DEV
    signs = jnp.where(column % 2 == 0, 1.0, -1.0).astype(jnp.float32)
    return spectra[1:] + signs * spectra[:-1]


def products(x_spec, g_spec):
    xr, xi = x_spec[..., :T_DEV], x_spec[..., T_DEV:]
    gr, gi = g_spec[..., :T_DEV], g_spec[..., T_DEV:]
    return (
        jnp.sum(xr * gr, axis=0),
        jnp.sum(xi * gi, axis=0),
        jnp.sum(xr * gi, axis=0),
        jnp.sum(xi * gr, axis=0),
    )


def by_gather(arrivals, counts, short_taps, filter_taps, skip_gain, out_weight):
    n_ctx = lax.axis_size("ctx")
    device = lax.axis_index("ctx")
    channels = arrivals.shape[1]
    capacity = arrivals.shape[2]
    n_blocks = filter_taps.shape[1] // T_DEV
    forward, inverse = dft_tables()

    every_count = lax.all_gather(counts, "ctx", axis=0, tiled=True)
    earlier = jnp.arange(n_ctx, dtype=jnp.int32) < device
    offset = jnp.sum(jnp.where(earlier, every_count, 0))
    count = counts[0]

    frame = 2 * T_DEV
    row = jnp.arange(capacity, dtype=jnp.int32)[:, None]
    col = jnp.arange(frame, dtype=jnp.int32)[None, :]
    shift = offset - device * T_DEV + HALF
    select = ((row + shift == col) & (row < count)).astype(jnp.bfloat16)
    placed = jnp.einsum(
        "pcr,rj->pcj", arrivals, select, preferred_element_type=jnp.float32
    ).astype(jnp.bfloat16)
    to_prev = placed[:, :, :HALF]
    to_next = placed[:, :, frame - HALF - 2 :]
    from_next = lax.ppermute(to_prev, "ctx", [(i + 1, i) for i in range(n_ctx - 1)])
    from_prev = lax.ppermute(to_next, "ctx", [(i, i + 1) for i in range(n_ctx - 1)])
    window = placed[:, :, HALF - 2 : HALF + T_DEV]
    window = window + jnp.pad(from_prev, ((0, 0), (0, 0), (0, T_DEV - HALF)))
    window = window + jnp.pad(from_next, ((0, 0), (0, 0), (T_DEV + 2 - HALF, 0)))
    wide = window.astype(jnp.float32)
    shorted = short_taps[:, 0, :, None] * wide[:, :, 2:]
    shorted = shorted + short_taps[:, 1, :, None] * wide[:, :, 1:-1]
    shorted = shorted + short_taps[:, 2, :, None] * wide[:, :, :-2]
    mixed_input = (shorted[1] * shorted[2]).astype(jnp.bfloat16)

    tap_blocks = jnp.stack(
        [jnp.zeros((channels, T_DEV), filter_taps.dtype)]
        + [filter_taps[:, k * T_DEV : (k + 1) * T_DEV] for k in range(n_blocks)]
    )
    every_input = lax.all_gather(mixed_input, "ctx", axis=0)
    backwards = jnp.concatenate(
        [jnp.flip(every_input, 0), jnp.zeros_like(every_input)], axis=0
    )
    start = n_ctx - 1 - device
    if n_blocks <= GROUP:
        x_blocks = lax.dynamic_slice_in_dim(backwards, start, n_blocks, 0)
        sums = products(transform(x_blocks, forward), kernel_spectra(tap_blocks, forward))
    else:
        width = max(w for w in range(1, GROUP + 1) if n_blocks % w == 0)

        def group(g, acc):
            k0 = g * width
            x_blocks = lax.dynamic_slice_in_dim(backwards, start + k0, width, 0)
            taps = lax.dynamic_slice_in_dim(tap_blocks, k0, width + 1, 0)
            part = products(transform(x_blocks, forward), kernel_spectra(taps, forward))
            return tuple(a + b for a, b in zip(acc, part))

        zero = jnp.zeros((channels, T_DEV), jnp.float32)
        sums = lax.fori_loop(0, n_blocks // width, group, (zero, zero, zero, zero))
    rr, ii, ri, ir = sums
    first = jnp.arange(T_DEV, dtype=jnp.int32)[None, :] == 0
    spec_re = jnp.where(first, rr, rr - ii)
    spec_im = jnp.where(first, ii, ri + ir)
    spectrum = jnp.concatenate([spec_re, spec_im], axis=1)
    conv_core = jnp.dot(spectrum, inverse, precision=lax.Precision.HIGHEST)
    conv = conv_core + skip_gain[:, None] * mixed_input.astype(jnp.float32)
    gated = (shorted[0] * conv).astype(jnp.bfloat16)
    mixed = jnp.dot(
        out_weight,
        lax.all_gather(gated, "ch", axis=0, tiled=True),
        preferred_element_type=jnp.float32,
    )
    return mixed.astype(jnp.bfloat16)


def by_transpose(arrivals, counts, short_taps, filter_taps, skip_gain, out_weight):
    n_ctx = lax.axis_size("ctx")
    device = lax.axis_index("ctx")
    channels = arrivals.shape[1]
    capacity = arrivals.shape[2]
    length = filter_taps.shape[1]
    n_blocks = length // T_DEV
    own = channels // n_ctx
    forward, inverse = dft_tables()

    count = counts[0]
    pair = arrivals[1:].astype(jnp.float32)
    ahead = jnp.pad(pair, ((0, 0), (0, 0), (2, 0)))
    near = short_taps[1:, 0, :, None] * ahead[:, :, 2:]
    near = near + short_taps[1:, 1, :, None] * ahead[:, :, 1:-1]
    near = near + short_taps[1:, 2, :, None] * ahead[:, :, :-2]
    own_mixed = (near[0] * near[1]).astype(jnp.bfloat16)
    row = jnp.arange(capacity, dtype=jnp.int32)
    last = jnp.stack(
        [jnp.sum(jnp.where(row == count - 2 + k, pair, 0.0), axis=2) for k in range(2)], axis=2
    )
    edge = jnp.concatenate(
        [pair[0, :, :2], pair[1, :, :2], last[0], last[1]], axis=1
    ).astype(jnp.bfloat16)
    code = jnp.stack([count // 16, count % 16]).astype(jnp.bfloat16)
    edge_row = jnp.concatenate(
        [
            edge.reshape(n_ctx, own * 8),
            jnp.broadcast_to(code, (n_ctx, 2)),
            jnp.zeros((n_ctx, capacity - own * 8 - 2), jnp.bfloat16),
        ],
        axis=1,
    )
    payload = jnp.concatenate(
        [
            arrivals[0].reshape(n_ctx, own, capacity),
            own_mixed.reshape(n_ctx, own, capacity),
            edge_row[:, None, :],
        ],
        axis=1,
    )
    got = lax.all_to_all(payload, "ctx", 0, 0, tiled=False)
    rows = got[:, : 2 * own]
    edge_in = got[:, 2 * own]
    every_count = (
        edge_in[:, own * 8].astype(jnp.int32) * 16 + edge_in[:, own * 8 + 1].astype(jnp.int32)
    )
    offsets = jnp.cumsum(every_count) - every_count

    frame = 3 * T_DEV
    row = jnp.arange(capacity, dtype=jnp.int32)[None, :, None]
    col = jnp.arange(frame, dtype=jnp.int32)[None, None, :]
    sampler = jnp.arange(n_ctx, dtype=jnp.int32)[:, None, None]
    shift = offsets[:, None, None] - (sampler - 1) * T_DEV
    select = ((row + shift == col) & (row < every_count[:, None, None])).astype(jnp.bfloat16)
    placed = jnp.einsum("icr,irj->icj", rows, select, preferred_element_type=jnp.bfloat16)
    full = sum(
        jnp.pad(placed[i], ((0, 0), (i * T_DEV, (n_ctx - 1 - i) * T_DEV))) for i in range(n_ctx)
    )
    first = device * own
    taps = lax.dynamic_slice_in_dim(short_taps, first, own, 2)
    gate = full[:own, T_DEV - 2 : T_DEV + length].astype(jnp.float32)
    shorted_gate = taps[0, 0, :, None] * gate[:, 2:]
    shorted_gate = shorted_gate + taps[0, 1, :, None] * gate[:, 1:-1]
    shorted_gate = shorted_gate + taps[0, 2, :, None] * gate[:, :-2]
    from_senders = full[own:, T_DEV : T_DEV + length]

    values = edge_in[:, : own * 8].reshape(n_ctx, own, 8)
    count_col = every_count[:, None]
    at_row = jnp.concatenate(
        [jnp.zeros_like(count_col), jnp.ones_like(count_col), count_col - 2, count_col - 1], axis=1
    )
    valid = jnp.concatenate([at_row[:, :2] < count_col, at_row[:, 2:] >= 2], axis=1)
    spot = offsets[:, None] + at_row
    slot = jnp.arange(length + 2, dtype=jnp.int32)[None, None, :]
    marks = ((slot - 2 == spot[:, :, None]) & valid[:, :, None]).astype(jnp.bfloat16)
    near_in = []
    for part in range(2):
        pick = values[:, :, jnp.array([2 * part, 2 * part + 1, 4 + 2 * part, 5 + 2 * part])]
        around = jnp.einsum(
            "ics,isj->cj", pick, marks, preferred_element_type=jnp.float32
        )
        s = taps[1 + part, 0, :, None] * around[:, 2:]
        s = s + taps[1 + part, 1, :, None] * around[:, 1:-1]
        s = s + taps[1 + part, 2, :, None] * around[:, :-2]
        near_in.append(s)
    at_start = jnp.sum(marks[:, :2, 2:].astype(jnp.float32), axis=(0, 1)) > 0
    mixed_input = jnp.where(
        at_start[None, :], (near_in[0] * near_in[1]).astype(jnp.bfloat16), from_senders
    )

    x_spec = transform(mixed_input.reshape(own, n_blocks, T_DEV), forward, "cnt,tf->cnf")
    own_taps = lax.dynamic_slice_in_dim(filter_taps, first, own, 0)
    tap_blocks = jnp.concatenate(
        [jnp.zeros((own, T_DEV), own_taps.dtype), own_taps], axis=1
    ).reshape(own, n_blocks + 1, T_DEV)
    h_spec = transform(tap_blocks, forward, "cnt,tf->cnf")
    column = jnp.arange(PERIOD, dtype=jnp.int32) % T_DEV
    signs = jnp.where(column % 2 == 0, 1.0, -1.0).astype(jnp.float32)
    g_spec = h_spec[:, 1:] + signs * h_spec[:, :-1]
    xr, xi = x_spec[..., :T_DEV], x_spec[..., T_DEV:]
    gr, gi = g_spec[..., :T_DEV], g_spec[..., T_DEV:]
    sums = [jnp.zeros((own, n_blocks, T_DEV), jnp.float32) for _ in range(4)]
    for k in range(n_blocks):
        pad = ((0, 0), (k, 0), (0, 0))
        terms = (
            xr[:, : n_blocks - k] * gr[:, k : k + 1],
            xi[:, : n_blocks - k] * gi[:, k : k + 1],
            xr[:, : n_blocks - k] * gi[:, k : k + 1],
            xi[:, : n_blocks - k] * gr[:, k : k + 1],
        )
        sums = [s + jnp.pad(t, pad) for s, t in zip(sums, terms)]
    rr, ii, ri, ir = sums
    at_zero = jnp.arange(T_DEV, dtype=jnp.int32)[None, None, :] == 0
    spectrum = jnp.concatenate(
        [jnp.where(at_zero, rr, rr - ii), jnp.where(at_zero, ii, ri + ir)], axis=2
    )
    conv_core = jnp.einsum("cnf,ft->cnt", spectrum, inverse, precision=lax.Precision.HIGHEST)
    gains = lax.dynamic_slice_in_dim(skip_gain, first, own, 0)
    conv = conv_core.reshape(own, length) + gains[:, None] * mixed_input.astype(jnp.float32)
    gated = (shorted_gate * conv).astype(jnp.bfloat16)
    back = lax.all_to_all(gated.reshape(own, n_ctx, T_DEV), "ctx", 1, 0, tiled=False)
    gated_block = back.reshape(channels, T_DEV)
    mixed = jnp.dot(
        out_weight,
        lax.all_gather(gated_block, "ch", axis=0, tiled=True),
        preferred_element_type=jnp.float32,
    )
    return mixed.astype(jnp.bfloat16)


def on_device(arrivals, counts, short_taps, filter_taps, skip_gain, out_weight):
    n_ctx = lax.axis_size("ctx")
    blocks = filter_taps.shape[1] // T_DEV
    if arrivals.shape[1] % n_ctx == 0 and blocks == n_ctx:
        return by_transpose(arrivals, counts, short_taps, filter_taps, skip_gain, out_weight)
    return by_gather(arrivals, counts, short_taps, filter_taps, skip_gain, out_weight)


def solution(mesh):
    return jax.shard_map(
        on_device,
        mesh=mesh,
        in_specs=(
            P(None, "ch", "ctx"),
            P("ctx"),
            P(None, None, "ch"),
            P("ch", None),
            P("ch"),
            P("ch", None),
        ),
        out_specs=P("ch", "ctx"),
        check_vma=False,
    )
```

```python
import functools
import math

import jax
import jax.numpy as jnp
import ml_dtypes
import numpy as np
from jax import lax
from jax.experimental import pallas as pl
from jax.experimental.pallas import tpu as pltpu
from jax.sharding import PartitionSpec as P

T_DEV = 256
HALF = T_DEV // 2
PERIOD = 2 * T_DEV
GROUP = 8
EDGE = 128


def split_bf16(table):
    hi = table.astype(ml_dtypes.bfloat16)
    lo = (table - hi.astype(np.float64)).astype(ml_dtypes.bfloat16)
    return jnp.asarray(hi), jnp.asarray(lo)


def dft_tables():
    t = np.arange(T_DEV)[:, None]
    f = np.arange(T_DEV)[None, :]
    angle = 2.0 * np.pi * ((t * f) % PERIOD) / PERIOD
    forward = np.concatenate([np.cos(angle), -np.sin(angle)], axis=1)
    forward[:, T_DEV] = np.where(np.arange(T_DEV) % 2 == 0, 1.0, -1.0)
    fr = np.arange(T_DEV)[:, None]
    n = np.arange(T_DEV)[None, :]
    angle = 2.0 * np.pi * ((fr * n) % PERIOD) / PERIOD
    inv_re = 2.0 * np.cos(angle) / PERIOD
    inv_re[0, :] = 1.0 / PERIOD
    inv_im = -2.0 * np.sin(angle) / PERIOD
    inv_im[0, :] = np.where(np.arange(T_DEV) % 2 == 0, 1.0, -1.0) / PERIOD
    inverse = np.concatenate([inv_re, inv_im], axis=0).astype(np.float32)
    return split_bf16(forward), jnp.asarray(inverse)


def transform(blocks, forward, spec="kct,tf->kcf"):
    hi, lo = forward
    return jnp.einsum(spec, blocks, hi, preferred_element_type=jnp.float32) + jnp.einsum(
        spec, blocks, lo, preferred_element_type=jnp.float32
    )


def kernel_spectra(tap_blocks, forward):
    spectra = transform(tap_blocks, forward)
    column = jnp.arange(PERIOD, dtype=jnp.int32) % T_DEV
    signs = jnp.where(column % 2 == 0, 1.0, -1.0).astype(jnp.float32)
    return spectra[1:] + signs * spectra[:-1]


def products(x_spec, g_spec):
    xr, xi = x_spec[..., :T_DEV], x_spec[..., T_DEV:]
    gr, gi = g_spec[..., :T_DEV], g_spec[..., T_DEV:]
    return (
        jnp.sum(xr * gr, axis=0),
        jnp.sum(xi * gi, axis=0),
        jnp.sum(xr * gi, axis=0),
        jnp.sum(xi * gr, axis=0),
    )


def by_gather(arrivals, counts, short_taps, filter_taps, skip_gain, out_weight):
    n_ctx = lax.axis_size("ctx")
    device = lax.axis_index("ctx")
    channels = arrivals.shape[1]
    capacity = arrivals.shape[2]
    n_blocks = filter_taps.shape[1] // T_DEV
    forward, inverse = dft_tables()

    every_count = lax.all_gather(counts, "ctx", axis=0, tiled=True)
    earlier = jnp.arange(n_ctx, dtype=jnp.int32) < device
    offset = jnp.sum(jnp.where(earlier, every_count, 0))
    count = counts[0]

    frame = 2 * T_DEV
    row = jnp.arange(capacity, dtype=jnp.int32)[:, None]
    col = jnp.arange(frame, dtype=jnp.int32)[None, :]
    shift = offset - device * T_DEV + HALF
    select = ((row + shift == col) & (row < count)).astype(jnp.bfloat16)
    placed = jnp.einsum(
        "pcr,rj->pcj", arrivals, select, preferred_element_type=jnp.float32
    ).astype(jnp.bfloat16)
    to_prev = placed[:, :, :HALF]
    to_next = placed[:, :, frame - HALF - 2 :]
    from_next = lax.ppermute(to_prev, "ctx", [(i + 1, i) for i in range(n_ctx - 1)])
    from_prev = lax.ppermute(to_next, "ctx", [(i, i + 1) for i in range(n_ctx - 1)])
    window = placed[:, :, HALF - 2 : HALF + T_DEV]
    window = window + jnp.pad(from_prev, ((0, 0), (0, 0), (0, T_DEV - HALF)))
    window = window + jnp.pad(from_next, ((0, 0), (0, 0), (T_DEV + 2 - HALF, 0)))
    wide = window.astype(jnp.float32)
    shorted = short_taps[:, 0, :, None] * wide[:, :, 2:]
    shorted = shorted + short_taps[:, 1, :, None] * wide[:, :, 1:-1]
    shorted = shorted + short_taps[:, 2, :, None] * wide[:, :, :-2]
    mixed_input = (shorted[1] * shorted[2]).astype(jnp.bfloat16)

    tap_blocks = jnp.stack(
        [jnp.zeros((channels, T_DEV), filter_taps.dtype)]
        + [filter_taps[:, k * T_DEV : (k + 1) * T_DEV] for k in range(n_blocks)]
    )
    every_input = lax.all_gather(mixed_input, "ctx", axis=0)
    backwards = jnp.concatenate(
        [jnp.flip(every_input, 0), jnp.zeros_like(every_input)], axis=0
    )
    start = n_ctx - 1 - device
    if n_blocks <= GROUP:
        x_blocks = lax.dynamic_slice_in_dim(backwards, start, n_blocks, 0)
        sums = products(transform(x_blocks, forward), kernel_spectra(tap_blocks, forward))
    else:
        width = max(w for w in range(1, GROUP + 1) if n_blocks % w == 0)

        def group(g, acc):
            k0 = g * width
            x_blocks = lax.dynamic_slice_in_dim(backwards, start + k0, width, 0)
            taps = lax.dynamic_slice_in_dim(tap_blocks, k0, width + 1, 0)
            part = products(transform(x_blocks, forward), kernel_spectra(taps, forward))
            return tuple(a + b for a, b in zip(acc, part))

        zero = jnp.zeros((channels, T_DEV), jnp.float32)
        sums = lax.fori_loop(0, n_blocks // width, group, (zero, zero, zero, zero))
    rr, ii, ri, ir = sums
    first = jnp.arange(T_DEV, dtype=jnp.int32)[None, :] == 0
    spec_re = jnp.where(first, rr, rr - ii)
    spec_im = jnp.where(first, ii, ri + ir)
    spectrum = jnp.concatenate([spec_re, spec_im], axis=1)
    conv_core = jnp.dot(spectrum, inverse, precision=lax.Precision.HIGHEST)
    conv = conv_core + skip_gain[:, None] * mixed_input.astype(jnp.float32)
    gated = (shorted[0] * conv).astype(jnp.bfloat16)
    mixed = jnp.dot(
        out_weight,
        lax.all_gather(gated, "ch", axis=0, tiled=True),
        preferred_element_type=jnp.float32,
    )
    return mixed.astype(jnp.bfloat16)


def sender_kernel(count_ref, arrivals_ref, taps_ref, out_ref, *, n_ctx, own):
    count = count_ref[0]
    capacity = arrivals_ref.shape[2]
    lane = lax.broadcasted_iota(jnp.int32, arrivals_ref.shape[1:], 1)
    near = []
    firsts = []
    lasts = []
    for part in range(2):
        x = arrivals_ref[1 + part].astype(jnp.float32)
        back1 = jnp.where(lane >= 1, pltpu.roll(x, 1, 1), 0.0)
        back2 = jnp.where(lane >= 2, pltpu.roll(x, 2, 1), 0.0)
        s = taps_ref[3 * part] * x
        s = s + taps_ref[3 * part + 1] * back1
        s = s + taps_ref[3 * part + 2] * back2
        near.append(s)
        firsts += [x[:, 0:1], x[:, 1:2]]
        lasts += [
            jnp.sum(jnp.where(lane == count - 2 + k, x, 0.0), axis=1, keepdims=True)
            for k in range(2)
        ]
    mixed = (near[0] * near[1]).astype(jnp.bfloat16)
    edge_lane = lax.broadcasted_iota(jnp.int32, (arrivals_ref.shape[1], EDGE), 1)
    edge = jnp.zeros((arrivals_ref.shape[1], EDGE), jnp.float32)
    for k, value in enumerate(firsts[:2] + firsts[2:] + lasts[:2] + lasts[2:]):
        edge = jnp.where(edge_lane == k, value, edge)
    edge = jnp.where(edge_lane == 8, (count // 16).astype(jnp.float32), edge)
    edge = jnp.where(edge_lane == 9, (count % 16).astype(jnp.float32), edge)
    edge = edge.astype(jnp.bfloat16)
    for j in range(n_ctx):
        rows = slice(j * own, (j + 1) * own)
        out_ref[j, :own, :capacity] = arrivals_ref[0, rows, :]
        out_ref[j, :own, capacity:] = jnp.zeros((own, EDGE), jnp.bfloat16)
        out_ref[j, own:, :capacity] = mixed[rows]
        out_ref[j, own:, capacity:] = edge[rows]


def by_transpose(arrivals, counts, short_taps, filter_taps, skip_gain, out_weight):
    n_ctx = lax.axis_size("ctx")
    device = lax.axis_index("ctx")
    channels = arrivals.shape[1]
    capacity = arrivals.shape[2]
    length = filter_taps.shape[1]
    n_blocks = length // T_DEV
    own = channels // n_ctx
    forward, inverse = dft_tables()

    tap_column = short_taps[1:].reshape(6, channels)[:, :, None]
    payload = pl.pallas_call(
        functools.partial(sender_kernel, n_ctx=n_ctx, own=own),
        in_specs=[
            pl.BlockSpec(memory_space=pltpu.SMEM),
            pl.BlockSpec(memory_space=pltpu.VMEM),
            pl.BlockSpec(memory_space=pltpu.VMEM),
        ],
        out_specs=pl.BlockSpec(memory_space=pltpu.VMEM),
        out_shape=jax.ShapeDtypeStruct((n_ctx, 2 * own, capacity + EDGE), jnp.bfloat16),
    )(counts, arrivals, tap_column)
    got = lax.all_to_all(payload, "ctx", 0, 0, tiled=False)
    rows = got[:, :, :capacity]
    edge_in = got[:, own:, capacity:]
    every_count = edge_in[:, 0, 8].astype(jnp.int32) * 16 + edge_in[:, 0, 9].astype(jnp.int32)
    offsets = jnp.cumsum(every_count) - every_count

    frame = 3 * T_DEV
    row = jnp.arange(capacity, dtype=jnp.int32)[None, :, None]
    col = jnp.arange(frame, dtype=jnp.int32)[None, None, :]
    sampler = jnp.arange(n_ctx, dtype=jnp.int32)[:, None, None]
    shift = offsets[:, None, None] - (sampler - 1) * T_DEV
    select = ((row + shift == col) & (row < every_count[:, None, None])).astype(jnp.bfloat16)
    placed = jnp.einsum("icr,irj->icj", rows, select, preferred_element_type=jnp.bfloat16)
    full = sum(
        jnp.pad(placed[i], ((0, 0), (i * T_DEV, (n_ctx - 1 - i) * T_DEV))) for i in range(n_ctx)
    )
    first = device * own
    taps = lax.dynamic_slice_in_dim(short_taps, first, own, 2)
    gate = full[:own, T_DEV - 2 : T_DEV + length].astype(jnp.float32)
    shorted_gate = taps[0, 0, :, None] * gate[:, 2:]
    shorted_gate = shorted_gate + taps[0, 1, :, None] * gate[:, 1:-1]
    shorted_gate = shorted_gate + taps[0, 2, :, None] * gate[:, :-2]
    from_senders = full[own:, T_DEV : T_DEV + length]

    values = edge_in[:, :, :8]
    count_col = every_count[:, None]
    at_row = jnp.concatenate(
        [jnp.zeros_like(count_col), jnp.ones_like(count_col), count_col - 2, count_col - 1], axis=1
    )
    valid = jnp.concatenate([at_row[:, :2] < count_col, at_row[:, 2:] >= 2], axis=1)
    spot = offsets[:, None] + at_row
    slot = jnp.arange(length + 2, dtype=jnp.int32)[None, None, :]
    marks = ((slot - 2 == spot[:, :, None]) & valid[:, :, None]).astype(jnp.bfloat16)
    near_in = []
    for part in range(2):
        pick = jnp.concatenate(
            [values[:, :, 2 * part : 2 * part + 2], values[:, :, 4 + 2 * part : 6 + 2 * part]], axis=2
        )
        around = jnp.einsum(
            "ics,isj->cj", pick, marks, preferred_element_type=jnp.float32
        )
        s = taps[1 + part, 0, :, None] * around[:, 2:]
        s = s + taps[1 + part, 1, :, None] * around[:, 1:-1]
        s = s + taps[1 + part, 2, :, None] * around[:, :-2]
        near_in.append(s)
    at_start = jnp.sum(marks[:, :2, 2:].astype(jnp.float32), axis=(0, 1)) > 0
    mixed_input = jnp.where(
        at_start[None, :], (near_in[0] * near_in[1]).astype(jnp.bfloat16), from_senders
    )

    x_spec = transform(mixed_input.reshape(own, n_blocks, T_DEV), forward, "cnt,tf->cnf")
    own_taps = lax.dynamic_slice_in_dim(filter_taps, first, own, 0)
    tap_blocks = jnp.concatenate(
        [jnp.zeros((own, T_DEV), own_taps.dtype), own_taps], axis=1
    ).reshape(own, n_blocks + 1, T_DEV)
    h_spec = transform(tap_blocks, forward, "cnt,tf->cnf")
    column = jnp.arange(PERIOD, dtype=jnp.int32) % T_DEV
    signs = jnp.where(column % 2 == 0, 1.0, -1.0).astype(jnp.float32)
    g_spec = h_spec[:, 1:] + signs * h_spec[:, :-1]
    xr, xi = x_spec[..., :T_DEV], x_spec[..., T_DEV:]
    gr, gi = g_spec[..., :T_DEV], g_spec[..., T_DEV:]
    sums = [jnp.zeros((own, n_blocks, T_DEV), jnp.float32) for _ in range(4)]
    for k in range(n_blocks):
        pad = ((0, 0), (k, 0), (0, 0))
        terms = (
            xr[:, : n_blocks - k] * gr[:, k : k + 1],
            xi[:, : n_blocks - k] * gi[:, k : k + 1],
            xr[:, : n_blocks - k] * gi[:, k : k + 1],
            xi[:, : n_blocks - k] * gr[:, k : k + 1],
        )
        sums = [s + jnp.pad(t, pad) for s, t in zip(sums, terms)]
    rr, ii, ri, ir = sums
    at_zero = jnp.arange(T_DEV, dtype=jnp.int32)[None, None, :] == 0
    spectrum = jnp.concatenate(
        [jnp.where(at_zero, rr, rr - ii), jnp.where(at_zero, ii, ri + ir)], axis=2
    )
    conv_core = jnp.einsum("cnf,ft->cnt", spectrum, inverse, precision=lax.Precision.HIGHEST)
    gains = lax.dynamic_slice_in_dim(skip_gain, first, own, 0)
    conv = conv_core.reshape(own, length) + gains[:, None] * mixed_input.astype(jnp.float32)
    gated = (shorted_gate * conv).astype(jnp.bfloat16)
    back = lax.all_to_all(gated.reshape(own, n_ctx, T_DEV), "ctx", 1, 0, tiled=False)
    gated_block = back.reshape(channels, T_DEV)
    mixed = jnp.dot(
        out_weight,
        lax.all_gather(gated_block, "ch", axis=0, tiled=True),
        preferred_element_type=jnp.float32,
    )
    return mixed.astype(jnp.bfloat16)


def on_device(arrivals, counts, short_taps, filter_taps, skip_gain, out_weight):
    n_ctx = lax.axis_size("ctx")
    blocks = filter_taps.shape[1] // T_DEV
    if arrivals.shape[1] % n_ctx == 0 and blocks == n_ctx:
        return by_transpose(arrivals, counts, short_taps, filter_taps, skip_gain, out_weight)
    return by_gather(arrivals, counts, short_taps, filter_taps, skip_gain, out_weight)


def solution(mesh):
    return jax.shard_map(
        on_device,
        mesh=mesh,
        in_specs=(
            P(None, "ch", "ctx"),
            P("ctx"),
            P(None, None, "ch"),
            P("ch", None),
            P("ch"),
            P("ch", None),
        ),
        out_specs=P("ch", "ctx"),
        check_vma=False,
    )
```

```python
import functools
import math

import jax
import jax.numpy as jnp
import ml_dtypes
import numpy as np
from jax import lax
from jax.experimental import pallas as pl
from jax.experimental.pallas import tpu as pltpu
from jax.sharding import PartitionSpec as P

T_DEV = 256
HALF = T_DEV // 2
PERIOD = 2 * T_DEV
GROUP = 8
EDGE = 128


def split_bf16(table):
    hi = table.astype(ml_dtypes.bfloat16)
    lo = (table - hi.astype(np.float64)).astype(ml_dtypes.bfloat16)
    return jnp.asarray(hi), jnp.asarray(lo)


def dft_tables():
    t = np.arange(T_DEV)[:, None]
    f = np.arange(T_DEV)[None, :]
    angle = 2.0 * np.pi * ((t * f) % PERIOD) / PERIOD
    forward = np.concatenate([np.cos(angle), -np.sin(angle)], axis=1)
    forward[:, T_DEV] = np.where(np.arange(T_DEV) % 2 == 0, 1.0, -1.0)
    fr = np.arange(T_DEV)[:, None]
    n = np.arange(T_DEV)[None, :]
    angle = 2.0 * np.pi * ((fr * n) % PERIOD) / PERIOD
    inv_re = 2.0 * np.cos(angle) / PERIOD
    inv_re[0, :] = 1.0 / PERIOD
    inv_im = -2.0 * np.sin(angle) / PERIOD
    inv_im[0, :] = np.where(np.arange(T_DEV) % 2 == 0, 1.0, -1.0) / PERIOD
    inverse = np.concatenate([inv_re, inv_im], axis=0).astype(np.float32)
    return split_bf16(forward), jnp.asarray(inverse)


def transform(blocks, forward, spec="kct,tf->kcf"):
    hi, lo = forward
    return jnp.einsum(spec, blocks, hi, preferred_element_type=jnp.float32) + jnp.einsum(
        spec, blocks, lo, preferred_element_type=jnp.float32
    )


def kernel_spectra(tap_blocks, forward):
    spectra = transform(tap_blocks, forward)
    column = jnp.arange(PERIOD, dtype=jnp.int32) % T_DEV
    signs = jnp.where(column % 2 == 0, 1.0, -1.0).astype(jnp.float32)
    return spectra[1:] + signs * spectra[:-1]


def products(x_spec, g_spec):
    xr, xi = x_spec[..., :T_DEV], x_spec[..., T_DEV:]
    gr, gi = g_spec[..., :T_DEV], g_spec[..., T_DEV:]
    return (
        jnp.sum(xr * gr, axis=0),
        jnp.sum(xi * gi, axis=0),
        jnp.sum(xr * gi, axis=0),
        jnp.sum(xi * gr, axis=0),
    )


def by_gather(arrivals, counts, short_taps, filter_taps, skip_gain, out_weight):
    n_ctx = lax.axis_size("ctx")
    device = lax.axis_index("ctx")
    channels = arrivals.shape[1]
    capacity = arrivals.shape[2]
    n_blocks = filter_taps.shape[1] // T_DEV
    forward, inverse = dft_tables()

    every_count = lax.all_gather(counts, "ctx", axis=0, tiled=True)
    earlier = jnp.arange(n_ctx, dtype=jnp.int32) < device
    offset = jnp.sum(jnp.where(earlier, every_count, 0))
    count = counts[0]

    frame = 2 * T_DEV
    row = jnp.arange(capacity, dtype=jnp.int32)[:, None]
    col = jnp.arange(frame, dtype=jnp.int32)[None, :]
    shift = offset - device * T_DEV + HALF
    select = ((row + shift == col) & (row < count)).astype(jnp.bfloat16)
    placed = jnp.einsum(
        "pcr,rj->pcj", arrivals, select, preferred_element_type=jnp.float32
    ).astype(jnp.bfloat16)
    to_prev = placed[:, :, :HALF]
    to_next = placed[:, :, frame - HALF - 2 :]
    from_next = lax.ppermute(to_prev, "ctx", [(i + 1, i) for i in range(n_ctx - 1)])
    from_prev = lax.ppermute(to_next, "ctx", [(i, i + 1) for i in range(n_ctx - 1)])
    window = placed[:, :, HALF - 2 : HALF + T_DEV]
    window = window + jnp.pad(from_prev, ((0, 0), (0, 0), (0, T_DEV - HALF)))
    window = window + jnp.pad(from_next, ((0, 0), (0, 0), (T_DEV + 2 - HALF, 0)))
    wide = window.astype(jnp.float32)
    shorted = short_taps[:, 0, :, None] * wide[:, :, 2:]
    shorted = shorted + short_taps[:, 1, :, None] * wide[:, :, 1:-1]
    shorted = shorted + short_taps[:, 2, :, None] * wide[:, :, :-2]
    mixed_input = (shorted[1] * shorted[2]).astype(jnp.bfloat16)

    tap_blocks = jnp.stack(
        [jnp.zeros((channels, T_DEV), filter_taps.dtype)]
        + [filter_taps[:, k * T_DEV : (k + 1) * T_DEV] for k in range(n_blocks)]
    )
    every_input = lax.all_gather(mixed_input, "ctx", axis=0)
    backwards = jnp.concatenate(
        [jnp.flip(every_input, 0), jnp.zeros_like(every_input)], axis=0
    )
    start = n_ctx - 1 - device
    if n_blocks <= GROUP:
        x_blocks = lax.dynamic_slice_in_dim(backwards, start, n_blocks, 0)
        sums = products(transform(x_blocks, forward), kernel_spectra(tap_blocks, forward))
    else:
        width = max(w for w in range(1, GROUP + 1) if n_blocks % w == 0)

        def group(g, acc):
            k0 = g * width
            x_blocks = lax.dynamic_slice_in_dim(backwards, start + k0, width, 0)
            taps = lax.dynamic_slice_in_dim(tap_blocks, k0, width + 1, 0)
            part = products(transform(x_blocks, forward), kernel_spectra(taps, forward))
            return tuple(a + b for a, b in zip(acc, part))

        zero = jnp.zeros((channels, T_DEV), jnp.float32)
        sums = lax.fori_loop(0, n_blocks // width, group, (zero, zero, zero, zero))
    rr, ii, ri, ir = sums
    first = jnp.arange(T_DEV, dtype=jnp.int32)[None, :] == 0
    spec_re = jnp.where(first, rr, rr - ii)
    spec_im = jnp.where(first, ii, ri + ir)
    spectrum = jnp.concatenate([spec_re, spec_im], axis=1)
    conv_core = jnp.dot(spectrum, inverse, precision=lax.Precision.HIGHEST)
    conv = conv_core + skip_gain[:, None] * mixed_input.astype(jnp.float32)
    gated = (shorted[0] * conv).astype(jnp.bfloat16)
    mixed = jnp.dot(
        out_weight,
        lax.all_gather(gated, "ch", axis=0, tiled=True),
        preferred_element_type=jnp.float32,
    )
    return mixed.astype(jnp.bfloat16)


def sender_kernel(count_ref, arrivals_ref, taps_ref, out_ref, *, n_ctx, own):
    count = count_ref[0]
    capacity = arrivals_ref.shape[2]
    lane = lax.broadcasted_iota(jnp.int32, arrivals_ref.shape[1:], 1)
    row = lax.broadcasted_iota(jnp.int32, (capacity, EDGE), 0)
    column = lax.broadcasted_iota(jnp.int32, (capacity, EDGE), 1)
    near = []
    edge = jnp.where(column[:1] == 8, (count // 16).astype(jnp.float32), 0.0)
    edge = jnp.where(column[:1] == 9, (count % 16).astype(jnp.float32), edge)
    for part in range(2):
        raw = arrivals_ref[1 + part]
        x = raw.astype(jnp.float32)
        back1 = jnp.where(lane >= 1, pltpu.roll(x, 1, 1), 0.0)
        back2 = jnp.where(lane >= 2, pltpu.roll(x, 2, 1), 0.0)
        s = taps_ref[:, 3 * part : 3 * part + 1] * x
        s = s + taps_ref[:, 3 * part + 1 : 3 * part + 2] * back1
        s = s + taps_ref[:, 3 * part + 2 : 3 * part + 3] * back2
        near.append(s)
        wanted = jnp.where(column >= 4, count - 2 + column - 4 - 2 * part, column - 2 * part)
        inside = (column % 4 >= 2 * part) & (column % 4 < 2 * part + 2) & (column < 8)
        pick = ((row == wanted) & inside).astype(jnp.bfloat16)
        edge = edge + jnp.dot(raw, pick, preferred_element_type=jnp.float32)
    mixed = (near[0] * near[1]).astype(jnp.bfloat16)
    edge = edge.astype(jnp.bfloat16)
    for j in range(n_ctx):
        rows = slice(j * own, (j + 1) * own)
        out_ref[j, :own, :capacity] = arrivals_ref[0, rows, :]
        out_ref[j, :own, capacity:] = jnp.zeros((own, EDGE), jnp.bfloat16)
        out_ref[j, own:, :capacity] = mixed[rows]
        out_ref[j, own:, capacity:] = edge[rows]


def by_transpose(arrivals, counts, short_taps, filter_taps, skip_gain, out_weight):
    n_ctx = lax.axis_size("ctx")
    device = lax.axis_index("ctx")
    channels = arrivals.shape[1]
    capacity = arrivals.shape[2]
    length = filter_taps.shape[1]
    n_blocks = length // T_DEV
    own = channels // n_ctx
    forward, inverse = dft_tables()

    tap_column = short_taps[1:].reshape(6, channels).T
    payload = pl.pallas_call(
        functools.partial(sender_kernel, n_ctx=n_ctx, own=own),
        in_specs=[
            pl.BlockSpec(memory_space=pltpu.SMEM),
            pl.BlockSpec(memory_space=pltpu.VMEM),
            pl.BlockSpec(memory_space=pltpu.VMEM),
        ],
        out_specs=pl.BlockSpec(memory_space=pltpu.VMEM),
        out_shape=jax.ShapeDtypeStruct((n_ctx, 2 * own, capacity + EDGE), jnp.bfloat16),
    )(counts, arrivals, tap_column)
    got = lax.all_to_all(payload, "ctx", 0, 0, tiled=False)
    rows = got[:, :, :capacity]
    edge_in = got[:, own:, capacity:]
    every_count = edge_in[:, 0, 8].astype(jnp.int32) * 16 + edge_in[:, 0, 9].astype(jnp.int32)
    offsets = jnp.cumsum(every_count) - every_count

    frame = 3 * T_DEV
    row = jnp.arange(capacity, dtype=jnp.int32)[None, :, None]
    col = jnp.arange(frame, dtype=jnp.int32)[None, None, :]
    sampler = jnp.arange(n_ctx, dtype=jnp.int32)[:, None, None]
    shift = offsets[:, None, None] - (sampler - 1) * T_DEV
    select = ((row + shift == col) & (row < every_count[:, None, None])).astype(jnp.bfloat16)
    placed = jnp.einsum("icr,irj->icj", rows, select, preferred_element_type=jnp.bfloat16)
    full = sum(
        jnp.pad(placed[i], ((0, 0), (i * T_DEV, (n_ctx - 1 - i) * T_DEV))) for i in range(n_ctx)
    )
    first = device * own
    taps = lax.dynamic_slice_in_dim(short_taps, first, own, 2)
    gate = full[:own, T_DEV - 2 : T_DEV + length].astype(jnp.float32)
    shorted_gate = taps[0, 0, :, None] * gate[:, 2:]
    shorted_gate = shorted_gate + taps[0, 1, :, None] * gate[:, 1:-1]
    shorted_gate = shorted_gate + taps[0, 2, :, None] * gate[:, :-2]
    from_senders = full[own:, T_DEV : T_DEV + length]

    values = edge_in[:, :, :8]
    count_col = every_count[:, None]
    at_row = jnp.concatenate(
        [jnp.zeros_like(count_col), jnp.ones_like(count_col), count_col - 2, count_col - 1], axis=1
    )
    valid = jnp.concatenate([at_row[:, :2] < count_col, at_row[:, 2:] >= 2], axis=1)
    spot = offsets[:, None] + at_row
    slot = jnp.arange(length + 2, dtype=jnp.int32)[None, None, :]
    marks = ((slot - 2 == spot[:, :, None]) & valid[:, :, None]).astype(jnp.bfloat16)
    near_in = []
    for part in range(2):
        pick = jnp.concatenate(
            [values[:, :, 2 * part : 2 * part + 2], values[:, :, 4 + 2 * part : 6 + 2 * part]], axis=2
        )
        around = jnp.einsum(
            "ics,isj->cj", pick, marks, preferred_element_type=jnp.float32
        )
        s = taps[1 + part, 0, :, None] * around[:, 2:]
        s = s + taps[1 + part, 1, :, None] * around[:, 1:-1]
        s = s + taps[1 + part, 2, :, None] * around[:, :-2]
        near_in.append(s)
    at_start = jnp.sum(marks[:, :2, 2:].astype(jnp.float32), axis=(0, 1)) > 0
    mixed_input = jnp.where(
        at_start[None, :], (near_in[0] * near_in[1]).astype(jnp.bfloat16), from_senders
    )

    x_spec = transform(mixed_input.reshape(own, n_blocks, T_DEV), forward, "cnt,tf->cnf")
    own_taps = lax.dynamic_slice_in_dim(filter_taps, first, own, 0)
    tap_blocks = jnp.concatenate(
        [jnp.zeros((own, T_DEV), own_taps.dtype), own_taps], axis=1
    ).reshape(own, n_blocks + 1, T_DEV)
    h_spec = transform(tap_blocks, forward, "cnt,tf->cnf")
    column = jnp.arange(PERIOD, dtype=jnp.int32) % T_DEV
    signs = jnp.where(column % 2 == 0, 1.0, -1.0).astype(jnp.float32)
    g_spec = h_spec[:, 1:] + signs * h_spec[:, :-1]
    xr, xi = x_spec[..., :T_DEV], x_spec[..., T_DEV:]
    gr, gi = g_spec[..., :T_DEV], g_spec[..., T_DEV:]
    sums = [jnp.zeros((own, n_blocks, T_DEV), jnp.float32) for _ in range(4)]
    for k in range(n_blocks):
        pad = ((0, 0), (k, 0), (0, 0))
        terms = (
            xr[:, : n_blocks - k] * gr[:, k : k + 1],
            xi[:, : n_blocks - k] * gi[:, k : k + 1],
            xr[:, : n_blocks - k] * gi[:, k : k + 1],
            xi[:, : n_blocks - k] * gr[:, k : k + 1],
        )
        sums = [s + jnp.pad(t, pad) for s, t in zip(sums, terms)]
    rr, ii, ri, ir = sums
    at_zero = jnp.arange(T_DEV, dtype=jnp.int32)[None, None, :] == 0
    spectrum = jnp.concatenate(
        [jnp.where(at_zero, rr, rr - ii), jnp.where(at_zero, ii, ri + ir)], axis=2
    )
    conv_core = jnp.einsum("cnf,ft->cnt", spectrum, inverse, precision=lax.Precision.HIGHEST)
    gains = lax.dynamic_slice_in_dim(skip_gain, first, own, 0)
    conv = conv_core.reshape(own, length) + gains[:, None] * mixed_input.astype(jnp.float32)
    gated = (shorted_gate * conv).astype(jnp.bfloat16)
    back = lax.all_to_all(gated.reshape(own, n_ctx, T_DEV), "ctx", 1, 0, tiled=False)
    gated_block = back.reshape(channels, T_DEV)
    mixed = jnp.dot(
        out_weight,
        lax.all_gather(gated_block, "ch", axis=0, tiled=True),
        preferred_element_type=jnp.float32,
    )
    return mixed.astype(jnp.bfloat16)


def on_device(arrivals, counts, short_taps, filter_taps, skip_gain, out_weight):
    n_ctx = lax.axis_size("ctx")
    blocks = filter_taps.shape[1] // T_DEV
    if arrivals.shape[1] % n_ctx == 0 and blocks == n_ctx:
        return by_transpose(arrivals, counts, short_taps, filter_taps, skip_gain, out_weight)
    return by_gather(arrivals, counts, short_taps, filter_taps, skip_gain, out_weight)


def solution(mesh):
    return jax.shard_map(
        on_device,
        mesh=mesh,
        in_specs=(
            P(None, "ch", "ctx"),
            P("ctx"),
            P(None, None, "ch"),
            P("ch", None),
            P("ch"),
            P("ch", None),
        ),
        out_specs=P("ch", "ctx"),
        check_vma=False,
    )
```

```python
import functools
import math

import jax
import jax.numpy as jnp
import ml_dtypes
import numpy as np
from jax import lax
from jax.experimental import pallas as pl
from jax.experimental.pallas import tpu as pltpu
from jax.sharding import PartitionSpec as P

T_DEV = 256
HALF = T_DEV // 2
PERIOD = 2 * T_DEV
GROUP = 8
EDGE = 128


def split_bf16(table):
    hi = table.astype(ml_dtypes.bfloat16)
    lo = (table - hi.astype(np.float64)).astype(ml_dtypes.bfloat16)
    return jnp.asarray(hi), jnp.asarray(lo)


def dft_tables():
    t = np.arange(T_DEV)[:, None]
    f = np.arange(T_DEV)[None, :]
    angle = 2.0 * np.pi * ((t * f) % PERIOD) / PERIOD
    forward = np.concatenate([np.cos(angle), -np.sin(angle)], axis=1)
    forward[:, T_DEV] = np.where(np.arange(T_DEV) % 2 == 0, 1.0, -1.0)
    fr = np.arange(T_DEV)[:, None]
    n = np.arange(T_DEV)[None, :]
    angle = 2.0 * np.pi * ((fr * n) % PERIOD) / PERIOD
    inv_re = 2.0 * np.cos(angle) / PERIOD
    inv_re[0, :] = 1.0 / PERIOD
    inv_im = -2.0 * np.sin(angle) / PERIOD
    inv_im[0, :] = np.where(np.arange(T_DEV) % 2 == 0, 1.0, -1.0) / PERIOD
    inverse = np.concatenate([inv_re, inv_im], axis=0).astype(np.float32)
    return split_bf16(forward), jnp.asarray(inverse)


def transform(blocks, forward, spec="kct,tf->kcf"):
    hi, lo = forward
    return jnp.einsum(spec, blocks, hi, preferred_element_type=jnp.float32) + jnp.einsum(
        spec, blocks, lo, preferred_element_type=jnp.float32
    )


def kernel_spectra(tap_blocks, forward):
    spectra = transform(tap_blocks, forward)
    column = jnp.arange(PERIOD, dtype=jnp.int32) % T_DEV
    signs = jnp.where(column % 2 == 0, 1.0, -1.0).astype(jnp.float32)
    return spectra[1:] + signs * spectra[:-1]


def products(x_spec, g_spec):
    xr, xi = x_spec[..., :T_DEV], x_spec[..., T_DEV:]
    gr, gi = g_spec[..., :T_DEV], g_spec[..., T_DEV:]
    return (
        jnp.sum(xr * gr, axis=0),
        jnp.sum(xi * gi, axis=0),
        jnp.sum(xr * gi, axis=0),
        jnp.sum(xi * gr, axis=0),
    )


def by_gather(arrivals, counts, short_taps, filter_taps, skip_gain, out_weight):
    n_ctx = lax.axis_size("ctx")
    device = lax.axis_index("ctx")
    channels = arrivals.shape[1]
    capacity = arrivals.shape[2]
    n_blocks = filter_taps.shape[1] // T_DEV
    forward, inverse = dft_tables()

    every_count = lax.all_gather(counts, "ctx", axis=0, tiled=True)
    earlier = jnp.arange(n_ctx, dtype=jnp.int32) < device
    offset = jnp.sum(jnp.where(earlier, every_count, 0))
    count = counts[0]

    frame = 2 * T_DEV
    row = jnp.arange(capacity, dtype=jnp.int32)[:, None]
    col = jnp.arange(frame, dtype=jnp.int32)[None, :]
    shift = offset - device * T_DEV + HALF
    select = ((row + shift == col) & (row < count)).astype(jnp.bfloat16)
    placed = jnp.einsum(
        "pcr,rj->pcj", arrivals, select, preferred_element_type=jnp.float32
    ).astype(jnp.bfloat16)
    to_prev = placed[:, :, :HALF]
    to_next = placed[:, :, frame - HALF - 2 :]
    from_next = lax.ppermute(to_prev, "ctx", [(i + 1, i) for i in range(n_ctx - 1)])
    from_prev = lax.ppermute(to_next, "ctx", [(i, i + 1) for i in range(n_ctx - 1)])
    window = placed[:, :, HALF - 2 : HALF + T_DEV]
    window = window + jnp.pad(from_prev, ((0, 0), (0, 0), (0, T_DEV - HALF)))
    window = window + jnp.pad(from_next, ((0, 0), (0, 0), (T_DEV + 2 - HALF, 0)))
    wide = window.astype(jnp.float32)
    shorted = short_taps[:, 0, :, None] * wide[:, :, 2:]
    shorted = shorted + short_taps[:, 1, :, None] * wide[:, :, 1:-1]
    shorted = shorted + short_taps[:, 2, :, None] * wide[:, :, :-2]
    mixed_input = (shorted[1] * shorted[2]).astype(jnp.bfloat16)

    tap_blocks = jnp.stack(
        [jnp.zeros((channels, T_DEV), filter_taps.dtype)]
        + [filter_taps[:, k * T_DEV : (k + 1) * T_DEV] for k in range(n_blocks)]
    )
    every_input = lax.all_gather(mixed_input, "ctx", axis=0)
    backwards = jnp.concatenate(
        [jnp.flip(every_input, 0), jnp.zeros_like(every_input)], axis=0
    )
    start = n_ctx - 1 - device
    if n_blocks <= GROUP:
        x_blocks = lax.dynamic_slice_in_dim(backwards, start, n_blocks, 0)
        sums = products(transform(x_blocks, forward), kernel_spectra(tap_blocks, forward))
    else:
        width = max(w for w in range(1, GROUP + 1) if n_blocks % w == 0)

        def group(g, acc):
            k0 = g * width
            x_blocks = lax.dynamic_slice_in_dim(backwards, start + k0, width, 0)
            taps = lax.dynamic_slice_in_dim(tap_blocks, k0, width + 1, 0)
            part = products(transform(x_blocks, forward), kernel_spectra(taps, forward))
            return tuple(a + b for a, b in zip(acc, part))

        zero = jnp.zeros((channels, T_DEV), jnp.float32)
        sums = lax.fori_loop(0, n_blocks // width, group, (zero, zero, zero, zero))
    rr, ii, ri, ir = sums
    first = jnp.arange(T_DEV, dtype=jnp.int32)[None, :] == 0
    spec_re = jnp.where(first, rr, rr - ii)
    spec_im = jnp.where(first, ii, ri + ir)
    spectrum = jnp.concatenate([spec_re, spec_im], axis=1)
    conv_core = jnp.dot(spectrum, inverse, precision=lax.Precision.HIGHEST)
    conv = conv_core + skip_gain[:, None] * mixed_input.astype(jnp.float32)
    gated = (shorted[0] * conv).astype(jnp.bfloat16)
    mixed = jnp.dot(
        out_weight,
        lax.all_gather(gated, "ch", axis=0, tiled=True),
        preferred_element_type=jnp.float32,
    )
    return mixed.astype(jnp.bfloat16)


def sender_kernel(count_ref, arrivals_ref, taps_ref, out_ref, *, n_ctx, own):
    count = count_ref[0]
    capacity = arrivals_ref.shape[2]
    lane = lax.broadcasted_iota(jnp.int32, arrivals_ref.shape[1:], 1)
    row = lax.broadcasted_iota(jnp.int32, (capacity, EDGE), 0)
    column = lax.broadcasted_iota(jnp.int32, (capacity, EDGE), 1)
    square = lax.broadcasted_iota(jnp.int32, (lane.shape[0], lane.shape[0]), 0)
    diagonal = square == lax.broadcasted_iota(jnp.int32, square.shape, 1)

    def tap(part, k):
        spread = jnp.where(diagonal, taps_ref[part, k : k + 1, :], 0.0)
        return jnp.sum(spread, axis=1, keepdims=True)

    near = []
    edge = jnp.where(column[:1] == 8, (count // 16).astype(jnp.float32), 0.0)
    edge = jnp.where(column[:1] == 9, (count % 16).astype(jnp.float32), edge)
    for part in range(2):
        raw = arrivals_ref[1 + part]
        x = raw.astype(jnp.float32)
        back1 = jnp.where(lane >= 1, pltpu.roll(x, 1, 1), 0.0)
        back2 = jnp.where(lane >= 2, pltpu.roll(x, 2, 1), 0.0)
        s = tap(1 + part, 0) * x
        s = s + tap(1 + part, 1) * back1
        s = s + tap(1 + part, 2) * back2
        near.append(s)
        wanted = jnp.where(column >= 4, count - 2 + column - 4 - 2 * part, column - 2 * part)
        inside = (column % 4 >= 2 * part) & (column % 4 < 2 * part + 2) & (column < 8)
        pick = ((row == wanted) & inside).astype(jnp.bfloat16)
        edge = edge + jnp.dot(raw, pick, preferred_element_type=jnp.float32)
    mixed = (near[0] * near[1]).astype(jnp.bfloat16)
    edge = edge.astype(jnp.bfloat16)
    for j in range(n_ctx):
        rows = slice(j * own, (j + 1) * own)
        out_ref[j, :own, :capacity] = arrivals_ref[0, rows, :]
        out_ref[j, :own, capacity:] = jnp.zeros((own, EDGE), jnp.bfloat16)
        out_ref[j, own:, :capacity] = mixed[rows]
        out_ref[j, own:, capacity:] = edge[rows]


def by_transpose(arrivals, counts, short_taps, filter_taps, skip_gain, out_weight):
    n_ctx = lax.axis_size("ctx")
    device = lax.axis_index("ctx")
    channels = arrivals.shape[1]
    capacity = arrivals.shape[2]
    length = filter_taps.shape[1]
    n_blocks = length // T_DEV
    own = channels // n_ctx
    forward, inverse = dft_tables()

    payload = pl.pallas_call(
        functools.partial(sender_kernel, n_ctx=n_ctx, own=own),
        in_specs=[
            pl.BlockSpec(memory_space=pltpu.SMEM),
            pl.BlockSpec(memory_space=pltpu.VMEM),
            pl.BlockSpec(memory_space=pltpu.VMEM),
        ],
        out_specs=pl.BlockSpec(memory_space=pltpu.VMEM),
        out_shape=jax.ShapeDtypeStruct((n_ctx, 2 * own, capacity + EDGE), jnp.bfloat16),
    )(counts, arrivals, short_taps)
    got = lax.all_to_all(payload, "ctx", 0, 0, tiled=False)
    rows = got[:, :, :capacity]
    edge_in = got[:, own:, capacity:]
    every_count = edge_in[:, 0, 8].astype(jnp.int32) * 16 + edge_in[:, 0, 9].astype(jnp.int32)
    offsets = jnp.cumsum(every_count) - every_count

    frame = 3 * T_DEV
    row = jnp.arange(capacity, dtype=jnp.int32)[None, :, None]
    col = jnp.arange(frame, dtype=jnp.int32)[None, None, :]
    sampler = jnp.arange(n_ctx, dtype=jnp.int32)[:, None, None]
    shift = offsets[:, None, None] - (sampler - 1) * T_DEV
    select = ((row + shift == col) & (row < every_count[:, None, None])).astype(jnp.bfloat16)
    placed = jnp.einsum("icr,irj->icj", rows, select, preferred_element_type=jnp.bfloat16)
    full = sum(
        jnp.pad(placed[i], ((0, 0), (i * T_DEV, (n_ctx - 1 - i) * T_DEV))) for i in range(n_ctx)
    )
    first = device * own
    taps = lax.dynamic_slice_in_dim(short_taps, first, own, 2)
    gate = full[:own, T_DEV - 2 : T_DEV + length].astype(jnp.float32)
    shorted_gate = taps[0, 0, :, None] * gate[:, 2:]
    shorted_gate = shorted_gate + taps[0, 1, :, None] * gate[:, 1:-1]
    shorted_gate = shorted_gate + taps[0, 2, :, None] * gate[:, :-2]
    from_senders = full[own:, T_DEV : T_DEV + length]

    values = edge_in[:, :, :8]
    count_col = every_count[:, None]
    at_row = jnp.concatenate(
        [jnp.zeros_like(count_col), jnp.ones_like(count_col), count_col - 2, count_col - 1], axis=1
    )
    valid = jnp.concatenate([at_row[:, :2] < count_col, at_row[:, 2:] >= 2], axis=1)
    spot = offsets[:, None] + at_row
    slot = jnp.arange(length + 2, dtype=jnp.int32)[None, None, :]
    marks = ((slot - 2 == spot[:, :, None]) & valid[:, :, None]).astype(jnp.bfloat16)
    near_in = []
    for part in range(2):
        pick = jnp.concatenate(
            [values[:, :, 2 * part : 2 * part + 2], values[:, :, 4 + 2 * part : 6 + 2 * part]], axis=2
        )
        around = jnp.einsum(
            "ics,isj->cj", pick, marks, preferred_element_type=jnp.float32
        )
        s = taps[1 + part, 0, :, None] * around[:, 2:]
        s = s + taps[1 + part, 1, :, None] * around[:, 1:-1]
        s = s + taps[1 + part, 2, :, None] * around[:, :-2]
        near_in.append(s)
    at_start = jnp.sum(marks[:, :2, 2:].astype(jnp.float32), axis=(0, 1)) > 0
    mixed_input = jnp.where(
        at_start[None, :], (near_in[0] * near_in[1]).astype(jnp.bfloat16), from_senders
    )

    x_spec = transform(mixed_input.reshape(own, n_blocks, T_DEV), forward, "cnt,tf->cnf")
    own_taps = lax.dynamic_slice_in_dim(filter_taps, first, own, 0)
    tap_blocks = jnp.concatenate(
        [jnp.zeros((own, T_DEV), own_taps.dtype), own_taps], axis=1
    ).reshape(own, n_blocks + 1, T_DEV)
    h_spec = transform(tap_blocks, forward, "cnt,tf->cnf")
    column = jnp.arange(PERIOD, dtype=jnp.int32) % T_DEV
    signs = jnp.where(column % 2 == 0, 1.0, -1.0).astype(jnp.float32)
    g_spec = h_spec[:, 1:] + signs * h_spec[:, :-1]
    xr, xi = x_spec[..., :T_DEV], x_spec[..., T_DEV:]
    gr, gi = g_spec[..., :T_DEV], g_spec[..., T_DEV:]
    sums = [jnp.zeros((own, n_blocks, T_DEV), jnp.float32) for _ in range(4)]
    for k in range(n_blocks):
        pad = ((0, 0), (k, 0), (0, 0))
        terms = (
            xr[:, : n_blocks - k] * gr[:, k : k + 1],
            xi[:, : n_blocks - k] * gi[:, k : k + 1],
            xr[:, : n_blocks - k] * gi[:, k : k + 1],
            xi[:, : n_blocks - k] * gr[:, k : k + 1],
        )
        sums = [s + jnp.pad(t, pad) for s, t in zip(sums, terms)]
    rr, ii, ri, ir = sums
    at_zero = jnp.arange(T_DEV, dtype=jnp.int32)[None, None, :] == 0
    spectrum = jnp.concatenate(
        [jnp.where(at_zero, rr, rr - ii), jnp.where(at_zero, ii, ri + ir)], axis=2
    )
    conv_core = jnp.einsum("cnf,ft->cnt", spectrum, inverse, precision=lax.Precision.HIGHEST)
    gains = lax.dynamic_slice_in_dim(skip_gain, first, own, 0)
    conv = conv_core.reshape(own, length) + gains[:, None] * mixed_input.astype(jnp.float32)
    gated = (shorted_gate * conv).astype(jnp.bfloat16)
    back = lax.all_to_all(gated.reshape(own, n_ctx, T_DEV), "ctx", 1, 0, tiled=False)
    gated_block = back.reshape(channels, T_DEV)
    mixed = jnp.dot(
        out_weight,
        lax.all_gather(gated_block, "ch", axis=0, tiled=True),
        preferred_element_type=jnp.float32,
    )
    return mixed.astype(jnp.bfloat16)


def on_device(arrivals, counts, short_taps, filter_taps, skip_gain, out_weight):
    n_ctx = lax.axis_size("ctx")
    blocks = filter_taps.shape[1] // T_DEV
    if arrivals.shape[1] % n_ctx == 0 and blocks == n_ctx:
        return by_transpose(arrivals, counts, short_taps, filter_taps, skip_gain, out_weight)
    return by_gather(arrivals, counts, short_taps, filter_taps, skip_gain, out_weight)


def solution(mesh):
    return jax.shard_map(
        on_device,
        mesh=mesh,
        in_specs=(
            P(None, "ch", "ctx"),
            P("ctx"),
            P(None, None, "ch"),
            P("ch", None),
            P("ch"),
            P("ch", None),
        ),
        out_specs=P("ch", "ctx"),
        check_vma=False,
    )
```

```python
import functools
import math

import jax
import jax.numpy as jnp
import ml_dtypes
import numpy as np
from jax import lax
from jax.experimental import pallas as pl
from jax.experimental.pallas import tpu as pltpu
from jax.sharding import PartitionSpec as P

T_DEV = 256
HALF = T_DEV // 2
PERIOD = 2 * T_DEV
GROUP = 8
EDGE = 128


def split_bf16(table):
    hi = table.astype(ml_dtypes.bfloat16)
    lo = (table - hi.astype(np.float64)).astype(ml_dtypes.bfloat16)
    return jnp.asarray(hi), jnp.asarray(lo)


def dft_tables():
    t = np.arange(T_DEV)[:, None]
    f = np.arange(T_DEV)[None, :]
    angle = 2.0 * np.pi * ((t * f) % PERIOD) / PERIOD
    forward = np.concatenate([np.cos(angle), -np.sin(angle)], axis=1)
    forward[:, T_DEV] = np.where(np.arange(T_DEV) % 2 == 0, 1.0, -1.0)
    fr = np.arange(T_DEV)[:, None]
    n = np.arange(T_DEV)[None, :]
    angle = 2.0 * np.pi * ((fr * n) % PERIOD) / PERIOD
    inv_re = 2.0 * np.cos(angle) / PERIOD
    inv_re[0, :] = 1.0 / PERIOD
    inv_im = -2.0 * np.sin(angle) / PERIOD
    inv_im[0, :] = np.where(np.arange(T_DEV) % 2 == 0, 1.0, -1.0) / PERIOD
    inverse = np.concatenate([inv_re, inv_im], axis=0).astype(np.float32)
    return split_bf16(forward), jnp.asarray(inverse)


def transform(blocks, forward, spec="kct,tf->kcf"):
    hi, lo = forward
    return jnp.einsum(spec, blocks, hi, preferred_element_type=jnp.float32) + jnp.einsum(
        spec, blocks, lo, preferred_element_type=jnp.float32
    )


def kernel_spectra(tap_blocks, forward):
    spectra = transform(tap_blocks, forward)
    column = jnp.arange(PERIOD, dtype=jnp.int32) % T_DEV
    signs = jnp.where(column % 2 == 0, 1.0, -1.0).astype(jnp.float32)
    return spectra[1:] + signs * spectra[:-1]


def products(x_spec, g_spec):
    xr, xi = x_spec[..., :T_DEV], x_spec[..., T_DEV:]
    gr, gi = g_spec[..., :T_DEV], g_spec[..., T_DEV:]
    return (
        jnp.sum(xr * gr, axis=0),
        jnp.sum(xi * gi, axis=0),
        jnp.sum(xr * gi, axis=0),
        jnp.sum(xi * gr, axis=0),
    )


def by_gather(arrivals, counts, short_taps, filter_taps, skip_gain, out_weight):
    n_ctx = lax.axis_size("ctx")
    device = lax.axis_index("ctx")
    channels = arrivals.shape[1]
    capacity = arrivals.shape[2]
    n_blocks = filter_taps.shape[1] // T_DEV
    forward, inverse = dft_tables()

    every_count = lax.all_gather(counts, "ctx", axis=0, tiled=True)
    earlier = jnp.arange(n_ctx, dtype=jnp.int32) < device
    offset = jnp.sum(jnp.where(earlier, every_count, 0))
    count = counts[0]

    frame = 2 * T_DEV
    row = jnp.arange(capacity, dtype=jnp.int32)[:, None]
    col = jnp.arange(frame, dtype=jnp.int32)[None, :]
    shift = offset - device * T_DEV + HALF
    select = ((row + shift == col) & (row < count)).astype(jnp.bfloat16)
    placed = jnp.einsum(
        "pcr,rj->pcj", arrivals, select, preferred_element_type=jnp.float32
    ).astype(jnp.bfloat16)
    to_prev = placed[:, :, :HALF]
    to_next = placed[:, :, frame - HALF - 2 :]
    from_next = lax.ppermute(to_prev, "ctx", [(i + 1, i) for i in range(n_ctx - 1)])
    from_prev = lax.ppermute(to_next, "ctx", [(i, i + 1) for i in range(n_ctx - 1)])
    window = placed[:, :, HALF - 2 : HALF + T_DEV]
    window = window + jnp.pad(from_prev, ((0, 0), (0, 0), (0, T_DEV - HALF)))
    window = window + jnp.pad(from_next, ((0, 0), (0, 0), (T_DEV + 2 - HALF, 0)))
    wide = window.astype(jnp.float32)
    shorted = short_taps[:, 0, :, None] * wide[:, :, 2:]
    shorted = shorted + short_taps[:, 1, :, None] * wide[:, :, 1:-1]
    shorted = shorted + short_taps[:, 2, :, None] * wide[:, :, :-2]
    mixed_input = (shorted[1] * shorted[2]).astype(jnp.bfloat16)

    tap_blocks = jnp.stack(
        [jnp.zeros((channels, T_DEV), filter_taps.dtype)]
        + [filter_taps[:, k * T_DEV : (k + 1) * T_DEV] for k in range(n_blocks)]
    )
    every_input = lax.all_gather(mixed_input, "ctx", axis=0)
    backwards = jnp.concatenate(
        [jnp.flip(every_input, 0), jnp.zeros_like(every_input)], axis=0
    )
    start = n_ctx - 1 - device
    if n_blocks <= GROUP:
        x_blocks = lax.dynamic_slice_in_dim(backwards, start, n_blocks, 0)
        sums = products(transform(x_blocks, forward), kernel_spectra(tap_blocks, forward))
    else:
        width = max(w for w in range(1, GROUP + 1) if n_blocks % w == 0)

        def group(g, acc):
            k0 = g * width
            x_blocks = lax.dynamic_slice_in_dim(backwards, start + k0, width, 0)
            taps = lax.dynamic_slice_in_dim(tap_blocks, k0, width + 1, 0)
            part = products(transform(x_blocks, forward), kernel_spectra(taps, forward))
            return tuple(a + b for a, b in zip(acc, part))

        zero = jnp.zeros((channels, T_DEV), jnp.float32)
        sums = lax.fori_loop(0, n_blocks // width, group, (zero, zero, zero, zero))
    rr, ii, ri, ir = sums
    first = jnp.arange(T_DEV, dtype=jnp.int32)[None, :] == 0
    spec_re = jnp.where(first, rr, rr - ii)
    spec_im = jnp.where(first, ii, ri + ir)
    spectrum = jnp.concatenate([spec_re, spec_im], axis=1)
    conv_core = jnp.dot(spectrum, inverse, precision=lax.Precision.HIGHEST)
    conv = conv_core + skip_gain[:, None] * mixed_input.astype(jnp.float32)
    gated = (shorted[0] * conv).astype(jnp.bfloat16)
    mixed = jnp.dot(
        out_weight,
        lax.all_gather(gated, "ch", axis=0, tiled=True),
        preferred_element_type=jnp.float32,
    )
    return mixed.astype(jnp.bfloat16)


def sender_kernel(count_ref, arrivals_ref, taps_ref, out_ref, *, n_ctx, own):
    count = count_ref[0]
    capacity = arrivals_ref.shape[2]
    lane = lax.broadcasted_iota(jnp.int32, arrivals_ref.shape[1:], 1)
    row = lax.broadcasted_iota(jnp.int32, (capacity, EDGE), 0)
    column = lax.broadcasted_iota(jnp.int32, (capacity, EDGE), 1)
    square = lax.broadcasted_iota(jnp.int32, (lane.shape[0], lane.shape[0]), 0)
    diagonal = square == lax.broadcasted_iota(jnp.int32, square.shape, 1)

    def tap(part, k):
        spread = jnp.where(diagonal, taps_ref[part, k : k + 1, :], 0.0)
        return jnp.sum(spread, axis=1, keepdims=True)

    near = []
    edge = jnp.where(column[:1] == 8, (count // 16).astype(jnp.float32), 0.0)
    edge = jnp.where(column[:1] == 9, (count % 16).astype(jnp.float32), edge)
    for part in range(2):
        raw = arrivals_ref[1 + part]
        x = raw.astype(jnp.float32)
        back1 = jnp.where(lane >= 1, pltpu.roll(x, 1, 1), 0.0)
        back2 = jnp.where(lane >= 2, pltpu.roll(x, 2, 1), 0.0)
        s = tap(1 + part, 0) * x
        s = s + tap(1 + part, 1) * back1
        s = s + tap(1 + part, 2) * back2
        near.append(s)
        wanted = jnp.where(column >= 4, count - 2 + column - 4 - 2 * part, column - 2 * part)
        inside = (column % 4 >= 2 * part) & (column % 4 < 2 * part + 2) & (column < 8)
        pick = ((row == wanted) & inside).astype(jnp.bfloat16)
        edge = edge + jnp.dot(raw, pick, preferred_element_type=jnp.float32)
    mixed = (near[0] * near[1]).astype(jnp.bfloat16)
    edge = edge.astype(jnp.bfloat16)
    flat_lane = lax.broadcasted_iota(jnp.int32, (EDGE, capacity), 1)
    spread = (
        (flat_lane < 8 * own) & (flat_lane % 8 == lax.broadcasted_iota(jnp.int32, (EDGE, capacity), 0))
    ).astype(jnp.bfloat16)
    channel = lax.broadcasted_iota(jnp.int32, (own, capacity), 0)
    lane_out = lax.broadcasted_iota(jnp.int32, (own, capacity), 1)
    code = jnp.where(lane_out[:1] == 8 * own, (count // 16).astype(jnp.float32), 0.0)
    code = jnp.where(lane_out[:1] == 8 * own + 1, (count % 16).astype(jnp.float32), code)
    for j in range(n_ctx):
        rows = slice(j * own, (j + 1) * own)
        out_ref[j, :own, :] = arrivals_ref[0, rows, :]
        out_ref[j, own : 2 * own, :] = mixed[rows]
        tiled = jnp.dot(edge[rows], spread, preferred_element_type=jnp.float32)
        flat = jnp.sum(jnp.where(lane_out // 8 == channel, tiled, 0.0), axis=0, keepdims=True)
        out_ref[j, 2 * own : 2 * own + 1, :] = (flat + code).astype(jnp.bfloat16)


def by_transpose(arrivals, counts, short_taps, filter_taps, skip_gain, out_weight):
    n_ctx = lax.axis_size("ctx")
    device = lax.axis_index("ctx")
    channels = arrivals.shape[1]
    capacity = arrivals.shape[2]
    length = filter_taps.shape[1]
    n_blocks = length // T_DEV
    own = channels // n_ctx
    forward, inverse = dft_tables()

    payload = pl.pallas_call(
        functools.partial(sender_kernel, n_ctx=n_ctx, own=own),
        in_specs=[
            pl.BlockSpec(memory_space=pltpu.SMEM),
            pl.BlockSpec(memory_space=pltpu.VMEM),
            pl.BlockSpec(memory_space=pltpu.VMEM),
        ],
        out_specs=pl.BlockSpec(memory_space=pltpu.VMEM),
        out_shape=jax.ShapeDtypeStruct((n_ctx, 2 * own + 1, capacity), jnp.bfloat16),
    )(counts, arrivals, short_taps)
    got = lax.all_to_all(payload, "ctx", 0, 0, tiled=False)
    rows = got[:, : 2 * own]
    edge_in = got[:, 2 * own]
    every_count = (
        edge_in[:, own * 8].astype(jnp.int32) * 16 + edge_in[:, own * 8 + 1].astype(jnp.int32)
    )
    offsets = jnp.cumsum(every_count) - every_count

    frame = 3 * T_DEV
    row = jnp.arange(capacity, dtype=jnp.int32)[None, :, None]
    col = jnp.arange(frame, dtype=jnp.int32)[None, None, :]
    sampler = jnp.arange(n_ctx, dtype=jnp.int32)[:, None, None]
    shift = offsets[:, None, None] - (sampler - 1) * T_DEV
    select = ((row + shift == col) & (row < every_count[:, None, None])).astype(jnp.bfloat16)
    placed = jnp.einsum("icr,irj->icj", rows, select, preferred_element_type=jnp.bfloat16)
    full = sum(
        jnp.pad(placed[i], ((0, 0), (i * T_DEV, (n_ctx - 1 - i) * T_DEV))) for i in range(n_ctx)
    )
    first = device * own
    taps = lax.dynamic_slice_in_dim(short_taps, first, own, 2)
    gate = full[:own, T_DEV - 2 : T_DEV + length].astype(jnp.float32)
    shorted_gate = taps[0, 0, :, None] * gate[:, 2:]
    shorted_gate = shorted_gate + taps[0, 1, :, None] * gate[:, 1:-1]
    shorted_gate = shorted_gate + taps[0, 2, :, None] * gate[:, :-2]
    from_senders = full[own:, T_DEV : T_DEV + length]

    values = edge_in[:, : own * 8].reshape(n_ctx, own, 8)
    count_col = every_count[:, None]
    at_row = jnp.concatenate(
        [jnp.zeros_like(count_col), jnp.ones_like(count_col), count_col - 2, count_col - 1], axis=1
    )
    valid = jnp.concatenate([at_row[:, :2] < count_col, at_row[:, 2:] >= 2], axis=1)
    spot = offsets[:, None] + at_row
    slot = jnp.arange(length + 2, dtype=jnp.int32)[None, None, :]
    marks = ((slot - 2 == spot[:, :, None]) & valid[:, :, None]).astype(jnp.bfloat16)
    near_in = []
    for part in range(2):
        pick = jnp.concatenate(
            [values[:, :, 2 * part : 2 * part + 2], values[:, :, 4 + 2 * part : 6 + 2 * part]], axis=2
        )
        around = jnp.einsum(
            "ics,isj->cj", pick, marks, preferred_element_type=jnp.float32
        )
        s = taps[1 + part, 0, :, None] * around[:, 2:]
        s = s + taps[1 + part, 1, :, None] * around[:, 1:-1]
        s = s + taps[1 + part, 2, :, None] * around[:, :-2]
        near_in.append(s)
    at_start = jnp.sum(marks[:, :2, 2:].astype(jnp.float32), axis=(0, 1)) > 0
    mixed_input = jnp.where(
        at_start[None, :], (near_in[0] * near_in[1]).astype(jnp.bfloat16), from_senders
    )

    x_spec = transform(mixed_input.reshape(own, n_blocks, T_DEV), forward, "cnt,tf->cnf")
    own_taps = lax.dynamic_slice_in_dim(filter_taps, first, own, 0)
    tap_blocks = jnp.concatenate(
        [jnp.zeros((own, T_DEV), own_taps.dtype), own_taps], axis=1
    ).reshape(own, n_blocks + 1, T_DEV)
    h_spec = transform(tap_blocks, forward, "cnt,tf->cnf")
    column = jnp.arange(PERIOD, dtype=jnp.int32) % T_DEV
    signs = jnp.where(column % 2 == 0, 1.0, -1.0).astype(jnp.float32)
    g_spec = h_spec[:, 1:] + signs * h_spec[:, :-1]
    xr, xi = x_spec[..., :T_DEV], x_spec[..., T_DEV:]
    gr, gi = g_spec[..., :T_DEV], g_spec[..., T_DEV:]
    sums = [jnp.zeros((own, n_blocks, T_DEV), jnp.float32) for _ in range(4)]
    for k in range(n_blocks):
        pad = ((0, 0), (k, 0), (0, 0))
        terms = (
            xr[:, : n_blocks - k] * gr[:, k : k + 1],
            xi[:, : n_blocks - k] * gi[:, k : k + 1],
            xr[:, : n_blocks - k] * gi[:, k : k + 1],
            xi[:, : n_blocks - k] * gr[:, k : k + 1],
        )
        sums = [s + jnp.pad(t, pad) for s, t in zip(sums, terms)]
    rr, ii, ri, ir = sums
    at_zero = jnp.arange(T_DEV, dtype=jnp.int32)[None, None, :] == 0
    spectrum = jnp.concatenate(
        [jnp.where(at_zero, rr, rr - ii), jnp.where(at_zero, ii, ri + ir)], axis=2
    )
    conv_core = jnp.einsum("cnf,ft->cnt", spectrum, inverse, precision=lax.Precision.HIGHEST)
    gains = lax.dynamic_slice_in_dim(skip_gain, first, own, 0)
    conv = conv_core.reshape(own, length) + gains[:, None] * mixed_input.astype(jnp.float32)
    gated = (shorted_gate * conv).astype(jnp.bfloat16)
    back = lax.all_to_all(gated.reshape(own, n_ctx, T_DEV), "ctx", 1, 0, tiled=False)
    gated_block = back.reshape(channels, T_DEV)
    mixed = jnp.dot(
        out_weight,
        lax.all_gather(gated_block, "ch", axis=0, tiled=True),
        preferred_element_type=jnp.float32,
    )
    return mixed.astype(jnp.bfloat16)


def on_device(arrivals, counts, short_taps, filter_taps, skip_gain, out_weight):
    n_ctx = lax.axis_size("ctx")
    blocks = filter_taps.shape[1] // T_DEV
    if arrivals.shape[1] % n_ctx == 0 and blocks == n_ctx:
        return by_transpose(arrivals, counts, short_taps, filter_taps, skip_gain, out_weight)
    return by_gather(arrivals, counts, short_taps, filter_taps, skip_gain, out_weight)


def solution(mesh):
    return jax.shard_map(
        on_device,
        mesh=mesh,
        in_specs=(
            P(None, "ch", "ctx"),
            P("ctx"),
            P(None, None, "ch"),
            P("ch", None),
            P("ch"),
            P("ch", None),
        ),
        out_specs=P("ch", "ctx"),
        check_vma=False,
    )
```

```python
import functools
import math

import jax
import jax.numpy as jnp
import ml_dtypes
import numpy as np
from jax import lax
from jax.experimental import pallas as pl
from jax.experimental.pallas import tpu as pltpu
from jax.sharding import PartitionSpec as P

T_DEV = 256
HALF = T_DEV // 2
PERIOD = 2 * T_DEV
GROUP = 8
EDGE = 128


def split_bf16(table):
    hi = table.astype(ml_dtypes.bfloat16)
    lo = (table - hi.astype(np.float64)).astype(ml_dtypes.bfloat16)
    return jnp.asarray(hi), jnp.asarray(lo)


def dft_tables():
    t = np.arange(T_DEV)[:, None]
    f = np.arange(T_DEV)[None, :]
    angle = 2.0 * np.pi * ((t * f) % PERIOD) / PERIOD
    forward = np.concatenate([np.cos(angle), -np.sin(angle)], axis=1)
    forward[:, T_DEV] = np.where(np.arange(T_DEV) % 2 == 0, 1.0, -1.0)
    fr = np.arange(T_DEV)[:, None]
    n = np.arange(T_DEV)[None, :]
    angle = 2.0 * np.pi * ((fr * n) % PERIOD) / PERIOD
    inv_re = 2.0 * np.cos(angle) / PERIOD
    inv_re[0, :] = 1.0 / PERIOD
    inv_im = -2.0 * np.sin(angle) / PERIOD
    inv_im[0, :] = np.where(np.arange(T_DEV) % 2 == 0, 1.0, -1.0) / PERIOD
    inverse = np.concatenate([inv_re, inv_im], axis=0).astype(np.float32)
    return split_bf16(forward), jnp.asarray(inverse)


def transform(blocks, forward, spec="kct,tf->kcf"):
    hi, lo = forward
    return jnp.einsum(spec, blocks, hi, preferred_element_type=jnp.float32) + jnp.einsum(
        spec, blocks, lo, preferred_element_type=jnp.float32
    )


def kernel_spectra(tap_blocks, forward):
    spectra = transform(tap_blocks, forward)
    column = jnp.arange(PERIOD, dtype=jnp.int32) % T_DEV
    signs = jnp.where(column % 2 == 0, 1.0, -1.0).astype(jnp.float32)
    return spectra[1:] + signs * spectra[:-1]


def products(x_spec, g_spec):
    xr, xi = x_spec[..., :T_DEV], x_spec[..., T_DEV:]
    gr, gi = g_spec[..., :T_DEV], g_spec[..., T_DEV:]
    return (
        jnp.sum(xr * gr, axis=0),
        jnp.sum(xi * gi, axis=0),
        jnp.sum(xr * gi, axis=0),
        jnp.sum(xi * gr, axis=0),
    )


def by_gather(arrivals, counts, short_taps, filter_taps, skip_gain, out_weight):
    n_ctx = lax.axis_size("ctx")
    device = lax.axis_index("ctx")
    channels = arrivals.shape[1]
    capacity = arrivals.shape[2]
    n_blocks = filter_taps.shape[1] // T_DEV
    forward, inverse = dft_tables()

    every_count = lax.all_gather(counts, "ctx", axis=0, tiled=True)
    earlier = jnp.arange(n_ctx, dtype=jnp.int32) < device
    offset = jnp.sum(jnp.where(earlier, every_count, 0))
    count = counts[0]

    frame = 2 * T_DEV
    row = jnp.arange(capacity, dtype=jnp.int32)[:, None]
    col = jnp.arange(frame, dtype=jnp.int32)[None, :]
    shift = offset - device * T_DEV + HALF
    select = ((row + shift == col) & (row < count)).astype(jnp.bfloat16)
    placed = jnp.einsum(
        "pcr,rj->pcj", arrivals, select, preferred_element_type=jnp.float32
    ).astype(jnp.bfloat16)
    to_prev = placed[:, :, :HALF]
    to_next = placed[:, :, frame - HALF - 2 :]
    from_next = lax.ppermute(to_prev, "ctx", [(i + 1, i) for i in range(n_ctx - 1)])
    from_prev = lax.ppermute(to_next, "ctx", [(i, i + 1) for i in range(n_ctx - 1)])
    window = placed[:, :, HALF - 2 : HALF + T_DEV]
    window = window + jnp.pad(from_prev, ((0, 0), (0, 0), (0, T_DEV - HALF)))
    window = window + jnp.pad(from_next, ((0, 0), (0, 0), (T_DEV + 2 - HALF, 0)))
    wide = window.astype(jnp.float32)
    shorted = short_taps[:, 0, :, None] * wide[:, :, 2:]
    shorted = shorted + short_taps[:, 1, :, None] * wide[:, :, 1:-1]
    shorted = shorted + short_taps[:, 2, :, None] * wide[:, :, :-2]
    mixed_input = (shorted[1] * shorted[2]).astype(jnp.bfloat16)

    tap_blocks = jnp.stack(
        [jnp.zeros((channels, T_DEV), filter_taps.dtype)]
        + [filter_taps[:, k * T_DEV : (k + 1) * T_DEV] for k in range(n_blocks)]
    )
    every_input = lax.all_gather(mixed_input, "ctx", axis=0)
    backwards = jnp.concatenate(
        [jnp.flip(every_input, 0), jnp.zeros_like(every_input)], axis=0
    )
    start = n_ctx - 1 - device
    if n_blocks <= GROUP:
        x_blocks = lax.dynamic_slice_in_dim(backwards, start, n_blocks, 0)
        sums = products(transform(x_blocks, forward), kernel_spectra(tap_blocks, forward))
    else:
        width = max(w for w in range(1, GROUP + 1) if n_blocks % w == 0)

        def group(g, acc):
            k0 = g * width
            x_blocks = lax.dynamic_slice_in_dim(backwards, start + k0, width, 0)
            taps = lax.dynamic_slice_in_dim(tap_blocks, k0, width + 1, 0)
            part = products(transform(x_blocks, forward), kernel_spectra(taps, forward))
            return tuple(a + b for a, b in zip(acc, part))

        zero = jnp.zeros((channels, T_DEV), jnp.float32)
        sums = lax.fori_loop(0, n_blocks // width, group, (zero, zero, zero, zero))
    rr, ii, ri, ir = sums
    first = jnp.arange(T_DEV, dtype=jnp.int32)[None, :] == 0
    spec_re = jnp.where(first, rr, rr - ii)
    spec_im = jnp.where(first, ii, ri + ir)
    spectrum = jnp.concatenate([spec_re, spec_im], axis=1)
    conv_core = jnp.dot(spectrum, inverse, precision=lax.Precision.HIGHEST)
    conv = conv_core + skip_gain[:, None] * mixed_input.astype(jnp.float32)
    gated = (shorted[0] * conv).astype(jnp.bfloat16)
    mixed = jnp.dot(
        out_weight,
        lax.all_gather(gated, "ch", axis=0, tiled=True),
        preferred_element_type=jnp.float32,
    )
    return mixed.astype(jnp.bfloat16)


def sender_kernel(count_ref, arrivals_ref, taps_ref, out_ref, *, n_ctx, own):
    count = count_ref[0]
    capacity = arrivals_ref.shape[2]
    lane = lax.broadcasted_iota(jnp.int32, arrivals_ref.shape[1:], 1)
    row = lax.broadcasted_iota(jnp.int32, (capacity, EDGE), 0)
    column = lax.broadcasted_iota(jnp.int32, (capacity, EDGE), 1)
    square = lax.broadcasted_iota(jnp.int32, (lane.shape[0], lane.shape[0]), 0)
    diagonal = square == lax.broadcasted_iota(jnp.int32, square.shape, 1)

    def tap(part, k):
        spread = jnp.where(diagonal, taps_ref[part, k : k + 1, :], 0.0)
        return jnp.sum(spread, axis=1, keepdims=True)

    near = []
    edge = jnp.where(column[:1] == 8, (count // 16).astype(jnp.float32), 0.0)
    edge = jnp.where(column[:1] == 9, (count % 16).astype(jnp.float32), edge)
    for part in range(2):
        raw = arrivals_ref[1 + part]
        x = raw.astype(jnp.float32)
        back1 = jnp.where(lane >= 1, pltpu.roll(x, 1, 1), 0.0)
        back2 = jnp.where(lane >= 2, pltpu.roll(x, 2, 1), 0.0)
        s = tap(1 + part, 0) * x
        s = s + tap(1 + part, 1) * back1
        s = s + tap(1 + part, 2) * back2
        near.append(s)
        wanted = jnp.where(column >= 4, count - 2 + column - 4 - 2 * part, column - 2 * part)
        inside = (column % 4 >= 2 * part) & (column % 4 < 2 * part + 2) & (column < 8)
        pick = ((row == wanted) & inside).astype(jnp.bfloat16)
        edge = edge + jnp.dot(raw, pick, preferred_element_type=jnp.float32)
    mixed = (near[0] * near[1]).astype(jnp.bfloat16)
    edge = edge.astype(jnp.bfloat16)
    flat_lane = lax.broadcasted_iota(jnp.int32, (EDGE, capacity), 1)
    spread = (
        (flat_lane < 8 * own) & (flat_lane % 8 == lax.broadcasted_iota(jnp.int32, (EDGE, capacity), 0))
    ).astype(jnp.bfloat16)
    channel = lax.broadcasted_iota(jnp.int32, (own, capacity), 0)
    lane_out = lax.broadcasted_iota(jnp.int32, (own, capacity), 1)
    code = jnp.where(lane_out[:1] == 8 * own, (count // 16).astype(jnp.float32), 0.0)
    code = jnp.where(lane_out[:1] == 8 * own + 1, (count % 16).astype(jnp.float32), code)
    for j in range(n_ctx):
        rows = slice(j * own, (j + 1) * own)
        out_ref[j, :own, :] = arrivals_ref[0, rows, :]
        out_ref[j, own : 2 * own, :] = mixed[rows]
        tiled = jnp.dot(edge[rows], spread, preferred_element_type=jnp.float32)
        flat = jnp.sum(jnp.where(lane_out // 8 == channel, tiled, 0.0), axis=0, keepdims=True)
        out_ref[j, 2 * own : 2 * own + 1, :] = (flat + code).astype(jnp.bfloat16)


def by_transpose(arrivals, counts, short_taps, filter_taps, skip_gain, out_weight):
    n_ctx = lax.axis_size("ctx")
    device = lax.axis_index("ctx")
    channels = arrivals.shape[1]
    capacity = arrivals.shape[2]
    length = filter_taps.shape[1]
    n_blocks = length // T_DEV
    own = channels // n_ctx
    forward, inverse = dft_tables()

    payload = pl.pallas_call(
        functools.partial(sender_kernel, n_ctx=n_ctx, own=own),
        in_specs=[
            pl.BlockSpec(memory_space=pltpu.SMEM),
            pl.BlockSpec(memory_space=pltpu.VMEM),
            pl.BlockSpec(memory_space=pltpu.VMEM),
        ],
        out_specs=pl.BlockSpec(memory_space=pltpu.VMEM),
        out_shape=jax.ShapeDtypeStruct((n_ctx, 2 * own + 1, capacity), jnp.bfloat16),
    )(counts, arrivals, short_taps)
    got = lax.all_to_all(payload, "ctx", 0, 0, tiled=False)
    rows = got[:, : 2 * own]
    edge_in = got[:, 2 * own]
    every_count = (
        edge_in[:, own * 8].astype(jnp.int32) * 16 + edge_in[:, own * 8 + 1].astype(jnp.int32)
    )
    offsets = jnp.cumsum(every_count) - every_count

    frame = 2 * T_DEV
    row = jnp.arange(capacity, dtype=jnp.int32)[None, :, None]
    col = jnp.arange(frame, dtype=jnp.int32)[None, None, :]
    sampler = jnp.arange(n_ctx, dtype=jnp.int32)[:, None, None]
    shift = offsets[:, None, None] - (sampler - 1) * T_DEV - HALF
    select = ((row + shift == col) & (row < every_count[:, None, None])).astype(jnp.bfloat16)
    placed = jnp.einsum("icr,irj->icj", rows, select, preferred_element_type=jnp.bfloat16)
    full = sum(
        jnp.pad(placed[i], ((0, 0), (i * T_DEV + HALF, (n_ctx - i) * T_DEV - HALF)))
        for i in range(n_ctx)
    )
    first = device * own
    taps = lax.dynamic_slice_in_dim(short_taps, first, own, 2)
    gate = full[:own, T_DEV - 2 : T_DEV + length].astype(jnp.float32)
    shorted_gate = taps[0, 0, :, None] * gate[:, 2:]
    shorted_gate = shorted_gate + taps[0, 1, :, None] * gate[:, 1:-1]
    shorted_gate = shorted_gate + taps[0, 2, :, None] * gate[:, :-2]
    from_senders = full[own:, T_DEV : T_DEV + length]

    values = edge_in[:, : own * 8].reshape(n_ctx, own, 8)
    count_col = every_count[:, None]
    at_row = jnp.concatenate(
        [jnp.zeros_like(count_col), jnp.ones_like(count_col), count_col - 2, count_col - 1], axis=1
    )
    valid = jnp.concatenate([at_row[:, :2] < count_col, at_row[:, 2:] >= 2], axis=1)
    spot = offsets[:, None] + at_row
    slot = jnp.arange(length + 2, dtype=jnp.int32)[None, None, :]
    marks = ((slot - 2 == spot[:, :, None]) & valid[:, :, None]).astype(jnp.bfloat16)
    near_in = []
    for part in range(2):
        pick = jnp.concatenate(
            [values[:, :, 2 * part : 2 * part + 2], values[:, :, 4 + 2 * part : 6 + 2 * part]], axis=2
        )
        around = jnp.einsum(
            "ics,isj->cj", pick, marks, preferred_element_type=jnp.float32
        )
        s = taps[1 + part, 0, :, None] * around[:, 2:]
        s = s + taps[1 + part, 1, :, None] * around[:, 1:-1]
        s = s + taps[1 + part, 2, :, None] * around[:, :-2]
        near_in.append(s)
    at_start = jnp.sum(marks[:, :2, 2:].astype(jnp.float32), axis=(0, 1)) > 0
    mixed_input = jnp.where(
        at_start[None, :], (near_in[0] * near_in[1]).astype(jnp.bfloat16), from_senders
    )

    x_spec = transform(mixed_input.reshape(own, n_blocks, T_DEV), forward, "cnt,tf->cnf")
    own_taps = lax.dynamic_slice_in_dim(filter_taps, first, own, 0)
    tap_blocks = jnp.concatenate(
        [jnp.zeros((own, T_DEV), own_taps.dtype), own_taps], axis=1
    ).reshape(own, n_blocks + 1, T_DEV)
    h_spec = transform(tap_blocks, forward, "cnt,tf->cnf")
    column = jnp.arange(PERIOD, dtype=jnp.int32) % T_DEV
    signs = jnp.where(column % 2 == 0, 1.0, -1.0).astype(jnp.float32)
    g_spec = h_spec[:, 1:] + signs * h_spec[:, :-1]
    xr, xi = x_spec[..., :T_DEV], x_spec[..., T_DEV:]
    gr, gi = g_spec[..., :T_DEV], g_spec[..., T_DEV:]
    sums = [jnp.zeros((own, n_blocks, T_DEV), jnp.float32) for _ in range(4)]
    for k in range(n_blocks):
        pad = ((0, 0), (k, 0), (0, 0))
        terms = (
            xr[:, : n_blocks - k] * gr[:, k : k + 1],
            xi[:, : n_blocks - k] * gi[:, k : k + 1],
            xr[:, : n_blocks - k] * gi[:, k : k + 1],
            xi[:, : n_blocks - k] * gr[:, k : k + 1],
        )
        sums = [s + jnp.pad(t, pad) for s, t in zip(sums, terms)]
    rr, ii, ri, ir = sums
    at_zero = jnp.arange(T_DEV, dtype=jnp.int32)[None, None, :] == 0
    spectrum = jnp.concatenate(
        [jnp.where(at_zero, rr, rr - ii), jnp.where(at_zero, ii, ri + ir)], axis=2
    )
    conv_core = jnp.einsum("cnf,ft->cnt", spectrum, inverse, precision=lax.Precision.HIGHEST)
    gains = lax.dynamic_slice_in_dim(skip_gain, first, own, 0)
    conv = conv_core.reshape(own, length) + gains[:, None] * mixed_input.astype(jnp.float32)
    gated = (shorted_gate * conv).astype(jnp.bfloat16)
    back = lax.all_to_all(gated.reshape(own, n_ctx, T_DEV), "ctx", 1, 0, tiled=False)
    gated_block = back.reshape(channels, T_DEV)
    mixed = jnp.dot(
        out_weight,
        lax.all_gather(gated_block, "ch", axis=0, tiled=True),
        preferred_element_type=jnp.float32,
    )
    return mixed.astype(jnp.bfloat16)


def on_device(arrivals, counts, short_taps, filter_taps, skip_gain, out_weight):
    n_ctx = lax.axis_size("ctx")
    blocks = filter_taps.shape[1] // T_DEV
    if arrivals.shape[1] % n_ctx == 0 and blocks == n_ctx:
        return by_transpose(arrivals, counts, short_taps, filter_taps, skip_gain, out_weight)
    return by_gather(arrivals, counts, short_taps, filter_taps, skip_gain, out_weight)


def solution(mesh):
    return jax.shard_map(
        on_device,
        mesh=mesh,
        in_specs=(
            P(None, "ch", "ctx"),
            P("ctx"),
            P(None, None, "ch"),
            P("ch", None),
            P("ch"),
            P("ch", None),
        ),
        out_specs=P("ch", "ctx"),
        check_vma=False,
    )
```

```python
import functools
import math

import jax
import jax.numpy as jnp
import ml_dtypes
import numpy as np
from jax import lax
from jax.experimental import pallas as pl
from jax.experimental.pallas import tpu as pltpu
from jax.sharding import PartitionSpec as P

T_DEV = 256
HALF = T_DEV // 2
PERIOD = 2 * T_DEV
GROUP = 8
EDGE = 128


def split_bf16(table):
    hi = table.astype(ml_dtypes.bfloat16)
    lo = (table - hi.astype(np.float64)).astype(ml_dtypes.bfloat16)
    return jnp.asarray(hi), jnp.asarray(lo)


def dft_tables():
    t = np.arange(T_DEV)[:, None]
    f = np.arange(T_DEV)[None, :]
    angle = 2.0 * np.pi * ((t * f) % PERIOD) / PERIOD
    forward = np.concatenate([np.cos(angle), -np.sin(angle)], axis=1)
    forward[:, T_DEV] = np.where(np.arange(T_DEV) % 2 == 0, 1.0, -1.0)
    fr = np.arange(T_DEV)[:, None]
    n = np.arange(T_DEV)[None, :]
    angle = 2.0 * np.pi * ((fr * n) % PERIOD) / PERIOD
    inv_re = 2.0 * np.cos(angle) / PERIOD
    inv_re[0, :] = 1.0 / PERIOD
    inv_im = -2.0 * np.sin(angle) / PERIOD
    inv_im[0, :] = np.where(np.arange(T_DEV) % 2 == 0, 1.0, -1.0) / PERIOD
    inverse = np.concatenate([inv_re, inv_im], axis=0).astype(np.float32)
    return split_bf16(forward), jnp.asarray(inverse)


def transform(blocks, forward, spec="kct,tf->kcf"):
    hi, lo = forward
    return jnp.einsum(spec, blocks, hi, preferred_element_type=jnp.float32) + jnp.einsum(
        spec, blocks, lo, preferred_element_type=jnp.float32
    )


def kernel_spectra(tap_blocks, forward):
    spectra = transform(tap_blocks, forward)
    column = jnp.arange(PERIOD, dtype=jnp.int32) % T_DEV
    signs = jnp.where(column % 2 == 0, 1.0, -1.0).astype(jnp.float32)
    return spectra[1:] + signs * spectra[:-1]


def products(x_spec, g_spec):
    xr, xi = x_spec[..., :T_DEV], x_spec[..., T_DEV:]
    gr, gi = g_spec[..., :T_DEV], g_spec[..., T_DEV:]
    return (
        jnp.sum(xr * gr, axis=0),
        jnp.sum(xi * gi, axis=0),
        jnp.sum(xr * gi, axis=0),
        jnp.sum(xi * gr, axis=0),
    )


def by_gather(arrivals, counts, short_taps, filter_taps, skip_gain, out_weight):
    n_ctx = lax.axis_size("ctx")
    device = lax.axis_index("ctx")
    channels = arrivals.shape[1]
    capacity = arrivals.shape[2]
    n_blocks = filter_taps.shape[1] // T_DEV
    forward, inverse = dft_tables()

    every_count = lax.all_gather(counts, "ctx", axis=0, tiled=True)
    earlier = jnp.arange(n_ctx, dtype=jnp.int32) < device
    offset = jnp.sum(jnp.where(earlier, every_count, 0))
    count = counts[0]

    frame = 2 * T_DEV
    row = jnp.arange(capacity, dtype=jnp.int32)[:, None]
    col = jnp.arange(frame, dtype=jnp.int32)[None, :]
    shift = offset - device * T_DEV + HALF
    select = ((row + shift == col) & (row < count)).astype(jnp.bfloat16)
    placed = jnp.einsum(
        "pcr,rj->pcj", arrivals, select, preferred_element_type=jnp.float32
    ).astype(jnp.bfloat16)
    to_prev = placed[:, :, :HALF]
    to_next = placed[:, :, frame - HALF - 2 :]
    from_next = lax.ppermute(to_prev, "ctx", [(i + 1, i) for i in range(n_ctx - 1)])
    from_prev = lax.ppermute(to_next, "ctx", [(i, i + 1) for i in range(n_ctx - 1)])
    window = placed[:, :, HALF - 2 : HALF + T_DEV]
    window = window + jnp.pad(from_prev, ((0, 0), (0, 0), (0, T_DEV - HALF)))
    window = window + jnp.pad(from_next, ((0, 0), (0, 0), (T_DEV + 2 - HALF, 0)))
    wide = window.astype(jnp.float32)
    shorted = short_taps[:, 0, :, None] * wide[:, :, 2:]
    shorted = shorted + short_taps[:, 1, :, None] * wide[:, :, 1:-1]
    shorted = shorted + short_taps[:, 2, :, None] * wide[:, :, :-2]
    mixed_input = (shorted[1] * shorted[2]).astype(jnp.bfloat16)

    tap_blocks = jnp.stack(
        [jnp.zeros((channels, T_DEV), filter_taps.dtype)]
        + [filter_taps[:, k * T_DEV : (k + 1) * T_DEV] for k in range(n_blocks)]
    )
    every_input = lax.all_gather(mixed_input, "ctx", axis=0)
    backwards = jnp.concatenate(
        [jnp.flip(every_input, 0), jnp.zeros_like(every_input)], axis=0
    )
    start = n_ctx - 1 - device
    if n_blocks <= GROUP:
        x_blocks = lax.dynamic_slice_in_dim(backwards, start, n_blocks, 0)
        sums = products(transform(x_blocks, forward), kernel_spectra(tap_blocks, forward))
    else:
        width = max(w for w in range(1, GROUP + 1) if n_blocks % w == 0)

        def group(g, acc):
            k0 = g * width
            x_blocks = lax.dynamic_slice_in_dim(backwards, start + k0, width, 0)
            taps = lax.dynamic_slice_in_dim(tap_blocks, k0, width + 1, 0)
            part = products(transform(x_blocks, forward), kernel_spectra(taps, forward))
            return tuple(a + b for a, b in zip(acc, part))

        zero = jnp.zeros((channels, T_DEV), jnp.float32)
        sums = lax.fori_loop(0, n_blocks // width, group, (zero, zero, zero, zero))
    rr, ii, ri, ir = sums
    first = jnp.arange(T_DEV, dtype=jnp.int32)[None, :] == 0
    spec_re = jnp.where(first, rr, rr - ii)
    spec_im = jnp.where(first, ii, ri + ir)
    spectrum = jnp.concatenate([spec_re, spec_im], axis=1)
    conv_core = jnp.dot(spectrum, inverse, precision=lax.Precision.HIGHEST)
    conv = conv_core + skip_gain[:, None] * mixed_input.astype(jnp.float32)
    gated = (shorted[0] * conv).astype(jnp.bfloat16)
    mixed = jnp.dot(
        out_weight,
        lax.all_gather(gated, "ch", axis=0, tiled=True),
        preferred_element_type=jnp.float32,
    )
    return mixed.astype(jnp.bfloat16)


def sender_kernel(count_ref, arrivals_ref, taps_ref, out_ref, *, n_ctx, own):
    count = count_ref[0]
    capacity = arrivals_ref.shape[2]
    lane = lax.broadcasted_iota(jnp.int32, arrivals_ref.shape[1:], 1)
    row = lax.broadcasted_iota(jnp.int32, (capacity, EDGE), 0)
    column = lax.broadcasted_iota(jnp.int32, (capacity, EDGE), 1)
    square = lax.broadcasted_iota(jnp.int32, (lane.shape[0], lane.shape[0]), 0)
    diagonal = square == lax.broadcasted_iota(jnp.int32, square.shape, 1)

    ones = jnp.ones((lane.shape[0], EDGE), jnp.float32)

    def tap(part, k):
        spread = jnp.where(diagonal, taps_ref[part, k : k + 1, :], 0.0)
        return jnp.dot(spread, ones, precision=lax.Precision.HIGHEST)[:, :1]

    near = []
    edge = jnp.where(column[:1] == 8, (count // 16).astype(jnp.float32), 0.0)
    edge = jnp.where(column[:1] == 9, (count % 16).astype(jnp.float32), edge)
    for part in range(2):
        raw = arrivals_ref[1 + part]
        x = raw.astype(jnp.float32)
        back1 = jnp.where(lane >= 1, pltpu.roll(x, 1, 1), 0.0)
        back2 = jnp.where(lane >= 2, pltpu.roll(x, 2, 1), 0.0)
        s = tap(1 + part, 0) * x
        s = s + tap(1 + part, 1) * back1
        s = s + tap(1 + part, 2) * back2
        near.append(s)
        wanted = jnp.where(column >= 4, count - 2 + column - 4 - 2 * part, column - 2 * part)
        inside = (column % 4 >= 2 * part) & (column % 4 < 2 * part + 2) & (column < 8)
        pick = ((row == wanted) & inside).astype(jnp.bfloat16)
        edge = edge + jnp.dot(raw, pick, preferred_element_type=jnp.float32)
    mixed = (near[0] * near[1]).astype(jnp.bfloat16)
    edge = edge.astype(jnp.bfloat16)
    flat_lane = lax.broadcasted_iota(jnp.int32, (EDGE, capacity), 1)
    spread = (
        (flat_lane < 8 * own) & (flat_lane % 8 == lax.broadcasted_iota(jnp.int32, (EDGE, capacity), 0))
    ).astype(jnp.bfloat16)
    channel = lax.broadcasted_iota(jnp.int32, (own, capacity), 0)
    lane_out = lax.broadcasted_iota(jnp.int32, (own, capacity), 1)
    code = jnp.where(lane_out[:1] == 8 * own, (count // 16).astype(jnp.float32), 0.0)
    code = jnp.where(lane_out[:1] == 8 * own + 1, (count % 16).astype(jnp.float32), code)
    for j in range(n_ctx):
        rows = slice(j * own, (j + 1) * own)
        out_ref[j, :own, :] = arrivals_ref[0, rows, :]
        out_ref[j, own : 2 * own, :] = mixed[rows]
        tiled = jnp.dot(edge[rows], spread, preferred_element_type=jnp.float32)
        flat = jnp.sum(jnp.where(lane_out // 8 == channel, tiled, 0.0), axis=0, keepdims=True)
        out_ref[j, 2 * own : 2 * own + 1, :] = (flat + code).astype(jnp.bfloat16)


def by_transpose(arrivals, counts, short_taps, filter_taps, skip_gain, out_weight):
    n_ctx = lax.axis_size("ctx")
    device = lax.axis_index("ctx")
    channels = arrivals.shape[1]
    capacity = arrivals.shape[2]
    length = filter_taps.shape[1]
    n_blocks = length // T_DEV
    own = channels // n_ctx
    forward, inverse = dft_tables()

    payload = pl.pallas_call(
        functools.partial(sender_kernel, n_ctx=n_ctx, own=own),
        in_specs=[
            pl.BlockSpec(memory_space=pltpu.SMEM),
            pl.BlockSpec(memory_space=pltpu.VMEM),
            pl.BlockSpec(memory_space=pltpu.VMEM),
        ],
        out_specs=pl.BlockSpec(memory_space=pltpu.VMEM),
        out_shape=jax.ShapeDtypeStruct((n_ctx, 2 * own + 1, capacity), jnp.bfloat16),
    )(counts, arrivals, short_taps)
    got = lax.all_to_all(payload, "ctx", 0, 0, tiled=False)
    rows = got[:, : 2 * own]
    edge_in = got[:, 2 * own]
    every_count = (
        edge_in[:, own * 8].astype(jnp.int32) * 16 + edge_in[:, own * 8 + 1].astype(jnp.int32)
    )
    offsets = jnp.cumsum(every_count) - every_count

    frame = 2 * T_DEV
    row = jnp.arange(capacity, dtype=jnp.int32)[None, :, None]
    col = jnp.arange(frame, dtype=jnp.int32)[None, None, :]
    sampler = jnp.arange(n_ctx, dtype=jnp.int32)[:, None, None]
    shift = offsets[:, None, None] - (sampler - 1) * T_DEV - HALF
    select = ((row + shift == col) & (row < every_count[:, None, None])).astype(jnp.bfloat16)
    placed = jnp.einsum("icr,irj->icj", rows, select, preferred_element_type=jnp.bfloat16)
    full = sum(
        jnp.pad(placed[i], ((0, 0), (i * T_DEV + HALF, (n_ctx - i) * T_DEV - HALF)))
        for i in range(n_ctx)
    )
    first = device * own
    taps = lax.dynamic_slice_in_dim(short_taps, first, own, 2)
    gate = full[:own, T_DEV - 2 : T_DEV + length].astype(jnp.float32)
    shorted_gate = taps[0, 0, :, None] * gate[:, 2:]
    shorted_gate = shorted_gate + taps[0, 1, :, None] * gate[:, 1:-1]
    shorted_gate = shorted_gate + taps[0, 2, :, None] * gate[:, :-2]
    from_senders = full[own:, T_DEV : T_DEV + length]

    values = edge_in[:, : own * 8].reshape(n_ctx, own, 8)
    count_col = every_count[:, None]
    at_row = jnp.concatenate(
        [jnp.zeros_like(count_col), jnp.ones_like(count_col), count_col - 2, count_col - 1], axis=1
    )
    valid = jnp.concatenate([at_row[:, :2] < count_col, at_row[:, 2:] >= 2], axis=1)
    spot = offsets[:, None] + at_row
    slot = jnp.arange(length + 2, dtype=jnp.int32)[None, None, :]
    marks = ((slot - 2 == spot[:, :, None]) & valid[:, :, None]).astype(jnp.bfloat16)
    near_in = []
    for part in range(2):
        pick = jnp.concatenate(
            [values[:, :, 2 * part : 2 * part + 2], values[:, :, 4 + 2 * part : 6 + 2 * part]], axis=2
        )
        around = jnp.einsum(
            "ics,isj->cj", pick, marks, preferred_element_type=jnp.float32
        )
        s = taps[1 + part, 0, :, None] * around[:, 2:]
        s = s + taps[1 + part, 1, :, None] * around[:, 1:-1]
        s = s + taps[1 + part, 2, :, None] * around[:, :-2]
        near_in.append(s)
    at_start = jnp.sum(marks[:, :2, 2:].astype(jnp.float32), axis=(0, 1)) > 0
    mixed_input = jnp.where(
        at_start[None, :], (near_in[0] * near_in[1]).astype(jnp.bfloat16), from_senders
    )

    x_spec = transform(mixed_input.reshape(own, n_blocks, T_DEV), forward, "cnt,tf->cnf")
    own_taps = lax.dynamic_slice_in_dim(filter_taps, first, own, 0)
    tap_blocks = jnp.concatenate(
        [jnp.zeros((own, T_DEV), own_taps.dtype), own_taps], axis=1
    ).reshape(own, n_blocks + 1, T_DEV)
    h_spec = transform(tap_blocks, forward, "cnt,tf->cnf")
    column = jnp.arange(PERIOD, dtype=jnp.int32) % T_DEV
    signs = jnp.where(column % 2 == 0, 1.0, -1.0).astype(jnp.float32)
    g_spec = h_spec[:, 1:] + signs * h_spec[:, :-1]
    xr, xi = x_spec[..., :T_DEV], x_spec[..., T_DEV:]
    gr, gi = g_spec[..., :T_DEV], g_spec[..., T_DEV:]
    sums = [jnp.zeros((own, n_blocks, T_DEV), jnp.float32) for _ in range(4)]
    for k in range(n_blocks):
        pad = ((0, 0), (k, 0), (0, 0))
        terms = (
            xr[:, : n_blocks - k] * gr[:, k : k + 1],
            xi[:, : n_blocks - k] * gi[:, k : k + 1],
            xr[:, : n_blocks - k] * gi[:, k : k + 1],
            xi[:, : n_blocks - k] * gr[:, k : k + 1],
        )
        sums = [s + jnp.pad(t, pad) for s, t in zip(sums, terms)]
    rr, ii, ri, ir = sums
    at_zero = jnp.arange(T_DEV, dtype=jnp.int32)[None, None, :] == 0
    spectrum = jnp.concatenate(
        [jnp.where(at_zero, rr, rr - ii), jnp.where(at_zero, ii, ri + ir)], axis=2
    )
    conv_core = jnp.einsum("cnf,ft->cnt", spectrum, inverse, precision=lax.Precision.HIGHEST)
    gains = lax.dynamic_slice_in_dim(skip_gain, first, own, 0)
    conv = conv_core.reshape(own, length) + gains[:, None] * mixed_input.astype(jnp.float32)
    gated = (shorted_gate * conv).astype(jnp.bfloat16)
    back = lax.all_to_all(gated.reshape(own, n_ctx, T_DEV), "ctx", 1, 0, tiled=False)
    gated_block = back.reshape(channels, T_DEV)
    mixed = jnp.dot(
        out_weight,
        lax.all_gather(gated_block, "ch", axis=0, tiled=True),
        preferred_element_type=jnp.float32,
    )
    return mixed.astype(jnp.bfloat16)


def on_device(arrivals, counts, short_taps, filter_taps, skip_gain, out_weight):
    n_ctx = lax.axis_size("ctx")
    blocks = filter_taps.shape[1] // T_DEV
    if arrivals.shape[1] % n_ctx == 0 and blocks == n_ctx:
        return by_transpose(arrivals, counts, short_taps, filter_taps, skip_gain, out_weight)
    return by_gather(arrivals, counts, short_taps, filter_taps, skip_gain, out_weight)


def solution(mesh):
    return jax.shard_map(
        on_device,
        mesh=mesh,
        in_specs=(
            P(None, "ch", "ctx"),
            P("ctx"),
            P(None, None, "ch"),
            P("ch", None),
            P("ch"),
            P("ch", None),
        ),
        out_specs=P("ch", "ctx"),
        check_vma=False,
    )
```

```python
import functools
import math

import jax
import jax.numpy as jnp
import ml_dtypes
import numpy as np
from jax import lax
from jax.experimental import pallas as pl
from jax.experimental.pallas import tpu as pltpu
from jax.sharding import PartitionSpec as P

T_DEV = 256
HALF = T_DEV // 2
PERIOD = 2 * T_DEV
GROUP = 8
EDGE = 128


def split_bf16(table):
    hi = table.astype(ml_dtypes.bfloat16)
    lo = (table - hi.astype(np.float64)).astype(ml_dtypes.bfloat16)
    return jnp.asarray(hi), jnp.asarray(lo)


def dft_tables():
    t = np.arange(T_DEV)[:, None]
    f = np.arange(T_DEV)[None, :]
    angle = 2.0 * np.pi * ((t * f) % PERIOD) / PERIOD
    forward = np.concatenate([np.cos(angle), -np.sin(angle)], axis=1)
    forward[:, T_DEV] = np.where(np.arange(T_DEV) % 2 == 0, 1.0, -1.0)
    fr = np.arange(T_DEV)[:, None]
    n = np.arange(T_DEV)[None, :]
    angle = 2.0 * np.pi * ((fr * n) % PERIOD) / PERIOD
    inv_re = 2.0 * np.cos(angle) / PERIOD
    inv_re[0, :] = 1.0 / PERIOD
    inv_im = -2.0 * np.sin(angle) / PERIOD
    inv_im[0, :] = np.where(np.arange(T_DEV) % 2 == 0, 1.0, -1.0) / PERIOD
    inverse = np.concatenate([inv_re, inv_im], axis=0).astype(np.float32)
    return split_bf16(forward), jnp.asarray(inverse)


def transform(blocks, forward, spec="kct,tf->kcf"):
    hi, lo = forward
    return jnp.einsum(spec, blocks, hi, preferred_element_type=jnp.float32) + jnp.einsum(
        spec, blocks, lo, preferred_element_type=jnp.float32
    )


def kernel_spectra(tap_blocks, forward):
    spectra = transform(tap_blocks, forward)
    column = jnp.arange(PERIOD, dtype=jnp.int32) % T_DEV
    signs = jnp.where(column % 2 == 0, 1.0, -1.0).astype(jnp.float32)
    return spectra[1:] + signs * spectra[:-1]


def products(x_spec, g_spec):
    xr, xi = x_spec[..., :T_DEV], x_spec[..., T_DEV:]
    gr, gi = g_spec[..., :T_DEV], g_spec[..., T_DEV:]
    return (
        jnp.sum(xr * gr, axis=0),
        jnp.sum(xi * gi, axis=0),
        jnp.sum(xr * gi, axis=0),
        jnp.sum(xi * gr, axis=0),
    )


def by_gather(arrivals, counts, short_taps, filter_taps, skip_gain, out_weight):
    n_ctx = lax.axis_size("ctx")
    device = lax.axis_index("ctx")
    channels = arrivals.shape[1]
    capacity = arrivals.shape[2]
    n_blocks = filter_taps.shape[1] // T_DEV
    forward, inverse = dft_tables()

    every_count = lax.all_gather(counts, "ctx", axis=0, tiled=True)
    earlier = jnp.arange(n_ctx, dtype=jnp.int32) < device
    offset = jnp.sum(jnp.where(earlier, every_count, 0))
    count = counts[0]

    frame = 2 * T_DEV
    row = jnp.arange(capacity, dtype=jnp.int32)[:, None]
    col = jnp.arange(frame, dtype=jnp.int32)[None, :]
    shift = offset - device * T_DEV + HALF
    select = ((row + shift == col) & (row < count)).astype(jnp.bfloat16)
    placed = jnp.einsum(
        "pcr,rj->pcj", arrivals, select, preferred_element_type=jnp.float32
    ).astype(jnp.bfloat16)
    to_prev = placed[:, :, :HALF]
    to_next = placed[:, :, frame - HALF - 2 :]
    from_next = lax.ppermute(to_prev, "ctx", [(i + 1, i) for i in range(n_ctx - 1)])
    from_prev = lax.ppermute(to_next, "ctx", [(i, i + 1) for i in range(n_ctx - 1)])
    window = placed[:, :, HALF - 2 : HALF + T_DEV]
    window = window + jnp.pad(from_prev, ((0, 0), (0, 0), (0, T_DEV - HALF)))
    window = window + jnp.pad(from_next, ((0, 0), (0, 0), (T_DEV + 2 - HALF, 0)))
    wide = window.astype(jnp.float32)
    shorted = short_taps[:, 0, :, None] * wide[:, :, 2:]
    shorted = shorted + short_taps[:, 1, :, None] * wide[:, :, 1:-1]
    shorted = shorted + short_taps[:, 2, :, None] * wide[:, :, :-2]
    mixed_input = (shorted[1] * shorted[2]).astype(jnp.bfloat16)

    tap_blocks = jnp.stack(
        [jnp.zeros((channels, T_DEV), filter_taps.dtype)]
        + [filter_taps[:, k * T_DEV : (k + 1) * T_DEV] for k in range(n_blocks)]
    )
    every_input = lax.all_gather(mixed_input, "ctx", axis=0)
    backwards = jnp.concatenate(
        [jnp.flip(every_input, 0), jnp.zeros_like(every_input)], axis=0
    )
    start = n_ctx - 1 - device
    if n_blocks <= GROUP:
        x_blocks = lax.dynamic_slice_in_dim(backwards, start, n_blocks, 0)
        sums = products(transform(x_blocks, forward), kernel_spectra(tap_blocks, forward))
    else:
        width = max(w for w in range(1, GROUP + 1) if n_blocks % w == 0)

        def group(g, acc):
            k0 = g * width
            x_blocks = lax.dynamic_slice_in_dim(backwards, start + k0, width, 0)
            taps = lax.dynamic_slice_in_dim(tap_blocks, k0, width + 1, 0)
            part = products(transform(x_blocks, forward), kernel_spectra(taps, forward))
            return tuple(a + b for a, b in zip(acc, part))

        zero = jnp.zeros((channels, T_DEV), jnp.float32)
        sums = lax.fori_loop(0, n_blocks // width, group, (zero, zero, zero, zero))
    rr, ii, ri, ir = sums
    first = jnp.arange(T_DEV, dtype=jnp.int32)[None, :] == 0
    spec_re = jnp.where(first, rr, rr - ii)
    spec_im = jnp.where(first, ii, ri + ir)
    spectrum = jnp.concatenate([spec_re, spec_im], axis=1)
    conv_core = jnp.dot(spectrum, inverse, precision=lax.Precision.HIGHEST)
    conv = conv_core + skip_gain[:, None] * mixed_input.astype(jnp.float32)
    gated = (shorted[0] * conv).astype(jnp.bfloat16)
    mixed = jnp.dot(
        out_weight,
        lax.all_gather(gated, "ch", axis=0, tiled=True),
        preferred_element_type=jnp.float32,
    )
    return mixed.astype(jnp.bfloat16)


def sender_kernel(count_ref, arrivals_ref, taps_ref, out_ref, *, n_ctx, own):
    count = count_ref[0]
    capacity = arrivals_ref.shape[2]
    channels = arrivals_ref.shape[1]
    lane = lax.broadcasted_iota(jnp.int32, (own, capacity), 1)
    channel = lax.broadcasted_iota(jnp.int32, (own, capacity), 0)
    row = lax.broadcasted_iota(jnp.int32, (capacity, EDGE), 0)
    column = lax.broadcasted_iota(jnp.int32, (capacity, EDGE), 1)
    picks = []
    for part in range(2):
        wanted = jnp.where(column >= 4, count - 2 + column - 4 - 2 * part, column - 2 * part)
        inside = (column % 4 >= 2 * part) & (column % 4 < 2 * part + 2) & (column < 8)
        picks.append(((row == wanted) & inside).astype(jnp.bfloat16))
    flat_lane = lax.broadcasted_iota(jnp.int32, (EDGE, capacity), 1)
    spread = (
        (flat_lane < 8 * own) & (flat_lane % 8 == lax.broadcasted_iota(jnp.int32, (EDGE, capacity), 0))
    ).astype(jnp.bfloat16)
    code = jnp.where(lane[:1] == 8 * own, (count // 16).astype(jnp.float32), 0.0)
    code = jnp.where(lane[:1] == 8 * own + 1, (count % 16).astype(jnp.float32), code)
    tap_lane = lax.broadcasted_iota(jnp.int32, (own, channels), 1)
    tap_row = lax.broadcasted_iota(jnp.int32, (own, channels), 0)
    for j in range(n_ctx):
        rows = slice(j * own, (j + 1) * own)
        mine = tap_lane == tap_row + j * own

        def tap(part, k):
            return jnp.sum(jnp.where(mine, taps_ref[part, k : k + 1, :], 0.0), axis=1, keepdims=True)

        near = []
        edge = jnp.zeros((own, EDGE), jnp.float32)
        for part in range(2):
            raw = arrivals_ref[1 + part, rows, :]
            x = raw.astype(jnp.float32)
            back1 = jnp.where(lane >= 1, pltpu.roll(x, 1, 1), 0.0)
            back2 = jnp.where(lane >= 2, pltpu.roll(x, 2, 1), 0.0)
            s = tap(1 + part, 0) * x
            s = s + tap(1 + part, 1) * back1
            s = s + tap(1 + part, 2) * back2
            near.append(s)
            edge = edge + jnp.dot(raw, picks[part], preferred_element_type=jnp.float32)
        out_ref[j, :own, :] = arrivals_ref[0, rows, :]
        out_ref[j, own : 2 * own, :] = (near[0] * near[1]).astype(jnp.bfloat16)
        tiled = jnp.dot(edge.astype(jnp.bfloat16), spread, preferred_element_type=jnp.float32)
        flat = jnp.sum(jnp.where(lane // 8 == channel, tiled, 0.0), axis=0, keepdims=True)
        out_ref[j, 2 * own : 2 * own + 1, :] = (flat + code).astype(jnp.bfloat16)


def by_transpose(arrivals, counts, short_taps, filter_taps, skip_gain, out_weight):
    n_ctx = lax.axis_size("ctx")
    device = lax.axis_index("ctx")
    channels = arrivals.shape[1]
    capacity = arrivals.shape[2]
    length = filter_taps.shape[1]
    n_blocks = length // T_DEV
    own = channels // n_ctx
    forward, inverse = dft_tables()

    payload = pl.pallas_call(
        functools.partial(sender_kernel, n_ctx=n_ctx, own=own),
        in_specs=[
            pl.BlockSpec(memory_space=pltpu.SMEM),
            pl.BlockSpec(memory_space=pltpu.VMEM),
            pl.BlockSpec(memory_space=pltpu.VMEM),
        ],
        out_specs=pl.BlockSpec(memory_space=pltpu.VMEM),
        out_shape=jax.ShapeDtypeStruct((n_ctx, 2 * own + 1, capacity), jnp.bfloat16),
    )(counts, arrivals, short_taps)
    got = lax.all_to_all(payload, "ctx", 0, 0, tiled=False)
    rows = got[:, : 2 * own]
    edge_in = got[:, 2 * own]
    every_count = (
        edge_in[:, own * 8].astype(jnp.int32) * 16 + edge_in[:, own * 8 + 1].astype(jnp.int32)
    )
    offsets = jnp.cumsum(every_count) - every_count

    frame = 2 * T_DEV
    row = jnp.arange(capacity, dtype=jnp.int32)[None, :, None]
    col = jnp.arange(frame, dtype=jnp.int32)[None, None, :]
    sampler = jnp.arange(n_ctx, dtype=jnp.int32)[:, None, None]
    shift = offsets[:, None, None] - (sampler - 1) * T_DEV - HALF
    select = ((row + shift == col) & (row < every_count[:, None, None])).astype(jnp.bfloat16)
    placed = jnp.einsum("icr,irj->icj", rows, select, preferred_element_type=jnp.bfloat16)
    full = sum(
        jnp.pad(placed[i], ((0, 0), (i * T_DEV + HALF, (n_ctx - i) * T_DEV - HALF)))
        for i in range(n_ctx)
    )
    first = device * own
    taps = lax.dynamic_slice_in_dim(short_taps, first, own, 2)
    gate = full[:own, T_DEV - 2 : T_DEV + length].astype(jnp.float32)
    shorted_gate = taps[0, 0, :, None] * gate[:, 2:]
    shorted_gate = shorted_gate + taps[0, 1, :, None] * gate[:, 1:-1]
    shorted_gate = shorted_gate + taps[0, 2, :, None] * gate[:, :-2]
    from_senders = full[own:, T_DEV : T_DEV + length]

    values = edge_in[:, : own * 8].reshape(n_ctx, own, 8)
    count_col = every_count[:, None]
    at_row = jnp.concatenate(
        [jnp.zeros_like(count_col), jnp.ones_like(count_col), count_col - 2, count_col - 1], axis=1
    )
    valid = jnp.concatenate([at_row[:, :2] < count_col, at_row[:, 2:] >= 2], axis=1)
    spot = offsets[:, None] + at_row
    slot = jnp.arange(length + 2, dtype=jnp.int32)[None, None, :]
    marks = ((slot - 2 == spot[:, :, None]) & valid[:, :, None]).astype(jnp.bfloat16)
    near_in = []
    for part in range(2):
        pick = jnp.concatenate(
            [values[:, :, 2 * part : 2 * part + 2], values[:, :, 4 + 2 * part : 6 + 2 * part]], axis=2
        )
        around = jnp.einsum(
            "ics,isj->cj", pick, marks, preferred_element_type=jnp.float32
        )
        s = taps[1 + part, 0, :, None] * around[:, 2:]
        s = s + taps[1 + part, 1, :, None] * around[:, 1:-1]
        s = s + taps[1 + part, 2, :, None] * around[:, :-2]
        near_in.append(s)
    at_start = jnp.sum(marks[:, :2, 2:].astype(jnp.float32), axis=(0, 1)) > 0
    mixed_input = jnp.where(
        at_start[None, :], (near_in[0] * near_in[1]).astype(jnp.bfloat16), from_senders
    )

    x_spec = transform(mixed_input.reshape(own, n_blocks, T_DEV), forward, "cnt,tf->cnf")
    own_taps = lax.dynamic_slice_in_dim(filter_taps, first, own, 0)
    tap_blocks = jnp.concatenate(
        [jnp.zeros((own, T_DEV), own_taps.dtype), own_taps], axis=1
    ).reshape(own, n_blocks + 1, T_DEV)
    h_spec = transform(tap_blocks, forward, "cnt,tf->cnf")
    column = jnp.arange(PERIOD, dtype=jnp.int32) % T_DEV
    signs = jnp.where(column % 2 == 0, 1.0, -1.0).astype(jnp.float32)
    g_spec = h_spec[:, 1:] + signs * h_spec[:, :-1]
    xr, xi = x_spec[..., :T_DEV], x_spec[..., T_DEV:]
    gr, gi = g_spec[..., :T_DEV], g_spec[..., T_DEV:]
    sums = [jnp.zeros((own, n_blocks, T_DEV), jnp.float32) for _ in range(4)]
    for k in range(n_blocks):
        pad = ((0, 0), (k, 0), (0, 0))
        terms = (
            xr[:, : n_blocks - k] * gr[:, k : k + 1],
            xi[:, : n_blocks - k] * gi[:, k : k + 1],
            xr[:, : n_blocks - k] * gi[:, k : k + 1],
            xi[:, : n_blocks - k] * gr[:, k : k + 1],
        )
        sums = [s + jnp.pad(t, pad) for s, t in zip(sums, terms)]
    rr, ii, ri, ir = sums
    at_zero = jnp.arange(T_DEV, dtype=jnp.int32)[None, None, :] == 0
    spectrum = jnp.concatenate(
        [jnp.where(at_zero, rr, rr - ii), jnp.where(at_zero, ii, ri + ir)], axis=2
    )
    conv_core = jnp.einsum("cnf,ft->cnt", spectrum, inverse, precision=lax.Precision.HIGHEST)
    gains = lax.dynamic_slice_in_dim(skip_gain, first, own, 0)
    conv = conv_core.reshape(own, length) + gains[:, None] * mixed_input.astype(jnp.float32)
    gated = (shorted_gate * conv).astype(jnp.bfloat16)
    back = lax.all_to_all(gated.reshape(own, n_ctx, T_DEV), "ctx", 1, 0, tiled=False)
    gated_block = back.reshape(channels, T_DEV)
    mixed = jnp.dot(
        out_weight,
        lax.all_gather(gated_block, "ch", axis=0, tiled=True),
        preferred_element_type=jnp.float32,
    )
    return mixed.astype(jnp.bfloat16)


def on_device(arrivals, counts, short_taps, filter_taps, skip_gain, out_weight):
    n_ctx = lax.axis_size("ctx")
    blocks = filter_taps.shape[1] // T_DEV
    if arrivals.shape[1] % n_ctx == 0 and blocks == n_ctx:
        return by_transpose(arrivals, counts, short_taps, filter_taps, skip_gain, out_weight)
    return by_gather(arrivals, counts, short_taps, filter_taps, skip_gain, out_weight)


def solution(mesh):
    return jax.shard_map(
        on_device,
        mesh=mesh,
        in_specs=(
            P(None, "ch", "ctx"),
            P("ctx"),
            P(None, None, "ch"),
            P("ch", None),
            P("ch"),
            P("ch", None),
        ),
        out_specs=P("ch", "ctx"),
        check_vma=False,
    )
```

```python
import functools
import math

import jax
import jax.numpy as jnp
import ml_dtypes
import numpy as np
from jax import lax
from jax.experimental.layout import Layout, with_layout_constraint
from jax.experimental import pallas as pl
from jax.experimental.pallas import tpu as pltpu
from jax.sharding import PartitionSpec as P

T_DEV = 256
HALF = T_DEV // 2
PERIOD = 2 * T_DEV
GROUP = 8
EDGE = 128


def split_bf16(table):
    hi = table.astype(ml_dtypes.bfloat16)
    lo = (table - hi.astype(np.float64)).astype(ml_dtypes.bfloat16)
    return jnp.asarray(hi), jnp.asarray(lo)


def dft_tables():
    t = np.arange(T_DEV)[:, None]
    f = np.arange(T_DEV)[None, :]
    angle = 2.0 * np.pi * ((t * f) % PERIOD) / PERIOD
    forward = np.concatenate([np.cos(angle), -np.sin(angle)], axis=1)
    forward[:, T_DEV] = np.where(np.arange(T_DEV) % 2 == 0, 1.0, -1.0)
    fr = np.arange(T_DEV)[:, None]
    n = np.arange(T_DEV)[None, :]
    angle = 2.0 * np.pi * ((fr * n) % PERIOD) / PERIOD
    inv_re = 2.0 * np.cos(angle) / PERIOD
    inv_re[0, :] = 1.0 / PERIOD
    inv_im = -2.0 * np.sin(angle) / PERIOD
    inv_im[0, :] = np.where(np.arange(T_DEV) % 2 == 0, 1.0, -1.0) / PERIOD
    inverse = np.concatenate([inv_re, inv_im], axis=0).astype(np.float32)
    return split_bf16(forward), jnp.asarray(inverse)


def transform(blocks, forward, spec="kct,tf->kcf"):
    hi, lo = forward
    return jnp.einsum(spec, blocks, hi, preferred_element_type=jnp.float32) + jnp.einsum(
        spec, blocks, lo, preferred_element_type=jnp.float32
    )


def kernel_spectra(tap_blocks, forward):
    spectra = transform(tap_blocks, forward)
    column = jnp.arange(PERIOD, dtype=jnp.int32) % T_DEV
    signs = jnp.where(column % 2 == 0, 1.0, -1.0).astype(jnp.float32)
    return spectra[1:] + signs * spectra[:-1]


def products(x_spec, g_spec):
    xr, xi = x_spec[..., :T_DEV], x_spec[..., T_DEV:]
    gr, gi = g_spec[..., :T_DEV], g_spec[..., T_DEV:]
    return (
        jnp.sum(xr * gr, axis=0),
        jnp.sum(xi * gi, axis=0),
        jnp.sum(xr * gi, axis=0),
        jnp.sum(xi * gr, axis=0),
    )


def by_gather(arrivals, counts, short_taps, filter_taps, skip_gain, out_weight):
    n_ctx = lax.axis_size("ctx")
    device = lax.axis_index("ctx")
    channels = arrivals.shape[1]
    capacity = arrivals.shape[2]
    n_blocks = filter_taps.shape[1] // T_DEV
    forward, inverse = dft_tables()

    every_count = lax.all_gather(counts, "ctx", axis=0, tiled=True)
    earlier = jnp.arange(n_ctx, dtype=jnp.int32) < device
    offset = jnp.sum(jnp.where(earlier, every_count, 0))
    count = counts[0]

    frame = 2 * T_DEV
    row = jnp.arange(capacity, dtype=jnp.int32)[:, None]
    col = jnp.arange(frame, dtype=jnp.int32)[None, :]
    shift = offset - device * T_DEV + HALF
    select = ((row + shift == col) & (row < count)).astype(jnp.bfloat16)
    placed = jnp.einsum(
        "pcr,rj->pcj", arrivals, select, preferred_element_type=jnp.float32
    ).astype(jnp.bfloat16)
    to_prev = placed[:, :, :HALF]
    to_next = placed[:, :, frame - HALF - 2 :]
    from_next = lax.ppermute(to_prev, "ctx", [(i + 1, i) for i in range(n_ctx - 1)])
    from_prev = lax.ppermute(to_next, "ctx", [(i, i + 1) for i in range(n_ctx - 1)])
    window = placed[:, :, HALF - 2 : HALF + T_DEV]
    window = window + jnp.pad(from_prev, ((0, 0), (0, 0), (0, T_DEV - HALF)))
    window = window + jnp.pad(from_next, ((0, 0), (0, 0), (T_DEV + 2 - HALF, 0)))
    wide = window.astype(jnp.float32)
    shorted = short_taps[:, 0, :, None] * wide[:, :, 2:]
    shorted = shorted + short_taps[:, 1, :, None] * wide[:, :, 1:-1]
    shorted = shorted + short_taps[:, 2, :, None] * wide[:, :, :-2]
    mixed_input = (shorted[1] * shorted[2]).astype(jnp.bfloat16)

    tap_blocks = jnp.stack(
        [jnp.zeros((channels, T_DEV), filter_taps.dtype)]
        + [filter_taps[:, k * T_DEV : (k + 1) * T_DEV] for k in range(n_blocks)]
    )
    every_input = lax.all_gather(mixed_input, "ctx", axis=0)
    backwards = jnp.concatenate(
        [jnp.flip(every_input, 0), jnp.zeros_like(every_input)], axis=0
    )
    start = n_ctx - 1 - device
    if n_blocks <= GROUP:
        x_blocks = lax.dynamic_slice_in_dim(backwards, start, n_blocks, 0)
        sums = products(transform(x_blocks, forward), kernel_spectra(tap_blocks, forward))
    else:
        width = max(w for w in range(1, GROUP + 1) if n_blocks % w == 0)

        def group(g, acc):
            k0 = g * width
            x_blocks = lax.dynamic_slice_in_dim(backwards, start + k0, width, 0)
            taps = lax.dynamic_slice_in_dim(tap_blocks, k0, width + 1, 0)
            part = products(transform(x_blocks, forward), kernel_spectra(taps, forward))
            return tuple(a + b for a, b in zip(acc, part))

        zero = jnp.zeros((channels, T_DEV), jnp.float32)
        sums = lax.fori_loop(0, n_blocks // width, group, (zero, zero, zero, zero))
    rr, ii, ri, ir = sums
    first = jnp.arange(T_DEV, dtype=jnp.int32)[None, :] == 0
    spec_re = jnp.where(first, rr, rr - ii)
    spec_im = jnp.where(first, ii, ri + ir)
    spectrum = jnp.concatenate([spec_re, spec_im], axis=1)
    conv_core = jnp.dot(spectrum, inverse, precision=lax.Precision.HIGHEST)
    conv = conv_core + skip_gain[:, None] * mixed_input.astype(jnp.float32)
    gated = (shorted[0] * conv).astype(jnp.bfloat16)
    mixed = jnp.dot(
        out_weight,
        lax.all_gather(gated, "ch", axis=0, tiled=True),
        preferred_element_type=jnp.float32,
    )
    return mixed.astype(jnp.bfloat16)


def sender_kernel(count_ref, arrivals_ref, taps_ref, out_ref, *, n_ctx, own):
    count = count_ref[0]
    capacity = arrivals_ref.shape[2]
    lane = lax.broadcasted_iota(jnp.int32, arrivals_ref.shape[1:], 1)
    row = lax.broadcasted_iota(jnp.int32, (capacity, EDGE), 0)
    column = lax.broadcasted_iota(jnp.int32, (capacity, EDGE), 1)
    square = lax.broadcasted_iota(jnp.int32, (lane.shape[0], lane.shape[0]), 0)
    diagonal = square == lax.broadcasted_iota(jnp.int32, square.shape, 1)

    def tap(part, k):
        spread = jnp.where(diagonal, taps_ref[part, k : k + 1, :], 0.0)
        return jnp.sum(spread, axis=1, keepdims=True)

    near = []
    edge = jnp.where(column[:1] == 8, (count // 16).astype(jnp.float32), 0.0)
    edge = jnp.where(column[:1] == 9, (count % 16).astype(jnp.float32), edge)
    for part in range(2):
        raw = arrivals_ref[1 + part]
        x = raw.astype(jnp.float32)
        back1 = jnp.where(lane >= 1, pltpu.roll(x, 1, 1), 0.0)
        back2 = jnp.where(lane >= 2, pltpu.roll(x, 2, 1), 0.0)
        s = tap(1 + part, 0) * x
        s = s + tap(1 + part, 1) * back1
        s = s + tap(1 + part, 2) * back2
        near.append(s)
        wanted = jnp.where(column >= 4, count - 2 + column - 4 - 2 * part, column - 2 * part)
        inside = (column % 4 >= 2 * part) & (column % 4 < 2 * part + 2) & (column < 8)
        pick = ((row == wanted) & inside).astype(jnp.bfloat16)
        edge = edge + jnp.dot(raw, pick, preferred_element_type=jnp.float32)
    mixed = (near[0] * near[1]).astype(jnp.bfloat16)
    edge = edge.astype(jnp.bfloat16)
    flat_lane = lax.broadcasted_iota(jnp.int32, (EDGE, capacity), 1)
    spread = (
        (flat_lane < 8 * own) & (flat_lane % 8 == lax.broadcasted_iota(jnp.int32, (EDGE, capacity), 0))
    ).astype(jnp.bfloat16)
    channel = lax.broadcasted_iota(jnp.int32, (own, capacity), 0)
    lane_out = lax.broadcasted_iota(jnp.int32, (own, capacity), 1)
    code = jnp.where(lane_out[:1] == 8 * own, (count // 16).astype(jnp.float32), 0.0)
    code = jnp.where(lane_out[:1] == 8 * own + 1, (count % 16).astype(jnp.float32), code)
    for j in range(n_ctx):
        rows = slice(j * own, (j + 1) * own)
        out_ref[j, :own, :] = arrivals_ref[0, rows, :]
        out_ref[j, own : 2 * own, :] = mixed[rows]
        tiled = jnp.dot(edge[rows], spread, preferred_element_type=jnp.float32)
        flat = jnp.sum(jnp.where(lane_out // 8 == channel, tiled, 0.0), axis=0, keepdims=True)
        out_ref[j, 2 * own : 2 * own + 1, :] = (flat + code).astype(jnp.bfloat16)


def by_transpose(arrivals, counts, short_taps, filter_taps, skip_gain, out_weight):
    n_ctx = lax.axis_size("ctx")
    device = lax.axis_index("ctx")
    channels = arrivals.shape[1]
    capacity = arrivals.shape[2]
    length = filter_taps.shape[1]
    n_blocks = length // T_DEV
    own = channels // n_ctx
    forward, inverse = dft_tables()

    payload = pl.pallas_call(
        functools.partial(sender_kernel, n_ctx=n_ctx, own=own),
        in_specs=[
            pl.BlockSpec(memory_space=pltpu.SMEM),
            pl.BlockSpec(memory_space=pltpu.VMEM),
            pl.BlockSpec(memory_space=pltpu.VMEM),
        ],
        out_specs=pl.BlockSpec(memory_space=pltpu.VMEM),
        out_shape=jax.ShapeDtypeStruct((n_ctx, 2 * own + 1, capacity), jnp.bfloat16),
    )(counts, arrivals, short_taps)
    got = lax.all_to_all(payload, "ctx", 0, 0, tiled=False)
    rows = got[:, : 2 * own]
    edge_in = got[:, 2 * own]
    every_count = (
        edge_in[:, own * 8].astype(jnp.int32) * 16 + edge_in[:, own * 8 + 1].astype(jnp.int32)
    )
    offsets = jnp.cumsum(every_count) - every_count

    frame = 2 * T_DEV
    row = jnp.arange(capacity, dtype=jnp.int32)[None, :, None]
    col = jnp.arange(frame, dtype=jnp.int32)[None, None, :]
    sampler = jnp.arange(n_ctx, dtype=jnp.int32)[:, None, None]
    shift = offsets[:, None, None] - (sampler - 1) * T_DEV - HALF
    select = ((row + shift == col) & (row < every_count[:, None, None])).astype(jnp.bfloat16)
    placed = jnp.einsum("icr,irj->icj", rows, select, preferred_element_type=jnp.bfloat16)
    full = sum(
        jnp.pad(placed[i], ((0, 0), (i * T_DEV + HALF, (n_ctx - i) * T_DEV - HALF)))
        for i in range(n_ctx)
    )
    first = device * own
    taps = lax.dynamic_slice_in_dim(short_taps, first, own, 2)
    gate = full[:own, T_DEV - 2 : T_DEV + length].astype(jnp.float32)
    shorted_gate = taps[0, 0, :, None] * gate[:, 2:]
    shorted_gate = shorted_gate + taps[0, 1, :, None] * gate[:, 1:-1]
    shorted_gate = shorted_gate + taps[0, 2, :, None] * gate[:, :-2]
    from_senders = full[own:, T_DEV : T_DEV + length]

    values = edge_in[:, : own * 8].reshape(n_ctx, own, 8)
    count_col = every_count[:, None]
    at_row = jnp.concatenate(
        [jnp.zeros_like(count_col), jnp.ones_like(count_col), count_col - 2, count_col - 1], axis=1
    )
    valid = jnp.concatenate([at_row[:, :2] < count_col, at_row[:, 2:] >= 2], axis=1)
    spot = offsets[:, None] + at_row
    slot = jnp.arange(length + 2, dtype=jnp.int32)[None, None, :]
    marks = ((slot - 2 == spot[:, :, None]) & valid[:, :, None]).astype(jnp.bfloat16)
    near_in = []
    for part in range(2):
        pick = jnp.concatenate(
            [values[:, :, 2 * part : 2 * part + 2], values[:, :, 4 + 2 * part : 6 + 2 * part]], axis=2
        )
        around = jnp.einsum(
            "ics,isj->cj", pick, marks, preferred_element_type=jnp.float32
        )
        s = taps[1 + part, 0, :, None] * around[:, 2:]
        s = s + taps[1 + part, 1, :, None] * around[:, 1:-1]
        s = s + taps[1 + part, 2, :, None] * around[:, :-2]
        near_in.append(s)
    at_start = jnp.sum(marks[:, :2, 2:].astype(jnp.float32), axis=(0, 1)) > 0
    mixed_input = jnp.where(
        at_start[None, :], (near_in[0] * near_in[1]).astype(jnp.bfloat16), from_senders
    )

    x_spec = transform(mixed_input.reshape(own, n_blocks, T_DEV), forward, "cnt,tf->cnf")
    own_taps = lax.dynamic_slice_in_dim(filter_taps, first, own, 0)
    tap_blocks = jnp.concatenate(
        [jnp.zeros((own, T_DEV), own_taps.dtype), own_taps], axis=1
    ).reshape(own, n_blocks + 1, T_DEV)
    h_spec = transform(tap_blocks, forward, "cnt,tf->cnf")
    column = jnp.arange(PERIOD, dtype=jnp.int32) % T_DEV
    signs = jnp.where(column % 2 == 0, 1.0, -1.0).astype(jnp.float32)
    g_spec = h_spec[:, 1:] + signs * h_spec[:, :-1]
    xr, xi = x_spec[..., :T_DEV], x_spec[..., T_DEV:]
    gr, gi = g_spec[..., :T_DEV], g_spec[..., T_DEV:]
    sums = [jnp.zeros((own, n_blocks, T_DEV), jnp.float32) for _ in range(4)]
    for k in range(n_blocks):
        pad = ((0, 0), (k, 0), (0, 0))
        terms = (
            xr[:, : n_blocks - k] * gr[:, k : k + 1],
            xi[:, : n_blocks - k] * gi[:, k : k + 1],
            xr[:, : n_blocks - k] * gi[:, k : k + 1],
            xi[:, : n_blocks - k] * gr[:, k : k + 1],
        )
        sums = [s + jnp.pad(t, pad) for s, t in zip(sums, terms)]
    rr, ii, ri, ir = sums
    at_zero = jnp.arange(T_DEV, dtype=jnp.int32)[None, None, :] == 0
    spectrum = jnp.concatenate(
        [jnp.where(at_zero, rr, rr - ii), jnp.where(at_zero, ii, ri + ir)], axis=2
    )
    conv_core = jnp.einsum("cnf,ft->cnt", spectrum, inverse, precision=lax.Precision.HIGHEST)
    gains = lax.dynamic_slice_in_dim(skip_gain, first, own, 0)
    conv = conv_core.reshape(own, length) + gains[:, None] * mixed_input.astype(jnp.float32)
    gated = (shorted_gate * conv).astype(jnp.bfloat16)
    back = lax.all_to_all(gated.reshape(own, n_ctx, T_DEV), "ctx", 1, 0, tiled=False)
    gated_block = back.reshape(channels, T_DEV)
    mixed = jnp.dot(
        out_weight,
        lax.all_gather(gated_block, "ch", axis=0, tiled=True),
        preferred_element_type=jnp.float32,
    )
    return with_layout_constraint(mixed.astype(jnp.bfloat16), Layout((0, 1)))


def on_device(arrivals, counts, short_taps, filter_taps, skip_gain, out_weight):
    n_ctx = lax.axis_size("ctx")
    blocks = filter_taps.shape[1] // T_DEV
    if arrivals.shape[1] % n_ctx == 0 and blocks == n_ctx:
        return by_transpose(arrivals, counts, short_taps, filter_taps, skip_gain, out_weight)
    return by_gather(arrivals, counts, short_taps, filter_taps, skip_gain, out_weight)


def solution(mesh):
    return jax.shard_map(
        on_device,
        mesh=mesh,
        in_specs=(
            P(None, "ch", "ctx"),
            P("ctx"),
            P(None, None, "ch"),
            P("ch", None),
            P("ch"),
            P("ch", None),
        ),
        out_specs=P("ch", "ctx"),
        check_vma=False,
    )
```

```python
import functools
import math

import jax
import jax.numpy as jnp
import ml_dtypes
import numpy as np
from jax import lax
from jax.experimental.layout import Layout, with_layout_constraint
from jax.experimental import pallas as pl
from jax.experimental.pallas import tpu as pltpu
from jax.sharding import PartitionSpec as P

T_DEV = 256
HALF = T_DEV // 2
PERIOD = 2 * T_DEV
GROUP = 8
EDGE = 128


def split_bf16(table):
    hi = table.astype(ml_dtypes.bfloat16)
    lo = (table - hi.astype(np.float64)).astype(ml_dtypes.bfloat16)
    return jnp.asarray(hi), jnp.asarray(lo)


def dft_tables():
    t = np.arange(T_DEV)[:, None]
    f = np.arange(T_DEV)[None, :]
    angle = 2.0 * np.pi * ((t * f) % PERIOD) / PERIOD
    forward = np.concatenate([np.cos(angle), -np.sin(angle)], axis=1)
    forward[:, T_DEV] = np.where(np.arange(T_DEV) % 2 == 0, 1.0, -1.0)
    fr = np.arange(T_DEV)[:, None]
    n = np.arange(T_DEV)[None, :]
    angle = 2.0 * np.pi * ((fr * n) % PERIOD) / PERIOD
    inv_re = 2.0 * np.cos(angle) / PERIOD
    inv_re[0, :] = 1.0 / PERIOD
    inv_im = -2.0 * np.sin(angle) / PERIOD
    inv_im[0, :] = np.where(np.arange(T_DEV) % 2 == 0, 1.0, -1.0) / PERIOD
    inverse = np.concatenate([inv_re, inv_im], axis=0).astype(np.float32)
    return split_bf16(forward), jnp.asarray(inverse)


def transform(blocks, forward, spec="kct,tf->kcf"):
    hi, lo = forward
    return jnp.einsum(spec, blocks, hi, preferred_element_type=jnp.float32) + jnp.einsum(
        spec, blocks, lo, preferred_element_type=jnp.float32
    )


def kernel_spectra(tap_blocks, forward):
    spectra = transform(tap_blocks, forward)
    column = jnp.arange(PERIOD, dtype=jnp.int32) % T_DEV
    signs = jnp.where(column % 2 == 0, 1.0, -1.0).astype(jnp.float32)
    return spectra[1:] + signs * spectra[:-1]


def products(x_spec, g_spec):
    xr, xi = x_spec[..., :T_DEV], x_spec[..., T_DEV:]
    gr, gi = g_spec[..., :T_DEV], g_spec[..., T_DEV:]
    return (
        jnp.sum(xr * gr, axis=0),
        jnp.sum(xi * gi, axis=0),
        jnp.sum(xr * gi, axis=0),
        jnp.sum(xi * gr, axis=0),
    )


def by_gather(arrivals, counts, short_taps, filter_taps, skip_gain, out_weight):
    n_ctx = lax.axis_size("ctx")
    device = lax.axis_index("ctx")
    channels = arrivals.shape[1]
    capacity = arrivals.shape[2]
    n_blocks = filter_taps.shape[1] // T_DEV
    forward, inverse = dft_tables()

    every_count = lax.all_gather(counts, "ctx", axis=0, tiled=True)
    earlier = jnp.arange(n_ctx, dtype=jnp.int32) < device
    offset = jnp.sum(jnp.where(earlier, every_count, 0))
    count = counts[0]

    frame = 2 * T_DEV
    row = jnp.arange(capacity, dtype=jnp.int32)[:, None]
    col = jnp.arange(frame, dtype=jnp.int32)[None, :]
    shift = offset - device * T_DEV + HALF
    select = ((row + shift == col) & (row < count)).astype(jnp.bfloat16)
    placed = jnp.einsum(
        "pcr,rj->pcj", arrivals, select, preferred_element_type=jnp.float32
    ).astype(jnp.bfloat16)
    to_prev = placed[:, :, :HALF]
    to_next = placed[:, :, frame - HALF - 2 :]
    from_next = lax.ppermute(to_prev, "ctx", [(i + 1, i) for i in range(n_ctx - 1)])
    from_prev = lax.ppermute(to_next, "ctx", [(i, i + 1) for i in range(n_ctx - 1)])
    window = placed[:, :, HALF - 2 : HALF + T_DEV]
    window = window + jnp.pad(from_prev, ((0, 0), (0, 0), (0, T_DEV - HALF)))
    window = window + jnp.pad(from_next, ((0, 0), (0, 0), (T_DEV + 2 - HALF, 0)))
    wide = window.astype(jnp.float32)
    shorted = short_taps[:, 0, :, None] * wide[:, :, 2:]
    shorted = shorted + short_taps[:, 1, :, None] * wide[:, :, 1:-1]
    shorted = shorted + short_taps[:, 2, :, None] * wide[:, :, :-2]
    mixed_input = (shorted[1] * shorted[2]).astype(jnp.bfloat16)

    tap_blocks = jnp.stack(
        [jnp.zeros((channels, T_DEV), filter_taps.dtype)]
        + [filter_taps[:, k * T_DEV : (k + 1) * T_DEV] for k in range(n_blocks)]
    )
    every_input = lax.all_gather(mixed_input, "ctx", axis=0)
    backwards = jnp.concatenate(
        [jnp.flip(every_input, 0), jnp.zeros_like(every_input)], axis=0
    )
    start = n_ctx - 1 - device
    if n_blocks <= GROUP:
        x_blocks = lax.dynamic_slice_in_dim(backwards, start, n_blocks, 0)
        sums = products(transform(x_blocks, forward), kernel_spectra(tap_blocks, forward))
    else:
        width = max(w for w in range(1, GROUP + 1) if n_blocks % w == 0)

        def group(g, acc):
            k0 = g * width
            x_blocks = lax.dynamic_slice_in_dim(backwards, start + k0, width, 0)
            taps = lax.dynamic_slice_in_dim(tap_blocks, k0, width + 1, 0)
            part = products(transform(x_blocks, forward), kernel_spectra(taps, forward))
            return tuple(a + b for a, b in zip(acc, part))

        zero = jnp.zeros((channels, T_DEV), jnp.float32)
        sums = lax.fori_loop(0, n_blocks // width, group, (zero, zero, zero, zero))
    rr, ii, ri, ir = sums
    first = jnp.arange(T_DEV, dtype=jnp.int32)[None, :] == 0
    spec_re = jnp.where(first, rr, rr - ii)
    spec_im = jnp.where(first, ii, ri + ir)
    spectrum = jnp.concatenate([spec_re, spec_im], axis=1)
    conv_core = jnp.dot(spectrum, inverse, precision=lax.Precision.HIGHEST)
    conv = conv_core + skip_gain[:, None] * mixed_input.astype(jnp.float32)
    gated = (shorted[0] * conv).astype(jnp.bfloat16)
    mixed = jnp.dot(
        out_weight,
        lax.all_gather(gated, "ch", axis=0, tiled=True),
        preferred_element_type=jnp.float32,
    )
    return mixed.astype(jnp.bfloat16)


def sender_kernel(count_ref, arrivals_ref, taps_ref, out_ref, *, n_ctx, own):
    count = count_ref[0]
    capacity = arrivals_ref.shape[2]
    lane = lax.broadcasted_iota(jnp.int32, arrivals_ref.shape[1:], 1)
    row = lax.broadcasted_iota(jnp.int32, (capacity, EDGE), 0)
    column = lax.broadcasted_iota(jnp.int32, (capacity, EDGE), 1)
    square = lax.broadcasted_iota(jnp.int32, (lane.shape[0], lane.shape[0]), 0)
    diagonal = square == lax.broadcasted_iota(jnp.int32, square.shape, 1)

    def tap(part, k):
        spread = jnp.where(diagonal, taps_ref[part, k : k + 1, :], 0.0)
        return jnp.sum(spread, axis=1, keepdims=True)

    near = []
    edge = jnp.where(column[:1] == 8, (count // 16).astype(jnp.float32), 0.0)
    edge = jnp.where(column[:1] == 9, (count % 16).astype(jnp.float32), edge)
    for part in range(2):
        raw = arrivals_ref[1 + part]
        x = raw.astype(jnp.float32)
        back1 = jnp.where(lane >= 1, pltpu.roll(x, 1, 1), 0.0)
        back2 = jnp.where(lane >= 2, pltpu.roll(x, 2, 1), 0.0)
        s = tap(1 + part, 0) * x
        s = s + tap(1 + part, 1) * back1
        s = s + tap(1 + part, 2) * back2
        near.append(s)
        wanted = jnp.where(column >= 4, count - 2 + column - 4 - 2 * part, column - 2 * part)
        inside = (column % 4 >= 2 * part) & (column % 4 < 2 * part + 2) & (column < 8)
        pick = ((row == wanted) & inside).astype(jnp.bfloat16)
        edge = edge + jnp.dot(raw, pick, preferred_element_type=jnp.float32)
    mixed = (near[0] * near[1]).astype(jnp.bfloat16)
    edge = edge.astype(jnp.bfloat16)
    flat_lane = lax.broadcasted_iota(jnp.int32, (EDGE, capacity), 1)
    spread = (
        (flat_lane < 8 * own) & (flat_lane % 8 == lax.broadcasted_iota(jnp.int32, (EDGE, capacity), 0))
    ).astype(jnp.bfloat16)
    channel = lax.broadcasted_iota(jnp.int32, (own, capacity), 0)
    lane_out = lax.broadcasted_iota(jnp.int32, (own, capacity), 1)
    code = jnp.where(lane_out[:1] == 8 * own, (count // 16).astype(jnp.float32), 0.0)
    code = jnp.where(lane_out[:1] == 8 * own + 1, (count % 16).astype(jnp.float32), code)
    for j in range(n_ctx):
        rows = slice(j * own, (j + 1) * own)
        out_ref[j, :own, :] = arrivals_ref[0, rows, :]
        out_ref[j, own : 2 * own, :] = mixed[rows]
        tiled = jnp.dot(edge[rows], spread, preferred_element_type=jnp.float32)
        flat = jnp.sum(jnp.where(lane_out // 8 == channel, tiled, 0.0), axis=0, keepdims=True)
        out_ref[j, 2 * own : 2 * own + 1, :] = (flat + code).astype(jnp.bfloat16)


def by_transpose(arrivals, counts, short_taps, filter_taps, skip_gain, out_weight):
    n_ctx = lax.axis_size("ctx")
    device = lax.axis_index("ctx")
    channels = arrivals.shape[1]
    capacity = arrivals.shape[2]
    length = filter_taps.shape[1]
    n_blocks = length // T_DEV
    own = channels // n_ctx
    forward, inverse = dft_tables()

    payload = pl.pallas_call(
        functools.partial(sender_kernel, n_ctx=n_ctx, own=own),
        in_specs=[
            pl.BlockSpec(memory_space=pltpu.SMEM),
            pl.BlockSpec(memory_space=pltpu.VMEM),
            pl.BlockSpec(memory_space=pltpu.VMEM),
        ],
        out_specs=pl.BlockSpec(memory_space=pltpu.VMEM),
        out_shape=jax.ShapeDtypeStruct((n_ctx, 2 * own + 1, capacity), jnp.bfloat16),
    )(counts, arrivals, short_taps)
    got = lax.all_to_all(payload, "ctx", 0, 0, tiled=False)
    rows = got[:, : 2 * own]
    edge_in = got[:, 2 * own]
    every_count = (
        edge_in[:, own * 8].astype(jnp.int32) * 16 + edge_in[:, own * 8 + 1].astype(jnp.int32)
    )
    offsets = jnp.cumsum(every_count) - every_count

    frame = 2 * T_DEV
    row = jnp.arange(capacity, dtype=jnp.int32)[None, :, None]
    col = jnp.arange(frame, dtype=jnp.int32)[None, None, :]
    sampler = jnp.arange(n_ctx, dtype=jnp.int32)[:, None, None]
    shift = offsets[:, None, None] - (sampler - 1) * T_DEV - HALF
    select = ((row + shift == col) & (row < every_count[:, None, None])).astype(jnp.bfloat16)
    placed = jnp.einsum("icr,irj->icj", rows, select, preferred_element_type=jnp.bfloat16)
    full = sum(
        jnp.pad(placed[i], ((0, 0), (i * T_DEV + HALF, (n_ctx - i) * T_DEV - HALF)))
        for i in range(n_ctx)
    )
    first = device * own
    taps = lax.dynamic_slice_in_dim(short_taps, first, own, 2)
    gate = full[:own, T_DEV - 2 : T_DEV + length].astype(jnp.float32)
    shorted_gate = taps[0, 0, :, None] * gate[:, 2:]
    shorted_gate = shorted_gate + taps[0, 1, :, None] * gate[:, 1:-1]
    shorted_gate = shorted_gate + taps[0, 2, :, None] * gate[:, :-2]
    from_senders = full[own:, T_DEV : T_DEV + length]

    values = edge_in[:, : own * 8].reshape(n_ctx, own, 8)
    count_col = every_count[:, None]
    at_row = jnp.concatenate(
        [jnp.zeros_like(count_col), jnp.ones_like(count_col), count_col - 2, count_col - 1], axis=1
    )
    valid = jnp.concatenate([at_row[:, :2] < count_col, at_row[:, 2:] >= 2], axis=1)
    spot = offsets[:, None] + at_row
    slot = jnp.arange(length + 2, dtype=jnp.int32)[None, None, :]
    marks = (slot - 2 == spot[:, :, None]) & valid[:, :, None]
    slots = np.arange(8)
    spot8 = jnp.concatenate([spot[:, :2], spot[:, :2], spot[:, 2:], spot[:, 2:]], axis=1)
    valid8 = jnp.concatenate([valid[:, :2], valid[:, :2], valid[:, 2:], valid[:, 2:]], axis=1)
    by_slot = (slot - 2 == spot8[:, :, None]) & valid8[:, :, None]
    belongs = jnp.asarray((slots // 2) % 2 == np.arange(2)[:, None])
    spread = (by_slot[:, :, None, :] & belongs.T[None, :, :, None]).astype(jnp.bfloat16)
    around = jnp.einsum("ics,ispj->pcj", values, spread, preferred_element_type=jnp.float32)
    near_in = []
    for part in range(2):
        s = taps[1 + part, 0, :, None] * around[part, :, 2:]
        s = s + taps[1 + part, 1, :, None] * around[part, :, 1:-1]
        s = s + taps[1 + part, 2, :, None] * around[part, :, :-2]
        near_in.append(s)
    at_start = jnp.any(marks[:, :2, 2:], axis=(0, 1))
    mixed_input = jnp.where(
        at_start[None, :], (near_in[0] * near_in[1]).astype(jnp.bfloat16), from_senders
    )

    x_spec = transform(mixed_input.reshape(own, n_blocks, T_DEV), forward, "cnt,tf->cnf")
    own_taps = lax.dynamic_slice_in_dim(filter_taps, first, own, 0)
    tap_blocks = jnp.concatenate(
        [jnp.zeros((own, T_DEV), own_taps.dtype), own_taps], axis=1
    ).reshape(own, n_blocks + 1, T_DEV)
    h_spec = transform(tap_blocks, forward, "cnt,tf->cnf")
    column = jnp.arange(PERIOD, dtype=jnp.int32) % T_DEV
    signs = jnp.where(column % 2 == 0, 1.0, -1.0).astype(jnp.float32)
    g_spec = h_spec[:, 1:] + signs * h_spec[:, :-1]
    xr, xi = x_spec[..., :T_DEV], x_spec[..., T_DEV:]
    gr, gi = g_spec[..., :T_DEV], g_spec[..., T_DEV:]
    sums = [jnp.zeros((own, n_blocks, T_DEV), jnp.float32) for _ in range(4)]
    for k in range(n_blocks):
        pad = ((0, 0), (k, 0), (0, 0))
        terms = (
            xr[:, : n_blocks - k] * gr[:, k : k + 1],
            xi[:, : n_blocks - k] * gi[:, k : k + 1],
            xr[:, : n_blocks - k] * gi[:, k : k + 1],
            xi[:, : n_blocks - k] * gr[:, k : k + 1],
        )
        sums = [s + jnp.pad(t, pad) for s, t in zip(sums, terms)]
    rr, ii, ri, ir = sums
    at_zero = jnp.arange(T_DEV, dtype=jnp.int32)[None, None, :] == 0
    spectrum = jnp.concatenate(
        [jnp.where(at_zero, rr, rr - ii), jnp.where(at_zero, ii, ri + ir)], axis=2
    )
    conv_core = jnp.einsum("cnf,ft->cnt", spectrum, inverse, precision=lax.Precision.HIGHEST)
    gains = lax.dynamic_slice_in_dim(skip_gain, first, own, 0)
    conv = conv_core.reshape(own, length) + gains[:, None] * mixed_input.astype(jnp.float32)
    gated = (shorted_gate * conv).astype(jnp.bfloat16)
    back = lax.all_to_all(gated.reshape(own, n_ctx, T_DEV), "ctx", 1, 0, tiled=False)
    gated_block = back.reshape(channels, T_DEV)
    mixed = jnp.dot(
        out_weight,
        lax.all_gather(gated_block, "ch", axis=0, tiled=True),
        preferred_element_type=jnp.float32,
    )
    return with_layout_constraint(mixed.astype(jnp.bfloat16), Layout((0, 1)))


def on_device(arrivals, counts, short_taps, filter_taps, skip_gain, out_weight):
    n_ctx = lax.axis_size("ctx")
    blocks = filter_taps.shape[1] // T_DEV
    if arrivals.shape[1] % n_ctx == 0 and blocks == n_ctx:
        return by_transpose(arrivals, counts, short_taps, filter_taps, skip_gain, out_weight)
    return by_gather(arrivals, counts, short_taps, filter_taps, skip_gain, out_weight)


def solution(mesh):
    return jax.shard_map(
        on_device,
        mesh=mesh,
        in_specs=(
            P(None, "ch", "ctx"),
            P("ctx"),
            P(None, None, "ch"),
            P("ch", None),
            P("ch"),
            P("ch", None),
        ),
        out_specs=P("ch", "ctx"),
        check_vma=False,
    )
```

```python
import functools
import math

import jax
import jax.numpy as jnp
import ml_dtypes
import numpy as np
from jax import lax
from jax.experimental.layout import Layout, with_layout_constraint
from jax.experimental import pallas as pl
from jax.experimental.pallas import tpu as pltpu
from jax.sharding import PartitionSpec as P

T_DEV = 256
HALF = T_DEV // 2
PERIOD = 2 * T_DEV
GROUP = 8
EDGE = 128


def split_bf16(table):
    hi = table.astype(ml_dtypes.bfloat16)
    lo = (table - hi.astype(np.float64)).astype(ml_dtypes.bfloat16)
    return jnp.asarray(hi), jnp.asarray(lo)


def dft_tables():
    t = np.arange(T_DEV)[:, None]
    f = np.arange(T_DEV)[None, :]
    angle = 2.0 * np.pi * ((t * f) % PERIOD) / PERIOD
    forward = np.concatenate([np.cos(angle), -np.sin(angle)], axis=1)
    forward[:, T_DEV] = np.where(np.arange(T_DEV) % 2 == 0, 1.0, -1.0)
    fr = np.arange(T_DEV)[:, None]
    n = np.arange(T_DEV)[None, :]
    angle = 2.0 * np.pi * ((fr * n) % PERIOD) / PERIOD
    inv_re = 2.0 * np.cos(angle) / PERIOD
    inv_re[0, :] = 1.0 / PERIOD
    inv_im = -2.0 * np.sin(angle) / PERIOD
    inv_im[0, :] = np.where(np.arange(T_DEV) % 2 == 0, 1.0, -1.0) / PERIOD
    inverse = np.concatenate([inv_re, inv_im], axis=0).astype(np.float32)
    return split_bf16(forward), jnp.asarray(inverse)


def transform(blocks, forward, spec="kct,tf->kcf"):
    hi, lo = forward
    return jnp.einsum(spec, blocks, hi, preferred_element_type=jnp.float32) + jnp.einsum(
        spec, blocks, lo, preferred_element_type=jnp.float32
    )


def kernel_spectra(tap_blocks, forward):
    spectra = transform(tap_blocks, forward)
    column = jnp.arange(PERIOD, dtype=jnp.int32) % T_DEV
    signs = jnp.where(column % 2 == 0, 1.0, -1.0).astype(jnp.float32)
    return spectra[1:] + signs * spectra[:-1]


def products(x_spec, g_spec):
    xr, xi = x_spec[..., :T_DEV], x_spec[..., T_DEV:]
    gr, gi = g_spec[..., :T_DEV], g_spec[..., T_DEV:]
    return (
        jnp.sum(xr * gr, axis=0),
        jnp.sum(xi * gi, axis=0),
        jnp.sum(xr * gi, axis=0),
        jnp.sum(xi * gr, axis=0),
    )


def by_gather(arrivals, counts, short_taps, filter_taps, skip_gain, out_weight):
    n_ctx = lax.axis_size("ctx")
    device = lax.axis_index("ctx")
    channels = arrivals.shape[1]
    capacity = arrivals.shape[2]
    n_blocks = filter_taps.shape[1] // T_DEV
    forward, inverse = dft_tables()

    every_count = lax.all_gather(counts, "ctx", axis=0, tiled=True)
    earlier = jnp.arange(n_ctx, dtype=jnp.int32) < device
    offset = jnp.sum(jnp.where(earlier, every_count, 0))
    count = counts[0]

    frame = 2 * T_DEV
    row = jnp.arange(capacity, dtype=jnp.int32)[:, None]
    col = jnp.arange(frame, dtype=jnp.int32)[None, :]
    shift = offset - device * T_DEV + HALF
    select = ((row + shift == col) & (row < count)).astype(jnp.bfloat16)
    placed = jnp.einsum(
        "pcr,rj->pcj", arrivals, select, preferred_element_type=jnp.float32
    ).astype(jnp.bfloat16)
    to_prev = placed[:, :, :HALF]
    to_next = placed[:, :, frame - HALF - 2 :]
    from_next = lax.ppermute(to_prev, "ctx", [(i + 1, i) for i in range(n_ctx - 1)])
    from_prev = lax.ppermute(to_next, "ctx", [(i, i + 1) for i in range(n_ctx - 1)])
    window = placed[:, :, HALF - 2 : HALF + T_DEV]
    window = window + jnp.pad(from_prev, ((0, 0), (0, 0), (0, T_DEV - HALF)))
    window = window + jnp.pad(from_next, ((0, 0), (0, 0), (T_DEV + 2 - HALF, 0)))
    wide = window.astype(jnp.float32)
    shorted = short_taps[:, 0, :, None] * wide[:, :, 2:]
    shorted = shorted + short_taps[:, 1, :, None] * wide[:, :, 1:-1]
    shorted = shorted + short_taps[:, 2, :, None] * wide[:, :, :-2]
    mixed_input = (shorted[1] * shorted[2]).astype(jnp.bfloat16)

    tap_blocks = jnp.stack(
        [jnp.zeros((channels, T_DEV), filter_taps.dtype)]
        + [filter_taps[:, k * T_DEV : (k + 1) * T_DEV] for k in range(n_blocks)]
    )
    every_input = lax.all_gather(mixed_input, "ctx", axis=0)
    backwards = jnp.concatenate(
        [jnp.flip(every_input, 0), jnp.zeros_like(every_input)], axis=0
    )
    start = n_ctx - 1 - device
    if n_blocks <= GROUP:
        x_blocks = lax.dynamic_slice_in_dim(backwards, start, n_blocks, 0)
        sums = products(transform(x_blocks, forward), kernel_spectra(tap_blocks, forward))
    else:
        width = max(w for w in range(1, GROUP + 1) if n_blocks % w == 0)

        def group(g, acc):
            k0 = g * width
            x_blocks = lax.dynamic_slice_in_dim(backwards, start + k0, width, 0)
            taps = lax.dynamic_slice_in_dim(tap_blocks, k0, width + 1, 0)
            part = products(transform(x_blocks, forward), kernel_spectra(taps, forward))
            return tuple(a + b for a, b in zip(acc, part))

        zero = jnp.zeros((channels, T_DEV), jnp.float32)
        sums = lax.fori_loop(0, n_blocks // width, group, (zero, zero, zero, zero))
    rr, ii, ri, ir = sums
    first = jnp.arange(T_DEV, dtype=jnp.int32)[None, :] == 0
    spec_re = jnp.where(first, rr, rr - ii)
    spec_im = jnp.where(first, ii, ri + ir)
    spectrum = jnp.concatenate([spec_re, spec_im], axis=1)
    conv_core = jnp.dot(spectrum, inverse, precision=lax.Precision.HIGHEST)
    conv = conv_core + skip_gain[:, None] * mixed_input.astype(jnp.float32)
    gated = (shorted[0] * conv).astype(jnp.bfloat16)
    mixed = jnp.dot(
        out_weight,
        lax.all_gather(gated, "ch", axis=0, tiled=True),
        preferred_element_type=jnp.float32,
    )
    return mixed.astype(jnp.bfloat16)


def sender_kernel(count_ref, arrivals_ref, taps_ref, out_ref, *, n_ctx, own):
    count = count_ref[0]
    capacity = arrivals_ref.shape[2]
    lane = lax.broadcasted_iota(jnp.int32, arrivals_ref.shape[1:], 1)
    row = lax.broadcasted_iota(jnp.int32, (capacity, EDGE), 0)
    column = lax.broadcasted_iota(jnp.int32, (capacity, EDGE), 1)
    square = lax.broadcasted_iota(jnp.int32, (lane.shape[0], lane.shape[0]), 0)
    diagonal = square == lax.broadcasted_iota(jnp.int32, square.shape, 1)

    def tap(part, k):
        spread = jnp.where(diagonal, taps_ref[part, k : k + 1, :], 0.0)
        return jnp.sum(spread, axis=1, keepdims=True)

    edge = jnp.where(column[:1] == 8, (count // 16).astype(jnp.float32), 0.0)
    edge = jnp.where(column[:1] == 9, (count % 16).astype(jnp.float32), edge)
    columns = []
    for part in range(2):
        wanted = jnp.where(column >= 4, count - 2 + column - 4 - 2 * part, column - 2 * part)
        inside = (column % 4 >= 2 * part) & (column % 4 < 2 * part + 2) & (column < 8)
        pick = ((row == wanted) & inside).astype(jnp.bfloat16)
        edge = edge + jnp.dot(arrivals_ref[1 + part], pick, preferred_element_type=jnp.float32)
        columns.append([tap(1 + part, k) for k in range(3)])
    edge = edge.astype(jnp.bfloat16)
    block_lane = lane[:own]
    for j in range(n_ctx):
        rows = slice(j * own, (j + 1) * own)
        near = []
        for part in range(2):
            x = arrivals_ref[1 + part, rows, :].astype(jnp.float32)
            back1 = jnp.where(block_lane >= 1, pltpu.roll(x, 1, 1), 0.0)
            back2 = jnp.where(block_lane >= 2, pltpu.roll(x, 2, 1), 0.0)
            s = columns[part][0][rows] * x
            s = s + columns[part][1][rows] * back1
            s = s + columns[part][2][rows] * back2
            near.append(s)
        out_ref[j, own : 2 * own, :] = (near[0] * near[1]).astype(jnp.bfloat16)
    flat_lane = lax.broadcasted_iota(jnp.int32, (EDGE, capacity), 1)
    spread = (
        (flat_lane < 8 * own) & (flat_lane % 8 == lax.broadcasted_iota(jnp.int32, (EDGE, capacity), 0))
    ).astype(jnp.bfloat16)
    channel = lax.broadcasted_iota(jnp.int32, (own, capacity), 0)
    lane_out = lax.broadcasted_iota(jnp.int32, (own, capacity), 1)
    code = jnp.where(lane_out[:1] == 8 * own, (count // 16).astype(jnp.float32), 0.0)
    code = jnp.where(lane_out[:1] == 8 * own + 1, (count % 16).astype(jnp.float32), code)
    for j in range(n_ctx):
        rows = slice(j * own, (j + 1) * own)
        out_ref[j, :own, :] = arrivals_ref[0, rows, :]
        tiled = jnp.dot(edge[rows], spread, preferred_element_type=jnp.float32)
        flat = jnp.sum(jnp.where(lane_out // 8 == channel, tiled, 0.0), axis=0, keepdims=True)
        out_ref[j, 2 * own : 2 * own + 1, :] = (flat + code).astype(jnp.bfloat16)


def by_transpose(arrivals, counts, short_taps, filter_taps, skip_gain, out_weight):
    n_ctx = lax.axis_size("ctx")
    device = lax.axis_index("ctx")
    channels = arrivals.shape[1]
    capacity = arrivals.shape[2]
    length = filter_taps.shape[1]
    n_blocks = length // T_DEV
    own = channels // n_ctx
    forward, inverse = dft_tables()

    payload = pl.pallas_call(
        functools.partial(sender_kernel, n_ctx=n_ctx, own=own),
        in_specs=[
            pl.BlockSpec(memory_space=pltpu.SMEM),
            pl.BlockSpec(memory_space=pltpu.VMEM),
            pl.BlockSpec(memory_space=pltpu.VMEM),
        ],
        out_specs=pl.BlockSpec(memory_space=pltpu.VMEM),
        out_shape=jax.ShapeDtypeStruct((n_ctx, 2 * own + 1, capacity), jnp.bfloat16),
    )(counts, arrivals, short_taps)
    got = lax.all_to_all(payload, "ctx", 0, 0, tiled=False)
    rows = got[:, : 2 * own]
    edge_in = got[:, 2 * own]
    every_count = (
        edge_in[:, own * 8].astype(jnp.int32) * 16 + edge_in[:, own * 8 + 1].astype(jnp.int32)
    )
    offsets = jnp.cumsum(every_count) - every_count

    frame = 2 * T_DEV
    row = jnp.arange(capacity, dtype=jnp.int32)[None, :, None]
    col = jnp.arange(frame, dtype=jnp.int32)[None, None, :]
    sampler = jnp.arange(n_ctx, dtype=jnp.int32)[:, None, None]
    shift = offsets[:, None, None] - (sampler - 1) * T_DEV - HALF
    select = ((row + shift == col) & (row < every_count[:, None, None])).astype(jnp.bfloat16)
    placed = jnp.einsum("icr,irj->icj", rows, select, preferred_element_type=jnp.bfloat16)
    full = sum(
        jnp.pad(placed[i], ((0, 0), (i * T_DEV + HALF, (n_ctx - i) * T_DEV - HALF)))
        for i in range(n_ctx)
    )
    first = device * own
    taps = lax.dynamic_slice_in_dim(short_taps, first, own, 2)
    gate = full[:own, T_DEV - 2 : T_DEV + length].astype(jnp.float32)
    shorted_gate = taps[0, 0, :, None] * gate[:, 2:]
    shorted_gate = shorted_gate + taps[0, 1, :, None] * gate[:, 1:-1]
    shorted_gate = shorted_gate + taps[0, 2, :, None] * gate[:, :-2]
    from_senders = full[own:, T_DEV : T_DEV + length]

    values = edge_in[:, : own * 8].reshape(n_ctx, own, 8)
    count_col = every_count[:, None]
    at_row = jnp.concatenate(
        [jnp.zeros_like(count_col), jnp.ones_like(count_col), count_col - 2, count_col - 1], axis=1
    )
    valid = jnp.concatenate([at_row[:, :2] < count_col, at_row[:, 2:] >= 2], axis=1)
    spot = offsets[:, None] + at_row
    slot = jnp.arange(length + 2, dtype=jnp.int32)[None, None, :]
    marks = (slot - 2 == spot[:, :, None]) & valid[:, :, None]
    slots = np.arange(8)
    spot8 = jnp.concatenate([spot[:, :2], spot[:, :2], spot[:, 2:], spot[:, 2:]], axis=1)
    valid8 = jnp.concatenate([valid[:, :2], valid[:, :2], valid[:, 2:], valid[:, 2:]], axis=1)
    by_slot = (slot - 2 == spot8[:, :, None]) & valid8[:, :, None]
    belongs = jnp.asarray((slots // 2) % 2 == np.arange(2)[:, None])
    spread = (by_slot[:, :, None, :] & belongs.T[None, :, :, None]).astype(jnp.bfloat16)
    around = jnp.einsum("ics,ispj->pcj", values, spread, preferred_element_type=jnp.float32)
    near_in = []
    for part in range(2):
        s = taps[1 + part, 0, :, None] * around[part, :, 2:]
        s = s + taps[1 + part, 1, :, None] * around[part, :, 1:-1]
        s = s + taps[1 + part, 2, :, None] * around[part, :, :-2]
        near_in.append(s)
    at_start = jnp.any(marks[:, :2, 2:], axis=(0, 1))
    mixed_input = jnp.where(
        at_start[None, :], (near_in[0] * near_in[1]).astype(jnp.bfloat16), from_senders
    )

    x_spec = transform(mixed_input.reshape(own, n_blocks, T_DEV), forward, "cnt,tf->cnf")
    own_taps = lax.dynamic_slice_in_dim(filter_taps, first, own, 0)
    tap_blocks = jnp.concatenate(
        [jnp.zeros((own, T_DEV), own_taps.dtype), own_taps], axis=1
    ).reshape(own, n_blocks + 1, T_DEV)
    h_spec = transform(tap_blocks, forward, "cnt,tf->cnf")
    column = jnp.arange(PERIOD, dtype=jnp.int32) % T_DEV
    signs = jnp.where(column % 2 == 0, 1.0, -1.0).astype(jnp.float32)
    g_spec = h_spec[:, 1:] + signs * h_spec[:, :-1]
    xr, xi = x_spec[..., :T_DEV], x_spec[..., T_DEV:]
    gr, gi = g_spec[..., :T_DEV], g_spec[..., T_DEV:]
    sums = [jnp.zeros((own, n_blocks, T_DEV), jnp.float32) for _ in range(4)]
    for k in range(n_blocks):
        pad = ((0, 0), (k, 0), (0, 0))
        terms = (
            xr[:, : n_blocks - k] * gr[:, k : k + 1],
            xi[:, : n_blocks - k] * gi[:, k : k + 1],
            xr[:, : n_blocks - k] * gi[:, k : k + 1],
            xi[:, : n_blocks - k] * gr[:, k : k + 1],
        )
        sums = [s + jnp.pad(t, pad) for s, t in zip(sums, terms)]
    rr, ii, ri, ir = sums
    at_zero = jnp.arange(T_DEV, dtype=jnp.int32)[None, None, :] == 0
    spectrum = jnp.concatenate(
        [jnp.where(at_zero, rr, rr - ii), jnp.where(at_zero, ii, ri + ir)], axis=2
    )
    conv_core = jnp.einsum("cnf,ft->cnt", spectrum, inverse, precision=lax.Precision.HIGHEST)
    gains = lax.dynamic_slice_in_dim(skip_gain, first, own, 0)
    conv = conv_core.reshape(own, length) + gains[:, None] * mixed_input.astype(jnp.float32)
    gated = (shorted_gate * conv).astype(jnp.bfloat16)
    back = lax.all_to_all(gated.reshape(own, n_ctx, T_DEV), "ctx", 1, 0, tiled=False)
    gated_block = back.reshape(channels, T_DEV)
    mixed = jnp.dot(
        out_weight,
        lax.all_gather(gated_block, "ch", axis=0, tiled=True),
        preferred_element_type=jnp.float32,
    )
    return with_layout_constraint(mixed.astype(jnp.bfloat16), Layout((0, 1)))


def on_device(arrivals, counts, short_taps, filter_taps, skip_gain, out_weight):
    n_ctx = lax.axis_size("ctx")
    blocks = filter_taps.shape[1] // T_DEV
    if arrivals.shape[1] % n_ctx == 0 and blocks == n_ctx:
        return by_transpose(arrivals, counts, short_taps, filter_taps, skip_gain, out_weight)
    return by_gather(arrivals, counts, short_taps, filter_taps, skip_gain, out_weight)


def solution(mesh):
    return jax.shard_map(
        on_device,
        mesh=mesh,
        in_specs=(
            P(None, "ch", "ctx"),
            P("ctx"),
            P(None, None, "ch"),
            P("ch", None),
            P("ch"),
            P("ch", None),
        ),
        out_specs=P("ch", "ctx"),
        check_vma=False,
    )
```

```python
import functools
import math

import jax
import jax.numpy as jnp
import ml_dtypes
import numpy as np
from jax import lax
from jax.experimental.layout import Layout, with_layout_constraint
from jax.experimental import pallas as pl
from jax.experimental.pallas import tpu as pltpu
from jax.sharding import PartitionSpec as P

T_DEV = 256
HALF = T_DEV // 2
PERIOD = 2 * T_DEV
GROUP = 8
EDGE = 128


def split_bf16(table):
    hi = table.astype(ml_dtypes.bfloat16)
    lo = (table - hi.astype(np.float64)).astype(ml_dtypes.bfloat16)
    return jnp.asarray(hi), jnp.asarray(lo)


def dft_tables():
    t = np.arange(T_DEV)[:, None]
    f = np.arange(T_DEV)[None, :]
    angle = 2.0 * np.pi * ((t * f) % PERIOD) / PERIOD
    forward = np.concatenate([np.cos(angle), -np.sin(angle)], axis=1)
    forward[:, T_DEV] = np.where(np.arange(T_DEV) % 2 == 0, 1.0, -1.0)
    fr = np.arange(T_DEV)[:, None]
    n = np.arange(T_DEV)[None, :]
    angle = 2.0 * np.pi * ((fr * n) % PERIOD) / PERIOD
    inv_re = 2.0 * np.cos(angle) / PERIOD
    inv_re[0, :] = 1.0 / PERIOD
    inv_im = -2.0 * np.sin(angle) / PERIOD
    inv_im[0, :] = np.where(np.arange(T_DEV) % 2 == 0, 1.0, -1.0) / PERIOD
    inverse = np.concatenate([inv_re, inv_im], axis=0).astype(np.float32)
    return split_bf16(forward), jnp.asarray(inverse)


def transform(blocks, forward, spec="kct,tf->kcf"):
    hi, lo = forward
    return jnp.einsum(spec, blocks, hi, preferred_element_type=jnp.float32) + jnp.einsum(
        spec, blocks, lo, preferred_element_type=jnp.float32
    )


def kernel_spectra(tap_blocks, forward):
    spectra = transform(tap_blocks, forward)
    column = jnp.arange(PERIOD, dtype=jnp.int32) % T_DEV
    signs = jnp.where(column % 2 == 0, 1.0, -1.0).astype(jnp.float32)
    return spectra[1:] + signs * spectra[:-1]


def products(x_spec, g_spec):
    xr, xi = x_spec[..., :T_DEV], x_spec[..., T_DEV:]
    gr, gi = g_spec[..., :T_DEV], g_spec[..., T_DEV:]
    return (
        jnp.sum(xr * gr, axis=0),
        jnp.sum(xi * gi, axis=0),
        jnp.sum(xr * gi, axis=0),
        jnp.sum(xi * gr, axis=0),
    )


def by_gather(arrivals, counts, short_taps, filter_taps, skip_gain, out_weight):
    n_ctx = lax.axis_size("ctx")
    device = lax.axis_index("ctx")
    channels = arrivals.shape[1]
    capacity = arrivals.shape[2]
    n_blocks = filter_taps.shape[1] // T_DEV
    forward, inverse = dft_tables()

    every_count = lax.all_gather(counts, "ctx", axis=0, tiled=True)
    earlier = jnp.arange(n_ctx, dtype=jnp.int32) < device
    offset = jnp.sum(jnp.where(earlier, every_count, 0))
    count = counts[0]

    frame = 2 * T_DEV
    row = jnp.arange(capacity, dtype=jnp.int32)[:, None]
    col = jnp.arange(frame, dtype=jnp.int32)[None, :]
    shift = offset - device * T_DEV + HALF
    select = ((row + shift == col) & (row < count)).astype(jnp.bfloat16)
    placed = jnp.einsum(
        "pcr,rj->pcj", arrivals, select, preferred_element_type=jnp.float32
    ).astype(jnp.bfloat16)
    to_prev = placed[:, :, :HALF]
    to_next = placed[:, :, frame - HALF - 2 :]
    from_next = lax.ppermute(to_prev, "ctx", [(i + 1, i) for i in range(n_ctx - 1)])
    from_prev = lax.ppermute(to_next, "ctx", [(i, i + 1) for i in range(n_ctx - 1)])
    window = placed[:, :, HALF - 2 : HALF + T_DEV]
    window = window + jnp.pad(from_prev, ((0, 0), (0, 0), (0, T_DEV - HALF)))
    window = window + jnp.pad(from_next, ((0, 0), (0, 0), (T_DEV + 2 - HALF, 0)))
    wide = window.astype(jnp.float32)
    shorted = short_taps[:, 0, :, None] * wide[:, :, 2:]
    shorted = shorted + short_taps[:, 1, :, None] * wide[:, :, 1:-1]
    shorted = shorted + short_taps[:, 2, :, None] * wide[:, :, :-2]
    mixed_input = (shorted[1] * shorted[2]).astype(jnp.bfloat16)

    tap_blocks = jnp.stack(
        [jnp.zeros((channels, T_DEV), filter_taps.dtype)]
        + [filter_taps[:, k * T_DEV : (k + 1) * T_DEV] for k in range(n_blocks)]
    )
    every_input = lax.all_gather(mixed_input, "ctx", axis=0)
    backwards = jnp.concatenate(
        [jnp.flip(every_input, 0), jnp.zeros_like(every_input)], axis=0
    )
    start = n_ctx - 1 - device
    if n_blocks <= GROUP:
        x_blocks = lax.dynamic_slice_in_dim(backwards, start, n_blocks, 0)
        sums = products(transform(x_blocks, forward), kernel_spectra(tap_blocks, forward))
    else:
        width = max(w for w in range(1, GROUP + 1) if n_blocks % w == 0)

        def group(g, acc):
            k0 = g * width
            x_blocks = lax.dynamic_slice_in_dim(backwards, start + k0, width, 0)
            taps = lax.dynamic_slice_in_dim(tap_blocks, k0, width + 1, 0)
            part = products(transform(x_blocks, forward), kernel_spectra(taps, forward))
            return tuple(a + b for a, b in zip(acc, part))

        zero = jnp.zeros((channels, T_DEV), jnp.float32)
        sums = lax.fori_loop(0, n_blocks // width, group, (zero, zero, zero, zero))
    rr, ii, ri, ir = sums
    first = jnp.arange(T_DEV, dtype=jnp.int32)[None, :] == 0
    spec_re = jnp.where(first, rr, rr - ii)
    spec_im = jnp.where(first, ii, ri + ir)
    spectrum = jnp.concatenate([spec_re, spec_im], axis=1)
    conv_core = jnp.dot(spectrum, inverse, precision=lax.Precision.HIGHEST)
    conv = conv_core + skip_gain[:, None] * mixed_input.astype(jnp.float32)
    gated = (shorted[0] * conv).astype(jnp.bfloat16)
    mixed = jnp.dot(
        out_weight,
        lax.all_gather(gated, "ch", axis=0, tiled=True),
        preferred_element_type=jnp.float32,
    )
    return mixed.astype(jnp.bfloat16)


def sender_kernel(count_ref, arrivals_ref, taps_ref, out_ref, *, n_ctx, own):
    count = count_ref[0]
    capacity = arrivals_ref.shape[2]
    row = lax.broadcasted_iota(jnp.int32, (capacity, EDGE), 0)
    column = lax.broadcasted_iota(jnp.int32, (capacity, EDGE), 1)
    channels = arrivals_ref.shape[1]
    square = lax.broadcasted_iota(jnp.int32, (channels, channels), 0)
    diagonal = square == lax.broadcasted_iota(jnp.int32, square.shape, 1)

    def tap(part, k):
        spread = jnp.where(diagonal, taps_ref[part, k : k + 1, :], 0.0)
        return jnp.sum(spread, axis=1, keepdims=True)

    edge = jnp.where(column[:1] == 8, (count // 16).astype(jnp.float32), 0.0)
    edge = jnp.where(column[:1] == 9, (count % 16).astype(jnp.float32), edge)
    columns = []
    for part in range(2):
        wanted = jnp.where(column >= 4, count - 2 + column - 4 - 2 * part, column - 2 * part)
        inside = (column % 4 >= 2 * part) & (column % 4 < 2 * part + 2) & (column < 8)
        pick = ((row == wanted) & inside).astype(jnp.bfloat16)
        edge = edge + jnp.dot(arrivals_ref[1 + part], pick, preferred_element_type=jnp.float32)
        columns.append([tap(1 + part, k) for k in range(3)])
    edge = edge.astype(jnp.bfloat16)
    block_lane = lax.broadcasted_iota(jnp.int32, (own, capacity), 1)
    for j in range(n_ctx):
        rows = slice(j * own, (j + 1) * own)
        near = []
        for part in range(2):
            x = arrivals_ref[1 + part, rows, :].astype(jnp.float32)
            back1 = jnp.where(block_lane >= 1, pltpu.roll(x, 1, 1), 0.0)
            back2 = jnp.where(block_lane >= 2, pltpu.roll(x, 2, 1), 0.0)
            s = columns[part][0][rows] * x
            s = s + columns[part][1][rows] * back1
            s = s + columns[part][2][rows] * back2
            near.append(s)
        out_ref[j, own : 2 * own, :] = (near[0] * near[1]).astype(jnp.bfloat16)
    flat_lane = lax.broadcasted_iota(jnp.int32, (EDGE, capacity), 1)
    spread = (
        (flat_lane < 8 * own) & (flat_lane % 8 == lax.broadcasted_iota(jnp.int32, (EDGE, capacity), 0))
    ).astype(jnp.bfloat16)
    channel = lax.broadcasted_iota(jnp.int32, (own, capacity), 0)
    lane_out = lax.broadcasted_iota(jnp.int32, (own, capacity), 1)
    code = jnp.where(lane_out[:1] == 8 * own, (count // 16).astype(jnp.float32), 0.0)
    code = jnp.where(lane_out[:1] == 8 * own + 1, (count % 16).astype(jnp.float32), code)
    tiled_all = jnp.dot(edge, spread, preferred_element_type=jnp.float32)
    for j in range(n_ctx):
        rows = slice(j * own, (j + 1) * own)
        out_ref[j, :own, :] = arrivals_ref[0, rows, :]
        tiled = tiled_all[rows]
        flat = jnp.sum(jnp.where(lane_out // 8 == channel, tiled, 0.0), axis=0, keepdims=True)
        out_ref[j, 2 * own : 2 * own + 1, :] = (flat + code).astype(jnp.bfloat16)


def by_transpose(arrivals, counts, short_taps, filter_taps, skip_gain, out_weight):
    n_ctx = lax.axis_size("ctx")
    device = lax.axis_index("ctx")
    channels = arrivals.shape[1]
    capacity = arrivals.shape[2]
    length = filter_taps.shape[1]
    n_blocks = length // T_DEV
    own = channels // n_ctx
    forward, inverse = dft_tables()

    payload = pl.pallas_call(
        functools.partial(sender_kernel, n_ctx=n_ctx, own=own),
        in_specs=[
            pl.BlockSpec(memory_space=pltpu.SMEM),
            pl.BlockSpec(memory_space=pltpu.VMEM),
            pl.BlockSpec(memory_space=pltpu.VMEM),
        ],
        out_specs=pl.BlockSpec(memory_space=pltpu.VMEM),
        out_shape=jax.ShapeDtypeStruct((n_ctx, 2 * own + 1, capacity), jnp.bfloat16),
    )(counts, arrivals, short_taps)
    got = lax.all_to_all(payload, "ctx", 0, 0, tiled=False)
    rows = got[:, : 2 * own]
    edge_in = got[:, 2 * own]
    every_count = (
        edge_in[:, own * 8].astype(jnp.int32) * 16 + edge_in[:, own * 8 + 1].astype(jnp.int32)
    )
    offsets = jnp.cumsum(every_count) - every_count

    frame = 2 * T_DEV
    row = jnp.arange(capacity, dtype=jnp.int32)[None, :, None]
    col = jnp.arange(frame, dtype=jnp.int32)[None, None, :]
    sampler = jnp.arange(n_ctx, dtype=jnp.int32)[:, None, None]
    shift = offsets[:, None, None] - (sampler - 1) * T_DEV - HALF
    select = ((row + shift == col) & (row < every_count[:, None, None])).astype(jnp.bfloat16)
    placed = jnp.einsum("icr,irj->icj", rows, select, preferred_element_type=jnp.bfloat16)
    full = sum(
        jnp.pad(placed[i], ((0, 0), (i * T_DEV + HALF, (n_ctx - i) * T_DEV - HALF)))
        for i in range(n_ctx)
    )
    first = device * own
    taps = lax.dynamic_slice_in_dim(short_taps, first, own, 2)
    gate = full[:own, T_DEV - 2 : T_DEV + length].astype(jnp.float32)
    shorted_gate = taps[0, 0, :, None] * gate[:, 2:]
    shorted_gate = shorted_gate + taps[0, 1, :, None] * gate[:, 1:-1]
    shorted_gate = shorted_gate + taps[0, 2, :, None] * gate[:, :-2]
    from_senders = full[own:, T_DEV : T_DEV + length]

    values = edge_in[:, : own * 8].reshape(n_ctx, own, 8)
    count_col = every_count[:, None]
    at_row = jnp.concatenate(
        [jnp.zeros_like(count_col), jnp.ones_like(count_col), count_col - 2, count_col - 1], axis=1
    )
    valid = jnp.concatenate([at_row[:, :2] < count_col, at_row[:, 2:] >= 2], axis=1)
    spot = offsets[:, None] + at_row
    slot = jnp.arange(length + 2, dtype=jnp.int32)[None, None, :]
    marks = (slot - 2 == spot[:, :, None]) & valid[:, :, None]
    slots = np.arange(8)
    spot8 = jnp.concatenate([spot[:, :2], spot[:, :2], spot[:, 2:], spot[:, 2:]], axis=1)
    valid8 = jnp.concatenate([valid[:, :2], valid[:, :2], valid[:, 2:], valid[:, 2:]], axis=1)
    by_slot = (slot - 2 == spot8[:, :, None]) & valid8[:, :, None]
    belongs = jnp.asarray((slots // 2) % 2 == np.arange(2)[:, None])
    spread = (by_slot[:, :, None, :] & belongs.T[None, :, :, None]).astype(jnp.bfloat16)
    around = jnp.einsum("ics,ispj->pcj", values, spread, preferred_element_type=jnp.float32)
    near_in = []
    for part in range(2):
        s = taps[1 + part, 0, :, None] * around[part, :, 2:]
        s = s + taps[1 + part, 1, :, None] * around[part, :, 1:-1]
        s = s + taps[1 + part, 2, :, None] * around[part, :, :-2]
        near_in.append(s)
    at_start = jnp.any(marks[:, :2, 2:], axis=(0, 1))
    mixed_input = jnp.where(
        at_start[None, :], (near_in[0] * near_in[1]).astype(jnp.bfloat16), from_senders
    )

    x_spec = transform(mixed_input.reshape(own, n_blocks, T_DEV), forward, "cnt,tf->cnf")
    own_taps = lax.dynamic_slice_in_dim(filter_taps, first, own, 0)
    tap_blocks = jnp.concatenate(
        [jnp.zeros((own, T_DEV), own_taps.dtype), own_taps], axis=1
    ).reshape(own, n_blocks + 1, T_DEV)
    h_spec = transform(tap_blocks, forward, "cnt,tf->cnf")
    column = jnp.arange(PERIOD, dtype=jnp.int32) % T_DEV
    signs = jnp.where(column % 2 == 0, 1.0, -1.0).astype(jnp.float32)
    g_spec = h_spec[:, 1:] + signs * h_spec[:, :-1]
    xr, xi = x_spec[..., :T_DEV], x_spec[..., T_DEV:]
    gr, gi = g_spec[..., :T_DEV], g_spec[..., T_DEV:]
    sums = [jnp.zeros((own, n_blocks, T_DEV), jnp.float32) for _ in range(4)]
    for k in range(n_blocks):
        pad = ((0, 0), (k, 0), (0, 0))
        terms = (
            xr[:, : n_blocks - k] * gr[:, k : k + 1],
            xi[:, : n_blocks - k] * gi[:, k : k + 1],
            xr[:, : n_blocks - k] * gi[:, k : k + 1],
            xi[:, : n_blocks - k] * gr[:, k : k + 1],
        )
        sums = [s + jnp.pad(t, pad) for s, t in zip(sums, terms)]
    rr, ii, ri, ir = sums
    at_zero = jnp.arange(T_DEV, dtype=jnp.int32)[None, None, :] == 0
    spectrum = jnp.concatenate(
        [jnp.where(at_zero, rr, rr - ii), jnp.where(at_zero, ii, ri + ir)], axis=2
    )
    conv_core = jnp.einsum("cnf,ft->cnt", spectrum, inverse, precision=lax.Precision.HIGHEST)
    gains = lax.dynamic_slice_in_dim(skip_gain, first, own, 0)
    conv = conv_core.reshape(own, length) + gains[:, None] * mixed_input.astype(jnp.float32)
    gated = (shorted_gate * conv).astype(jnp.bfloat16)
    back = lax.all_to_all(gated.reshape(own, n_ctx, T_DEV), "ctx", 1, 0, tiled=False)
    gated_block = back.reshape(channels, T_DEV)
    mixed = jnp.dot(
        out_weight,
        lax.all_gather(gated_block, "ch", axis=0, tiled=True),
        preferred_element_type=jnp.float32,
    )
    return with_layout_constraint(mixed.astype(jnp.bfloat16), Layout((0, 1)))


def on_device(arrivals, counts, short_taps, filter_taps, skip_gain, out_weight):
    n_ctx = lax.axis_size("ctx")
    blocks = filter_taps.shape[1] // T_DEV
    if arrivals.shape[1] % n_ctx == 0 and blocks == n_ctx:
        return by_transpose(arrivals, counts, short_taps, filter_taps, skip_gain, out_weight)
    return by_gather(arrivals, counts, short_taps, filter_taps, skip_gain, out_weight)


def solution(mesh):
    return jax.shard_map(
        on_device,
        mesh=mesh,
        in_specs=(
            P(None, "ch", "ctx"),
            P("ctx"),
            P(None, None, "ch"),
            P("ch", None),
            P("ch"),
            P("ch", None),
        ),
        out_specs=P("ch", "ctx"),
        check_vma=False,
    )
```

```python
import functools
import math

import jax
import jax.numpy as jnp
import ml_dtypes
import numpy as np
from jax import lax
from jax.experimental.layout import Layout, with_layout_constraint
from jax.experimental import pallas as pl
from jax.experimental.pallas import tpu as pltpu
from jax.sharding import PartitionSpec as P

T_DEV = 256
HALF = T_DEV // 2
PERIOD = 2 * T_DEV
GROUP = 8
EDGE = 128


def split_bf16(table):
    hi = table.astype(ml_dtypes.bfloat16)
    lo = (table - hi.astype(np.float64)).astype(ml_dtypes.bfloat16)
    return jnp.asarray(hi), jnp.asarray(lo)


def dft_tables():
    t = np.arange(T_DEV)[:, None]
    f = np.arange(T_DEV)[None, :]
    angle = 2.0 * np.pi * ((t * f) % PERIOD) / PERIOD
    forward = np.concatenate([np.cos(angle), -np.sin(angle)], axis=1)
    forward[:, T_DEV] = np.where(np.arange(T_DEV) % 2 == 0, 1.0, -1.0)
    fr = np.arange(T_DEV)[:, None]
    n = np.arange(T_DEV)[None, :]
    angle = 2.0 * np.pi * ((fr * n) % PERIOD) / PERIOD
    inv_re = 2.0 * np.cos(angle) / PERIOD
    inv_re[0, :] = 1.0 / PERIOD
    inv_im = -2.0 * np.sin(angle) / PERIOD
    inv_im[0, :] = np.where(np.arange(T_DEV) % 2 == 0, 1.0, -1.0) / PERIOD
    inverse = np.concatenate([inv_re, inv_im], axis=0).astype(np.float32)
    return split_bf16(forward), jnp.asarray(inverse)


def transform(blocks, forward, spec="kct,tf->kcf"):
    hi, lo = forward
    return jnp.einsum(spec, blocks, hi, preferred_element_type=jnp.float32) + jnp.einsum(
        spec, blocks, lo, preferred_element_type=jnp.float32
    )


def kernel_spectra(tap_blocks, forward):
    spectra = transform(tap_blocks, forward)
    column = jnp.arange(PERIOD, dtype=jnp.int32) % T_DEV
    signs = jnp.where(column % 2 == 0, 1.0, -1.0).astype(jnp.float32)
    return spectra[1:] + signs * spectra[:-1]


def products(x_spec, g_spec):
    xr, xi = x_spec[..., :T_DEV], x_spec[..., T_DEV:]
    gr, gi = g_spec[..., :T_DEV], g_spec[..., T_DEV:]
    return (
        jnp.sum(xr * gr, axis=0),
        jnp.sum(xi * gi, axis=0),
        jnp.sum(xr * gi, axis=0),
        jnp.sum(xi * gr, axis=0),
    )


def by_gather(arrivals, counts, short_taps, filter_taps, skip_gain, out_weight):
    n_ctx = lax.axis_size("ctx")
    device = lax.axis_index("ctx")
    channels = arrivals.shape[1]
    capacity = arrivals.shape[2]
    n_blocks = filter_taps.shape[1] // T_DEV
    forward, inverse = dft_tables()

    every_count = lax.all_gather(counts, "ctx", axis=0, tiled=True)
    earlier = jnp.arange(n_ctx, dtype=jnp.int32) < device
    offset = jnp.sum(jnp.where(earlier, every_count, 0))
    count = counts[0]

    frame = 2 * T_DEV
    row = jnp.arange(capacity, dtype=jnp.int32)[:, None]
    col = jnp.arange(frame, dtype=jnp.int32)[None, :]
    shift = offset - device * T_DEV + HALF
    select = ((row + shift == col) & (row < count)).astype(jnp.bfloat16)
    placed = jnp.einsum(
        "pcr,rj->pcj", arrivals, select, preferred_element_type=jnp.float32
    ).astype(jnp.bfloat16)
    to_prev = placed[:, :, :HALF]
    to_next = placed[:, :, frame - HALF - 2 :]
    from_next = lax.ppermute(to_prev, "ctx", [(i + 1, i) for i in range(n_ctx - 1)])
    from_prev = lax.ppermute(to_next, "ctx", [(i, i + 1) for i in range(n_ctx - 1)])
    window = placed[:, :, HALF - 2 : HALF + T_DEV]
    window = window + jnp.pad(from_prev, ((0, 0), (0, 0), (0, T_DEV - HALF)))
    window = window + jnp.pad(from_next, ((0, 0), (0, 0), (T_DEV + 2 - HALF, 0)))
    wide = window.astype(jnp.float32)
    shorted = short_taps[:, 0, :, None] * wide[:, :, 2:]
    shorted = shorted + short_taps[:, 1, :, None] * wide[:, :, 1:-1]
    shorted = shorted + short_taps[:, 2, :, None] * wide[:, :, :-2]
    mixed_input = (shorted[1] * shorted[2]).astype(jnp.bfloat16)

    tap_blocks = jnp.stack(
        [jnp.zeros((channels, T_DEV), filter_taps.dtype)]
        + [filter_taps[:, k * T_DEV : (k + 1) * T_DEV] for k in range(n_blocks)]
    )
    every_input = lax.all_gather(mixed_input, "ctx", axis=0)
    backwards = jnp.concatenate(
        [jnp.flip(every_input, 0), jnp.zeros_like(every_input)], axis=0
    )
    start = n_ctx - 1 - device
    if n_blocks <= GROUP:
        x_blocks = lax.dynamic_slice_in_dim(backwards, start, n_blocks, 0)
        sums = products(transform(x_blocks, forward), kernel_spectra(tap_blocks, forward))
    else:
        width = max(w for w in range(1, GROUP + 1) if n_blocks % w == 0)

        def group(g, acc):
            k0 = g * width
            x_blocks = lax.dynamic_slice_in_dim(backwards, start + k0, width, 0)
            taps = lax.dynamic_slice_in_dim(tap_blocks, k0, width + 1, 0)
            part = products(transform(x_blocks, forward), kernel_spectra(taps, forward))
            return tuple(a + b for a, b in zip(acc, part))

        zero = jnp.zeros((channels, T_DEV), jnp.float32)
        sums = lax.fori_loop(0, n_blocks // width, group, (zero, zero, zero, zero))
    rr, ii, ri, ir = sums
    first = jnp.arange(T_DEV, dtype=jnp.int32)[None, :] == 0
    spec_re = jnp.where(first, rr, rr - ii)
    spec_im = jnp.where(first, ii, ri + ir)
    spectrum = jnp.concatenate([spec_re, spec_im], axis=1)
    conv_core = jnp.dot(spectrum, inverse, precision=lax.Precision.HIGHEST)
    conv = conv_core + skip_gain[:, None] * mixed_input.astype(jnp.float32)
    gated = (shorted[0] * conv).astype(jnp.bfloat16)
    mixed = jnp.dot(
        out_weight,
        lax.all_gather(gated, "ch", axis=0, tiled=True),
        preferred_element_type=jnp.float32,
    )
    return mixed.astype(jnp.bfloat16)


def sender_kernel(count_ref, arrivals_ref, taps_ref, out_ref, *, n_ctx, own):
    count = count_ref[0]
    capacity = arrivals_ref.shape[2]
    lane = lax.broadcasted_iota(jnp.int32, arrivals_ref.shape[1:], 1)
    row = lax.broadcasted_iota(jnp.int32, (capacity, EDGE), 0)
    column = lax.broadcasted_iota(jnp.int32, (capacity, EDGE), 1)
    square = lax.broadcasted_iota(jnp.int32, (own, own), 0)
    diagonal = square == lax.broadcasted_iota(jnp.int32, square.shape, 1)

    def tap(part, k, j):
        spread = jnp.where(diagonal, taps_ref[part, k : k + 1, j * own : (j + 1) * own], 0.0)
        return jnp.sum(spread, axis=1, keepdims=True)

    edge = jnp.where(column[:1] == 8, (count // 16).astype(jnp.float32), 0.0)
    edge = jnp.where(column[:1] == 9, (count % 16).astype(jnp.float32), edge)
    for part in range(2):
        wanted = jnp.where(column >= 4, count - 2 + column - 4 - 2 * part, column - 2 * part)
        inside = (column % 4 >= 2 * part) & (column % 4 < 2 * part + 2) & (column < 8)
        pick = ((row == wanted) & inside).astype(jnp.bfloat16)
        edge = edge + jnp.dot(arrivals_ref[1 + part], pick, preferred_element_type=jnp.float32)
    edge = edge.astype(jnp.bfloat16)
    block_lane = lane[:own]
    for j in range(n_ctx):
        rows = slice(j * own, (j + 1) * own)
        near = []
        for part in range(2):
            x = arrivals_ref[1 + part, rows, :].astype(jnp.float32)
            back1 = jnp.where(block_lane >= 1, pltpu.roll(x, 1, 1), 0.0)
            back2 = jnp.where(block_lane >= 2, pltpu.roll(x, 2, 1), 0.0)
            s = tap(1 + part, 0, j) * x
            s = s + tap(1 + part, 1, j) * back1
            s = s + tap(1 + part, 2, j) * back2
            near.append(s)
        out_ref[j, own : 2 * own, :] = (near[0] * near[1]).astype(jnp.bfloat16)
    flat_lane = lax.broadcasted_iota(jnp.int32, (EDGE, capacity), 1)
    spread = (
        (flat_lane < 8 * own) & (flat_lane % 8 == lax.broadcasted_iota(jnp.int32, (EDGE, capacity), 0))
    ).astype(jnp.bfloat16)
    channel = lax.broadcasted_iota(jnp.int32, (own, capacity), 0)
    lane_out = lax.broadcasted_iota(jnp.int32, (own, capacity), 1)
    code = jnp.where(lane_out[:1] == 8 * own, (count // 16).astype(jnp.float32), 0.0)
    code = jnp.where(lane_out[:1] == 8 * own + 1, (count % 16).astype(jnp.float32), code)
    for j in range(n_ctx):
        rows = slice(j * own, (j + 1) * own)
        out_ref[j, :own, :] = arrivals_ref[0, rows, :]
        tiled = jnp.dot(edge[rows], spread, preferred_element_type=jnp.float32)
        flat = jnp.sum(jnp.where(lane_out // 8 == channel, tiled, 0.0), axis=0, keepdims=True)
        out_ref[j, 2 * own : 2 * own + 1, :] = (flat + code).astype(jnp.bfloat16)


def by_transpose(arrivals, counts, short_taps, filter_taps, skip_gain, out_weight):
    n_ctx = lax.axis_size("ctx")
    device = lax.axis_index("ctx")
    channels = arrivals.shape[1]
    capacity = arrivals.shape[2]
    length = filter_taps.shape[1]
    n_blocks = length // T_DEV
    own = channels // n_ctx
    forward, inverse = dft_tables()

    payload = pl.pallas_call(
        functools.partial(sender_kernel, n_ctx=n_ctx, own=own),
        in_specs=[
            pl.BlockSpec(memory_space=pltpu.SMEM),
            pl.BlockSpec(memory_space=pltpu.VMEM),
            pl.BlockSpec(memory_space=pltpu.VMEM),
        ],
        out_specs=pl.BlockSpec(memory_space=pltpu.VMEM),
        out_shape=jax.ShapeDtypeStruct((n_ctx, 2 * own + 1, capacity), jnp.bfloat16),
    )(counts, arrivals, short_taps)
    got = lax.all_to_all(payload, "ctx", 0, 0, tiled=False)
    rows = got[:, : 2 * own]
    edge_in = got[:, 2 * own]
    every_count = (
        edge_in[:, own * 8].astype(jnp.int32) * 16 + edge_in[:, own * 8 + 1].astype(jnp.int32)
    )
    offsets = jnp.cumsum(every_count) - every_count

    frame = 2 * T_DEV
    row = jnp.arange(capacity, dtype=jnp.int32)[None, :, None]
    col = jnp.arange(frame, dtype=jnp.int32)[None, None, :]
    sampler = jnp.arange(n_ctx, dtype=jnp.int32)[:, None, None]
    shift = offsets[:, None, None] - (sampler - 1) * T_DEV - HALF
    select = ((row + shift == col) & (row < every_count[:, None, None])).astype(jnp.bfloat16)
    placed = jnp.einsum("icr,irj->icj", rows, select, preferred_element_type=jnp.bfloat16)
    full = sum(
        jnp.pad(placed[i], ((0, 0), (i * T_DEV + HALF, (n_ctx - i) * T_DEV - HALF)))
        for i in range(n_ctx)
    )
    first = device * own
    taps = lax.dynamic_slice_in_dim(short_taps, first, own, 2)
    gate = full[:own, T_DEV - 2 : T_DEV + length].astype(jnp.float32)
    shorted_gate = taps[0, 0, :, None] * gate[:, 2:]
    shorted_gate = shorted_gate + taps[0, 1, :, None] * gate[:, 1:-1]
    shorted_gate = shorted_gate + taps[0, 2, :, None] * gate[:, :-2]
    from_senders = full[own:, T_DEV : T_DEV + length]

    values = edge_in[:, : own * 8].reshape(n_ctx, own, 8)
    count_col = every_count[:, None]
    at_row = jnp.concatenate(
        [jnp.zeros_like(count_col), jnp.ones_like(count_col), count_col - 2, count_col - 1], axis=1
    )
    valid = jnp.concatenate([at_row[:, :2] < count_col, at_row[:, 2:] >= 2], axis=1)
    spot = offsets[:, None] + at_row
    slot = jnp.arange(length + 2, dtype=jnp.int32)[None, None, :]
    marks = (slot - 2 == spot[:, :, None]) & valid[:, :, None]
    slots = np.arange(8)
    spot8 = jnp.concatenate([spot[:, :2], spot[:, :2], spot[:, 2:], spot[:, 2:]], axis=1)
    valid8 = jnp.concatenate([valid[:, :2], valid[:, :2], valid[:, 2:], valid[:, 2:]], axis=1)
    by_slot = (slot - 2 == spot8[:, :, None]) & valid8[:, :, None]
    belongs = jnp.asarray((slots // 2) % 2 == np.arange(2)[:, None])
    spread = (by_slot[:, :, None, :] & belongs.T[None, :, :, None]).astype(jnp.bfloat16)
    around = jnp.einsum("ics,ispj->pcj", values, spread, preferred_element_type=jnp.float32)
    near_in = []
    for part in range(2):
        s = taps[1 + part, 0, :, None] * around[part, :, 2:]
        s = s + taps[1 + part, 1, :, None] * around[part, :, 1:-1]
        s = s + taps[1 + part, 2, :, None] * around[part, :, :-2]
        near_in.append(s)
    at_start = jnp.any(marks[:, :2, 2:], axis=(0, 1))
    mixed_input = jnp.where(
        at_start[None, :], (near_in[0] * near_in[1]).astype(jnp.bfloat16), from_senders
    )

    x_spec = transform(mixed_input.reshape(own, n_blocks, T_DEV), forward, "cnt,tf->cnf")
    own_taps = lax.dynamic_slice_in_dim(filter_taps, first, own, 0)
    tap_blocks = jnp.concatenate(
        [jnp.zeros((own, T_DEV), own_taps.dtype), own_taps], axis=1
    ).reshape(own, n_blocks + 1, T_DEV)
    h_spec = transform(tap_blocks, forward, "cnt,tf->cnf")
    column = jnp.arange(PERIOD, dtype=jnp.int32) % T_DEV
    signs = jnp.where(column % 2 == 0, 1.0, -1.0).astype(jnp.float32)
    g_spec = h_spec[:, 1:] + signs * h_spec[:, :-1]
    xr, xi = x_spec[..., :T_DEV], x_spec[..., T_DEV:]
    gr, gi = g_spec[..., :T_DEV], g_spec[..., T_DEV:]
    sums = [jnp.zeros((own, n_blocks, T_DEV), jnp.float32) for _ in range(4)]
    for k in range(n_blocks):
        pad = ((0, 0), (k, 0), (0, 0))
        terms = (
            xr[:, : n_blocks - k] * gr[:, k : k + 1],
            xi[:, : n_blocks - k] * gi[:, k : k + 1],
            xr[:, : n_blocks - k] * gi[:, k : k + 1],
            xi[:, : n_blocks - k] * gr[:, k : k + 1],
        )
        sums = [s + jnp.pad(t, pad) for s, t in zip(sums, terms)]
    rr, ii, ri, ir = sums
    at_zero = jnp.arange(T_DEV, dtype=jnp.int32)[None, None, :] == 0
    spectrum = jnp.concatenate(
        [jnp.where(at_zero, rr, rr - ii), jnp.where(at_zero, ii, ri + ir)], axis=2
    )
    conv_core = jnp.einsum("cnf,ft->cnt", spectrum, inverse, precision=lax.Precision.HIGHEST)
    gains = lax.dynamic_slice_in_dim(skip_gain, first, own, 0)
    conv = conv_core.reshape(own, length) + gains[:, None] * mixed_input.astype(jnp.float32)
    gated = (shorted_gate * conv).astype(jnp.bfloat16)
    back = lax.all_to_all(gated.reshape(own, n_ctx, T_DEV), "ctx", 1, 0, tiled=False)
    gated_block = back.reshape(channels, T_DEV)
    mixed = jnp.dot(
        out_weight,
        lax.all_gather(gated_block, "ch", axis=0, tiled=True),
        preferred_element_type=jnp.float32,
    )
    return with_layout_constraint(mixed.astype(jnp.bfloat16), Layout((0, 1)))


def on_device(arrivals, counts, short_taps, filter_taps, skip_gain, out_weight):
    n_ctx = lax.axis_size("ctx")
    blocks = filter_taps.shape[1] // T_DEV
    if arrivals.shape[1] % n_ctx == 0 and blocks == n_ctx:
        return by_transpose(arrivals, counts, short_taps, filter_taps, skip_gain, out_weight)
    return by_gather(arrivals, counts, short_taps, filter_taps, skip_gain, out_weight)


def solution(mesh):
    return jax.shard_map(
        on_device,
        mesh=mesh,
        in_specs=(
            P(None, "ch", "ctx"),
            P("ctx"),
            P(None, None, "ch"),
            P("ch", None),
            P("ch"),
            P("ch", None),
        ),
        out_specs=P("ch", "ctx"),
        check_vma=False,
    )
```

```python
import functools
import math

import jax
import jax.numpy as jnp
import ml_dtypes
import numpy as np
from jax import lax
from jax.experimental.layout import Layout, with_layout_constraint
from jax.experimental import pallas as pl
from jax.experimental.pallas import tpu as pltpu
from jax.sharding import PartitionSpec as P

T_DEV = 256
HALF = T_DEV // 2
PERIOD = 2 * T_DEV
GROUP = 8
EDGE = 128


def split_bf16(table):
    hi = table.astype(ml_dtypes.bfloat16)
    lo = (table - hi.astype(np.float64)).astype(ml_dtypes.bfloat16)
    return jnp.asarray(hi), jnp.asarray(lo)


def dft_tables():
    t = np.arange(T_DEV)[:, None]
    f = np.arange(T_DEV)[None, :]
    angle = 2.0 * np.pi * ((t * f) % PERIOD) / PERIOD
    forward = np.concatenate([np.cos(angle), -np.sin(angle)], axis=1)
    forward[:, T_DEV] = np.where(np.arange(T_DEV) % 2 == 0, 1.0, -1.0)
    fr = np.arange(T_DEV)[:, None]
    n = np.arange(T_DEV)[None, :]
    angle = 2.0 * np.pi * ((fr * n) % PERIOD) / PERIOD
    inv_re = 2.0 * np.cos(angle) / PERIOD
    inv_re[0, :] = 1.0 / PERIOD
    inv_im = -2.0 * np.sin(angle) / PERIOD
    inv_im[0, :] = np.where(np.arange(T_DEV) % 2 == 0, 1.0, -1.0) / PERIOD
    inverse = np.concatenate([inv_re, inv_im], axis=0)
    return split_bf16(forward), jnp.asarray(inverse.astype(np.float32)), split_bf16(inverse)


def transform(blocks, forward, spec="kct,tf->kcf"):
    hi, lo = forward
    return jnp.einsum(spec, blocks, hi, preferred_element_type=jnp.float32) + jnp.einsum(
        spec, blocks, lo, preferred_element_type=jnp.float32
    )


def kernel_spectra(tap_blocks, forward):
    spectra = transform(tap_blocks, forward)
    column = jnp.arange(PERIOD, dtype=jnp.int32) % T_DEV
    signs = jnp.where(column % 2 == 0, 1.0, -1.0).astype(jnp.float32)
    return spectra[1:] + signs * spectra[:-1]


def products(x_spec, g_spec):
    xr, xi = x_spec[..., :T_DEV], x_spec[..., T_DEV:]
    gr, gi = g_spec[..., :T_DEV], g_spec[..., T_DEV:]
    return (
        jnp.sum(xr * gr, axis=0),
        jnp.sum(xi * gi, axis=0),
        jnp.sum(xr * gi, axis=0),
        jnp.sum(xi * gr, axis=0),
    )


def by_gather(arrivals, counts, short_taps, filter_taps, skip_gain, out_weight):
    n_ctx = lax.axis_size("ctx")
    device = lax.axis_index("ctx")
    channels = arrivals.shape[1]
    capacity = arrivals.shape[2]
    n_blocks = filter_taps.shape[1] // T_DEV
    forward, inverse, _ = dft_tables()

    every_count = lax.all_gather(counts, "ctx", axis=0, tiled=True)
    earlier = jnp.arange(n_ctx, dtype=jnp.int32) < device
    offset = jnp.sum(jnp.where(earlier, every_count, 0))
    count = counts[0]

    frame = 2 * T_DEV
    row = jnp.arange(capacity, dtype=jnp.int32)[:, None]
    col = jnp.arange(frame, dtype=jnp.int32)[None, :]
    shift = offset - device * T_DEV + HALF
    select = ((row + shift == col) & (row < count)).astype(jnp.bfloat16)
    placed = jnp.einsum(
        "pcr,rj->pcj", arrivals, select, preferred_element_type=jnp.float32
    ).astype(jnp.bfloat16)
    to_prev = placed[:, :, :HALF]
    to_next = placed[:, :, frame - HALF - 2 :]
    from_next = lax.ppermute(to_prev, "ctx", [(i + 1, i) for i in range(n_ctx - 1)])
    from_prev = lax.ppermute(to_next, "ctx", [(i, i + 1) for i in range(n_ctx - 1)])
    window = placed[:, :, HALF - 2 : HALF + T_DEV]
    window = window + jnp.pad(from_prev, ((0, 0), (0, 0), (0, T_DEV - HALF)))
    window = window + jnp.pad(from_next, ((0, 0), (0, 0), (T_DEV + 2 - HALF, 0)))
    wide = window.astype(jnp.float32)
    shorted = short_taps[:, 0, :, None] * wide[:, :, 2:]
    shorted = shorted + short_taps[:, 1, :, None] * wide[:, :, 1:-1]
    shorted = shorted + short_taps[:, 2, :, None] * wide[:, :, :-2]
    mixed_input = (shorted[1] * shorted[2]).astype(jnp.bfloat16)

    tap_blocks = jnp.stack(
        [jnp.zeros((channels, T_DEV), filter_taps.dtype)]
        + [filter_taps[:, k * T_DEV : (k + 1) * T_DEV] for k in range(n_blocks)]
    )
    every_input = lax.all_gather(mixed_input, "ctx", axis=0)
    backwards = jnp.concatenate(
        [jnp.flip(every_input, 0), jnp.zeros_like(every_input)], axis=0
    )
    start = n_ctx - 1 - device
    if n_blocks <= GROUP:
        x_blocks = lax.dynamic_slice_in_dim(backwards, start, n_blocks, 0)
        sums = products(transform(x_blocks, forward), kernel_spectra(tap_blocks, forward))
    else:
        width = max(w for w in range(1, GROUP + 1) if n_blocks % w == 0)

        def group(g, acc):
            k0 = g * width
            x_blocks = lax.dynamic_slice_in_dim(backwards, start + k0, width, 0)
            taps = lax.dynamic_slice_in_dim(tap_blocks, k0, width + 1, 0)
            part = products(transform(x_blocks, forward), kernel_spectra(taps, forward))
            return tuple(a + b for a, b in zip(acc, part))

        zero = jnp.zeros((channels, T_DEV), jnp.float32)
        sums = lax.fori_loop(0, n_blocks // width, group, (zero, zero, zero, zero))
    rr, ii, ri, ir = sums
    first = jnp.arange(T_DEV, dtype=jnp.int32)[None, :] == 0
    spec_re = jnp.where(first, rr, rr - ii)
    spec_im = jnp.where(first, ii, ri + ir)
    spectrum = jnp.concatenate([spec_re, spec_im], axis=1)
    conv_core = jnp.dot(spectrum, inverse, precision=lax.Precision.HIGHEST)
    conv = conv_core + skip_gain[:, None] * mixed_input.astype(jnp.float32)
    gated = (shorted[0] * conv).astype(jnp.bfloat16)
    mixed = jnp.dot(
        out_weight,
        lax.all_gather(gated, "ch", axis=0, tiled=True),
        preferred_element_type=jnp.float32,
    )
    return mixed.astype(jnp.bfloat16)


def sender_kernel(count_ref, arrivals_ref, taps_ref, out_ref, *, n_ctx, own):
    count = count_ref[0]
    capacity = arrivals_ref.shape[2]
    lane = lax.broadcasted_iota(jnp.int32, arrivals_ref.shape[1:], 1)
    row = lax.broadcasted_iota(jnp.int32, (capacity, EDGE), 0)
    column = lax.broadcasted_iota(jnp.int32, (capacity, EDGE), 1)
    square = lax.broadcasted_iota(jnp.int32, (lane.shape[0], lane.shape[0]), 0)
    diagonal = square == lax.broadcasted_iota(jnp.int32, square.shape, 1)

    def tap(part, k):
        spread = jnp.where(diagonal, taps_ref[part, k : k + 1, :], 0.0)
        return jnp.sum(spread, axis=1, keepdims=True)

    edge = jnp.where(column[:1] == 8, (count // 16).astype(jnp.float32), 0.0)
    edge = jnp.where(column[:1] == 9, (count % 16).astype(jnp.float32), edge)
    columns = []
    for part in range(2):
        wanted = jnp.where(column >= 4, count - 2 + column - 4 - 2 * part, column - 2 * part)
        inside = (column % 4 >= 2 * part) & (column % 4 < 2 * part + 2) & (column < 8)
        pick = ((row == wanted) & inside).astype(jnp.bfloat16)
        edge = edge + jnp.dot(arrivals_ref[1 + part], pick, preferred_element_type=jnp.float32)
        columns.append([tap(1 + part, k) for k in range(3)])
    edge = edge.astype(jnp.bfloat16)
    block_lane = lane[:own]
    for j in range(n_ctx):
        rows = slice(j * own, (j + 1) * own)
        near = []
        for part in range(2):
            x = arrivals_ref[1 + part, rows, :].astype(jnp.float32)
            back1 = jnp.where(block_lane >= 1, pltpu.roll(x, 1, 1), 0.0)
            back2 = jnp.where(block_lane >= 2, pltpu.roll(x, 2, 1), 0.0)
            s = columns[part][0][rows] * x
            s = s + columns[part][1][rows] * back1
            s = s + columns[part][2][rows] * back2
            near.append(s)
        out_ref[j, own : 2 * own, :] = (near[0] * near[1]).astype(jnp.bfloat16)
    flat_lane = lax.broadcasted_iota(jnp.int32, (EDGE, capacity), 1)
    spread = (
        (flat_lane < 8 * own) & (flat_lane % 8 == lax.broadcasted_iota(jnp.int32, (EDGE, capacity), 0))
    ).astype(jnp.bfloat16)
    channel = lax.broadcasted_iota(jnp.int32, (own, capacity), 0)
    lane_out = lax.broadcasted_iota(jnp.int32, (own, capacity), 1)
    code = jnp.where(lane_out[:1] == 8 * own, (count // 16).astype(jnp.float32), 0.0)
    code = jnp.where(lane_out[:1] == 8 * own + 1, (count % 16).astype(jnp.float32), code)
    for j in range(n_ctx):
        rows = slice(j * own, (j + 1) * own)
        out_ref[j, :own, :] = arrivals_ref[0, rows, :]
        tiled = jnp.dot(edge[rows], spread, preferred_element_type=jnp.float32)
        flat = jnp.sum(jnp.where(lane_out // 8 == channel, tiled, 0.0), axis=0, keepdims=True)
        out_ref[j, 2 * own : 2 * own + 1, :] = (flat + code).astype(jnp.bfloat16)


def by_transpose(arrivals, counts, short_taps, filter_taps, skip_gain, out_weight):
    n_ctx = lax.axis_size("ctx")
    device = lax.axis_index("ctx")
    channels = arrivals.shape[1]
    capacity = arrivals.shape[2]
    length = filter_taps.shape[1]
    n_blocks = length // T_DEV
    own = channels // n_ctx
    forward, _, inverse = dft_tables()

    payload = pl.pallas_call(
        functools.partial(sender_kernel, n_ctx=n_ctx, own=own),
        in_specs=[
            pl.BlockSpec(memory_space=pltpu.SMEM),
            pl.BlockSpec(memory_space=pltpu.VMEM),
            pl.BlockSpec(memory_space=pltpu.VMEM),
        ],
        out_specs=pl.BlockSpec(memory_space=pltpu.VMEM),
        out_shape=jax.ShapeDtypeStruct((n_ctx, 2 * own + 1, capacity), jnp.bfloat16),
    )(counts, arrivals, short_taps)
    got = lax.all_to_all(payload, "ctx", 0, 0, tiled=False)
    rows = got[:, : 2 * own]
    edge_in = got[:, 2 * own]
    every_count = (
        edge_in[:, own * 8].astype(jnp.int32) * 16 + edge_in[:, own * 8 + 1].astype(jnp.int32)
    )
    offsets = jnp.cumsum(every_count) - every_count

    frame = 2 * T_DEV
    row = jnp.arange(capacity, dtype=jnp.int32)[None, :, None]
    col = jnp.arange(frame, dtype=jnp.int32)[None, None, :]
    sampler = jnp.arange(n_ctx, dtype=jnp.int32)[:, None, None]
    shift = offsets[:, None, None] - (sampler - 1) * T_DEV - HALF
    select = ((row + shift == col) & (row < every_count[:, None, None])).astype(jnp.bfloat16)
    placed = jnp.einsum("icr,irj->icj", rows, select, preferred_element_type=jnp.bfloat16)
    full = sum(
        jnp.pad(placed[i], ((0, 0), (i * T_DEV + HALF, (n_ctx - i) * T_DEV - HALF)))
        for i in range(n_ctx)
    )
    first = device * own
    taps = lax.dynamic_slice_in_dim(short_taps, first, own, 2)
    gate = full[:own, T_DEV - 2 : T_DEV + length].astype(jnp.float32)
    shorted_gate = taps[0, 0, :, None] * gate[:, 2:]
    shorted_gate = shorted_gate + taps[0, 1, :, None] * gate[:, 1:-1]
    shorted_gate = shorted_gate + taps[0, 2, :, None] * gate[:, :-2]
    from_senders = full[own:, T_DEV : T_DEV + length]

    values = edge_in[:, : own * 8].reshape(n_ctx, own, 8)
    count_col = every_count[:, None]
    at_row = jnp.concatenate(
        [jnp.zeros_like(count_col), jnp.ones_like(count_col), count_col - 2, count_col - 1], axis=1
    )
    valid = jnp.concatenate([at_row[:, :2] < count_col, at_row[:, 2:] >= 2], axis=1)
    spot = offsets[:, None] + at_row
    slot = jnp.arange(length + 2, dtype=jnp.int32)[None, None, :]
    marks = (slot - 2 == spot[:, :, None]) & valid[:, :, None]
    slots = np.arange(8)
    spot8 = jnp.concatenate([spot[:, :2], spot[:, :2], spot[:, 2:], spot[:, 2:]], axis=1)
    valid8 = jnp.concatenate([valid[:, :2], valid[:, :2], valid[:, 2:], valid[:, 2:]], axis=1)
    by_slot = (slot - 2 == spot8[:, :, None]) & valid8[:, :, None]
    belongs = jnp.asarray((slots // 2) % 2 == np.arange(2)[:, None])
    spread = (by_slot[:, :, None, :] & belongs.T[None, :, :, None]).astype(jnp.bfloat16)
    around = jnp.einsum("ics,ispj->pcj", values, spread, preferred_element_type=jnp.float32)
    near_in = []
    for part in range(2):
        s = taps[1 + part, 0, :, None] * around[part, :, 2:]
        s = s + taps[1 + part, 1, :, None] * around[part, :, 1:-1]
        s = s + taps[1 + part, 2, :, None] * around[part, :, :-2]
        near_in.append(s)
    at_start = jnp.any(marks[:, :2, 2:], axis=(0, 1))
    mixed_input = jnp.where(
        at_start[None, :], (near_in[0] * near_in[1]).astype(jnp.bfloat16), from_senders
    )

    x_spec = transform(mixed_input.reshape(own, n_blocks, T_DEV), forward, "cnt,tf->cnf")
    own_taps = lax.dynamic_slice_in_dim(filter_taps, first, own, 0)
    tap_blocks = jnp.concatenate(
        [jnp.zeros((own, T_DEV), own_taps.dtype), own_taps], axis=1
    ).reshape(own, n_blocks + 1, T_DEV)
    h_spec = transform(tap_blocks, forward, "cnt,tf->cnf")
    column = jnp.arange(PERIOD, dtype=jnp.int32) % T_DEV
    signs = jnp.where(column % 2 == 0, 1.0, -1.0).astype(jnp.float32)
    g_spec = h_spec[:, 1:] + signs * h_spec[:, :-1]
    xr, xi = x_spec[..., :T_DEV], x_spec[..., T_DEV:]
    gr, gi = g_spec[..., :T_DEV], g_spec[..., T_DEV:]
    sums = [jnp.zeros((own, n_blocks, T_DEV), jnp.float32) for _ in range(4)]
    for k in range(n_blocks):
        pad = ((0, 0), (k, 0), (0, 0))
        terms = (
            xr[:, : n_blocks - k] * gr[:, k : k + 1],
            xi[:, : n_blocks - k] * gi[:, k : k + 1],
            xr[:, : n_blocks - k] * gi[:, k : k + 1],
            xi[:, : n_blocks - k] * gr[:, k : k + 1],
        )
        sums = [s + jnp.pad(t, pad) for s, t in zip(sums, terms)]
    rr, ii, ri, ir = sums
    at_zero = jnp.arange(T_DEV, dtype=jnp.int32)[None, None, :] == 0
    spectrum = jnp.concatenate(
        [jnp.where(at_zero, rr, rr - ii), jnp.where(at_zero, ii, ri + ir)], axis=2
    )
    spec_hi = spectrum.astype(jnp.bfloat16)
    spec_lo = (spectrum - spec_hi.astype(jnp.float32)).astype(jnp.bfloat16)
    inv_hi, inv_lo = inverse
    conv_core = sum(
        jnp.einsum("cnf,ft->cnt", a, b, preferred_element_type=jnp.float32)
        for a, b in ((spec_hi, inv_hi), (spec_hi, inv_lo), (spec_lo, inv_hi))
    )
    gains = lax.dynamic_slice_in_dim(skip_gain, first, own, 0)
    conv = conv_core.reshape(own, length) + gains[:, None] * mixed_input.astype(jnp.float32)
    gated = (shorted_gate * conv).astype(jnp.bfloat16)
    back = lax.all_to_all(gated.reshape(own, n_ctx, T_DEV), "ctx", 1, 0, tiled=False)
    gated_block = back.reshape(channels, T_DEV)
    mixed = jnp.dot(
        out_weight,
        lax.all_gather(gated_block, "ch", axis=0, tiled=True),
        preferred_element_type=jnp.float32,
    )
    return with_layout_constraint(mixed.astype(jnp.bfloat16), Layout((0, 1)))


def on_device(arrivals, counts, short_taps, filter_taps, skip_gain, out_weight):
    n_ctx = lax.axis_size("ctx")
    blocks = filter_taps.shape[1] // T_DEV
    if arrivals.shape[1] % n_ctx == 0 and blocks == n_ctx:
        return by_transpose(arrivals, counts, short_taps, filter_taps, skip_gain, out_weight)
    return by_gather(arrivals, counts, short_taps, filter_taps, skip_gain, out_weight)


def solution(mesh):
    return jax.shard_map(
        on_device,
        mesh=mesh,
        in_specs=(
            P(None, "ch", "ctx"),
            P("ctx"),
            P(None, None, "ch"),
            P("ch", None),
            P("ch"),
            P("ch", None),
        ),
        out_specs=P("ch", "ctx"),
        check_vma=False,
    )
```
